32 devices in a mesh: wide: 8 (over y, x, core), narrow: 4 (over z).
Axes of the slice: x: 2, y: 2, z: 4, core: 2. Of those that a mesh axis runs over, the one named last changes fastest.
Arguments:
- tokens: bfloat16 [2048, 3072], P('wide'), may hold values from -6 to 6
- gain: bfloat16 [3072], replicated, may hold values from 0.5 to 1.5
- w_qkv: bfloat16 [3072, 3, 3072], P('wide', None, 'narrow'), may hold values from -0.109375 to 0.109375
- w_out: bfloat16 [3072, 3072], P('wide', 'narrow'), may hold values from -3 to 3
- cache: bfloat16 [256, 64, 2, 3072], P('wide', None, None, 'narrow'), may hold values from -104 to 104
- lengths: int32 [4], replicated, may hold values from 1 to 3584, as said below
- order: int32 [32], replicated, may hold values from 0 to 31, each once
- pages: int32 [256], replicated, may hold values from 0 to 255, each once
Outputs:
- mixed: bfloat16 [2048, 3072], P('wide', 'narrow')
The draws below stay inside these ranges and needn't reach their ends.
Inputs may be any that keep to these rules, and one draw needn't show every extreme that they name: `lengths`: some request has exactly 3584 cached positions. `order`: each query block index once. `pages`: each cache block once.
All inputs are finite; a program needn't handle non-finite values.
Results may differ from the reference program's by a relative error of at most 0.02.
The reference program's roundings to bfloat16 on the way (of `normed`, `queries`, `weights` and `attention`) count: a program that leaves them out, or rounds other values in their place, can miss the bound.
Values may be sent and summed in bfloat16 or wider, within the bound.
No kernel may reach another device: no remote copies, remote signals or barrier semaphores. Data moves between devices by JAX's collectives and lax.ppermute only.
A program may use at most 192 MiB of HBM per device.

```python
import jax
import jax.numpy as jnp
from jax import lax

D = 3072
HEADS = 32
HD = 96
BLK = 64
MAXB = 64
CB_DEV = 32
QB_DEV = 4
CB = 256
NQB = 32
REQ = 4
NEW = 512
BPR = 8
TOKENS = 2048
CACHE = 4096
N_WIDE = 8


def draw_cache(key, part):
    first_key = jax.random.fold_in(key, 11)
    full_shape = (CB, BLK, 2, HEADS * HD)
    sampled = jnp.clip(jax.random.normal(first_key, full_shape, jnp.float32), -6.0, 6.0)
    return sampled.astype(jnp.bfloat16)


def draw_lengths(key, part):
    first_key = jax.random.fold_in(key, 21)
    second_key = jax.random.fold_in(key, 22)
    longest_len = CACHE - NEW
    sampled = jax.random.randint(first_key, (REQ,), 1, longest_len + 1, dtype=jnp.int32)
    longest = jax.random.randint(second_key, (), 0, REQ, dtype=jnp.int32)
    return jnp.where(jnp.arange(REQ, dtype=jnp.int32) == longest, longest_len, sampled).astype(jnp.int32)


def shard_levels(key, dims, pieces, low, largest):
    level, own = 1.0, jax.random.fold_in(key, 6)
    for position, parts in pieces:
        steps = jnp.exp(jax.random.uniform(jax.random.fold_in(own, position), (parts,), jnp.float32, low / len(pieces), largest / len(pieces)))
        level = level * jnp.repeat(steps, dims[position] // parts).reshape([-1 if axis == position else 1 for axis in range(len(dims))])
    return level


def gaussian(stream_key, dims, scale, reach, cuts=(), kind=jnp.bfloat16):
    values = jax.random.normal(stream_key, dims, jnp.float32) * scale
    if len(cuts) > 0:
        values = shard_levels(stream_key, dims, cuts, -0.22, 0.18) * values
    return jnp.clip(values, min=-reach, max=reach).astype(kind)


def setup_inputs(seed: int = 0) -> dict:
    key_list = jax.random.split(jax.random.key(seed), 9)
    return {
        "tokens": gaussian(key_list[0], (TOKENS, D), 1.0, 6.0, ((0, 8),)),
        "gain": jnp.clip(1.0 + 0.1 * jax.random.normal(key_list[1], (D,), jnp.float32), 0.5, 1.5).astype(jnp.bfloat16),
        "w_qkv": gaussian(key_list[2], (D, 3, HEADS * HD), D ** -0.5, 0.109375, ((0, 8), (2, 4))),
        "w_out": gaussian(key_list[3], (D, HEADS * HD), 0.3, 3.0, ((0, 8), (1, 4))),
        "cache": draw_cache(jax.random.fold_in(key_list[8], 71), 0),
        "lengths": draw_lengths(jax.random.fold_in(key_list[8], 71), 0),
        "order": jax.random.permutation(key_list[6], NQB).astype(jnp.int32),
        "pages": jax.random.permutation(key_list[7], CB).astype(jnp.int32),
    }


negative = -1e+30
beyond = 1073741824

def rotate(values, positions):
    half_dim = values.shape[-1] // 2
    frequency = 10000.0 ** (-2.0 * jnp.arange(half_dim, dtype=jnp.float32) / values.shape[-1])
    angles = positions.astype(jnp.float32)[:, None] * frequency[None, :]
    cos_part = jnp.cos(angles)[:, None, :]
    sin_part = jnp.sin(angles)[:, None, :]
    lower_half = values[..., :half_dim]
    upper_half = values[..., half_dim:]
    return jnp.concatenate([lower_half * cos_part - upper_half * sin_part, upper_half * cos_part + lower_half * sin_part], axis=-1)

def attend(chosen, key_rows, values, block_req, block_pos, query_pos, requests):
    score_scale = key_rows.shape[-1] ** (-0.5)
    scores = jnp.einsum('lqhe,lkhe->lhqk', chosen.astype(jnp.float32), key_rows.astype(jnp.float32)) * score_scale
    allowed = block_pos[:, None, None, :] <= query_pos[:, None, :, None]
    masked = jnp.where(allowed, scores, negative)
    block_max = lax.optimization_barrier(jnp.max(masked, axis=3))
    owners = block_req[:, None] == jnp.arange(requests, dtype=jnp.int32)[None, :]
    dev_max = lax.optimization_barrier(jnp.max(jnp.where(owners[:, :, None, None], block_max[:, None], negative), axis=0))
    local_max = dev_max[block_req]
    exp_terms = jnp.where(allowed, jnp.exp(masked - local_max[..., None]), 0.0)
    den_terms = lax.optimization_barrier(jnp.sum(exp_terms, axis=3))
    weights = lax.optimization_barrier(exp_terms.astype(jnp.bfloat16))
    num_terms = jnp.einsum('lhqk,lkhe->lqhe', weights.astype(jnp.float32), values.astype(jnp.float32))
    onehot = owners.astype(jnp.float32)
    dev_num = jnp.einsum('lr,lqhe->rqhe', onehot, num_terms, precision=lax.Precision.HIGHEST)
    dev_den = jnp.einsum('lr,lhq->rqh', onehot, den_terms, precision=lax.Precision.HIGHEST)
    return (jnp.transpose(dev_max, (0, 2, 1)), dev_num, dev_den)

def reference(tokens, gain, w_qkv, w_out, cache, lengths, order, pages):
    tok_float = tokens.astype(jnp.float32)
    inv_rms = lax.rsqrt(lax.optimization_barrier(jnp.mean(tok_float * tok_float, axis=1, keepdims=True)) + 1e-05)
    normed = (tok_float * inv_rms * gain.astype(jnp.float32)[None, :]).astype(jnp.bfloat16)
    projected = jnp.einsum('tk,kcj->tcj', normed.astype(jnp.float32), w_qkv.astype(jnp.float32))
    blk_idx = jnp.arange(BLK, dtype=jnp.int32)
    slot_req = (order // BPR).astype(jnp.int32)
    slot_start = lengths[slot_req] + order % BPR * BLK
    slot_pos = slot_start[:, None] + blk_idx[None, :]
    positions = slot_pos.reshape(TOKENS)
    queries = rotate(projected[:, 0].reshape(TOKENS, HEADS, HD), positions).astype(jnp.bfloat16)
    keys_new = rotate(projected[:, 1].reshape(TOKENS, HEADS, HD), positions).astype(jnp.bfloat16).reshape(NQB, BLK, HEADS, HD)
    vals_new = projected[:, 2].astype(jnp.bfloat16).reshape(NQB, BLK, HEADS, HD)
    block_ids = jnp.arange(NQB, dtype=jnp.int32)
    slot_of = lax.optimization_barrier(jnp.sum(jnp.where(order[None, :] == block_ids[:, None], block_ids[None, :], 0), axis=1)).astype(jnp.int32)
    ordered = queries.reshape(NQB, BLK, HEADS, HD)[slot_of].reshape(REQ, NEW, HEADS, HD)
    entry_of = jnp.zeros((CB,), jnp.int32).at[pages].set(jnp.arange(CB, dtype=jnp.int32))
    cache_keys = cache[:, :, 0].reshape(CB, BLK, HEADS, HD)
    cache_vals = cache[:, :, 1].reshape(CB, BLK, HEADS, HD)

    def group_part(group_idx):
        cache_ids = (group_idx * CB_DEV + jnp.arange(CB_DEV, dtype=jnp.int32)).astype(jnp.int32)
        entries = entry_of[cache_ids]
        cache_req = (entries // MAXB).astype(jnp.int32)
        cache_pos = (entries % MAXB)[:, None] * BLK + blk_idx[None, :]
        cache_pos = jnp.where(cache_pos < lengths[cache_req][:, None], cache_pos, beyond)
        slot_ids = (group_idx * QB_DEV + jnp.arange(QB_DEV, dtype=jnp.int32)).astype(jnp.int32)
        block_req = jnp.concatenate([cache_req, slot_req[slot_ids]])
        block_pos = jnp.concatenate([cache_pos, slot_pos[slot_ids]])
        key_rows = jnp.concatenate([cache_keys[cache_ids], keys_new[slot_ids]])
        values = jnp.concatenate([cache_vals[cache_ids], vals_new[slot_ids]])
        chosen = ordered[block_req]
        query_pos = lengths[block_req][:, None] + jnp.arange(NEW, dtype=jnp.int32)[None, :]
        return attend(chosen, key_rows, values, block_req, block_pos, query_pos, REQ)

    def merge_group(carried, group_idx):
        best_max, total_num, total_den = carried
        group_max, group_num, group_den = group_part(group_idx)
        top_max = jnp.maximum(best_max, group_max)
        keep_old = jnp.exp(best_max - top_max)
        keep_new = jnp.exp(group_max - top_max)
        merged = (top_max, total_num * keep_old[..., None] + group_num * keep_new[..., None], total_den * keep_old + group_den * keep_new)
        return (merged, None)
    initial = (jnp.full((REQ, NEW, HEADS), negative, jnp.float32), jnp.zeros((REQ, NEW, HEADS, HD), jnp.float32), jnp.zeros((REQ, NEW, HEADS), jnp.float32))
    final_state, ignored = lax.scan(merge_group, initial, jnp.arange(N_WIDE, dtype=jnp.int32))
    total_num = final_state[1]
    total_den = final_state[2]
    attention = (total_num / total_den[..., None]).astype(jnp.bfloat16).reshape(TOKENS, HEADS * HD)
    return jnp.dot(attention, w_out.T, preferred_element_type=jnp.float32).astype(jnp.bfloat16)
```

```python
import jax
import jax.numpy as jnp
from jax import lax
from jax.experimental import pallas as pl
from jax.experimental.pallas import tpu as pltpu
from jax.sharding import PartitionSpec as P

HD = 96


negative = -1e30
beyond = 1073741824


def rotate(values, positions):
    half_dim = values.shape[-1] // 2
    frequency = 10000.0 ** (-2.0 * jnp.arange(half_dim, dtype=jnp.float32) / values.shape[-1])
    angles = positions.astype(jnp.float32)[:, None] * frequency[None, :]
    cos_part = jnp.cos(angles)[:, None, :]
    sin_part = jnp.sin(angles)[:, None, :]
    lower_half = values[..., :half_dim]
    upper_half = values[..., half_dim:]
    return jnp.concatenate(
        [
            lower_half * cos_part - upper_half * sin_part,
            upper_half * cos_part + lower_half * sin_part,
        ],
        axis=-1,
    )


def lookup(small_table, key_index):
    matches = key_index[..., None] == jnp.arange(small_table.shape[0], dtype=jnp.int32)
    return jnp.sum(jnp.where(matches, small_table, 0), axis=-1)


def attend_kernel(carry_in):
    def kernel(req_ref, base_ref, limit_ref, len_ref, *refs):
        if carry_in:
            q_ref, k_ref, v_ref, m0_ref, l0_ref, o0_ref, m_ref, l_ref, o_ref = refs
        else:
            q_ref, k_ref, v_ref, m_ref, l_ref, o_ref = refs
        step = pl.program_id(0)

        @pl.when(step == 0)
        def _():
            if carry_in:
                m_ref[...] = m0_ref[...]
                l_ref[...] = l0_ref[...]
                o_ref[...] = o0_ref[...]
            else:
                m_ref[...] = jnp.full(m_ref.shape, negative, jnp.float32)
                l_ref[...] = jnp.zeros(l_ref.shape, jnp.float32)
                o_ref[...] = jnp.zeros(o_ref.shape, jnp.float32)

        req = req_ref[step]
        base = base_ref[step]
        limit = limit_ref[step]
        qlen = len_ref[req]
        queries = q_ref[req]
        keys = k_ref[0]
        vals = v_ref[0]
        blk_len = keys.shape[1]
        q_len = queries.shape[1]
        scale = keys.shape[-1] ** (-0.5)
        scores = (
            jnp.einsum("hkd,hqd->hkq", keys, queries, preferred_element_type=jnp.float32)
            * scale
        )
        key_pos = base + lax.broadcasted_iota(jnp.int32, (blk_len, q_len), 0)
        query_pos = qlen + lax.broadcasted_iota(jnp.int32, (blk_len, q_len), 1)
        allowed = ((key_pos < limit) & (key_pos <= query_pos))[None]
        masked = jnp.where(allowed, scores, negative)
        m_old = m_ref[req]
        m_new = jnp.maximum(m_old, jnp.max(masked, axis=1, keepdims=True))
        exp_terms = jnp.where(allowed, jnp.exp(masked - m_new), 0.0)
        alpha = jnp.exp(m_old - m_new)
        l_ref[req] = alpha * l_ref[req] + jnp.sum(exp_terms, axis=1, keepdims=True)
        weighted = jnp.einsum(
            "hdk,hkq->hdq", vals, exp_terms.astype(jnp.bfloat16),
            preferred_element_type=jnp.float32,
        )
        o_ref[req] = alpha * o_ref[req] + weighted
        m_ref[req] = m_new

    return kernel


def attend_blocks(queries, keys, vals_t, blk_req, blk_base, blk_limit, lengths, carry=None):
    req_count, head_count, q_len, head_dim = queries.shape
    blk_count, _, blk_len, _ = keys.shape
    vmem = pltpu.MemorySpace.VMEM
    whole = pl.BlockSpec(memory_space=vmem)
    in_specs = [
        whole,
        pl.BlockSpec((1, head_count, blk_len, head_dim), lambda j, *_: (j, 0, 0, 0)),
        pl.BlockSpec((1, head_count, head_dim, blk_len), lambda j, *_: (j, 0, 0, 0)),
    ]
    args = [queries, keys, vals_t]
    if carry is not None:
        in_specs += [whole, whole, whole]
        args += list(carry)
    out_shape = (
        jax.ShapeDtypeStruct((req_count, head_count, 1, q_len), jnp.float32),
        jax.ShapeDtypeStruct((req_count, head_count, 1, q_len), jnp.float32),
        jax.ShapeDtypeStruct((req_count, head_count, head_dim, q_len), jnp.float32),
    )
    grid_spec = pltpu.PrefetchScalarGridSpec(
        num_scalar_prefetch=4,
        grid=(blk_count,),
        in_specs=in_specs,
        out_specs=(whole, whole, whole),
    )
    return pl.pallas_call(
        attend_kernel(carry is not None),
        out_shape=out_shape,
        grid_spec=grid_spec,
        compiler_params=pltpu.CompilerParams(
            dimension_semantics=("arbitrary",)
        ),
    )(blk_req, blk_base, blk_limit, lengths, *args)


def body(tokens, gain, w_qkv, w_out, cache, lengths, order, pages):
    wide_count = lax.axis_size("wide")
    wide_index = lax.axis_index("wide")
    tok_rows = tokens.shape[0]
    cache_count = cache.shape[0]
    blk_len = cache.shape[1]
    lane_width = cache.shape[3]
    head_count = lane_width // HD
    slot_count = tok_rows // blk_len
    block_total = order.shape[0]
    req_count = lengths.shape[0]
    per_request = block_total // req_count
    fresh_len = per_request * blk_len
    table_len = pages.shape[0] // req_count
    tok_float = tokens.astype(jnp.float32)
    inv_rms = lax.rsqrt(jnp.mean(tok_float * tok_float, axis=1, keepdims=True) + 1e-05)
    normed = (tok_float * inv_rms * gain.astype(jnp.float32)[None, :]).astype(jnp.bfloat16)

    w_q = lax.all_gather(w_qkv[:, 0], "wide", axis=0, tiled=True)
    blk_idx = jnp.arange(blk_len, dtype=jnp.int32)
    slot_blocks = lax.dynamic_slice_in_dim(order, wide_index * slot_count, slot_count)
    slot_req = slot_blocks // per_request
    slot_start = lookup(lengths, slot_req) + slot_blocks % per_request * blk_len
    slot_pos = slot_start[:, None] + blk_idx[None, :]
    positions = slot_pos.reshape(tok_rows)
    q_proj = jnp.dot(normed, w_q, preferred_element_type=jnp.float32)
    queries = (
        rotate(q_proj.reshape(tok_rows, head_count, HD), positions)
        .astype(jnp.bfloat16)
        .reshape(tok_rows, lane_width)
    )
    all_queries = lax.all_gather(queries, "wide", axis=0, tiled=True)
    all_queries, w_kv_local = lax.optimization_barrier((all_queries, w_qkv[:, 1:]))
    w_kv = lax.all_gather(w_kv_local, "wide", axis=0, tiled=True)

    block_ids = jnp.arange(block_total, dtype=jnp.int32)
    slot_of = jnp.sum(
        jnp.where(order[None, :] == block_ids[:, None], block_ids[None, :], 0), axis=1
    )
    ordered = all_queries.reshape(block_total, blk_len, lane_width)[slot_of].reshape(
        req_count, fresh_len, head_count, HD
    )
    q_heads = jnp.transpose(ordered, (0, 2, 1, 3))

    cache_ids = wide_index * cache_count + jnp.arange(cache_count, dtype=jnp.int32)
    page_ids = jnp.arange(pages.shape[0], dtype=jnp.int32)
    entries = jnp.sum(jnp.where(pages[None, :] == cache_ids[:, None], page_ids[None, :], 0), axis=1)
    cache_req = entries // table_len
    cache_base = (entries % table_len) * blk_len
    cache_limit = lookup(lengths, cache_req)
    cache_keys = jnp.transpose(
        cache[:, :, 0].reshape(cache_count, blk_len, head_count, HD), (0, 2, 1, 3)
    )
    cache_vals = jnp.transpose(
        cache[:, :, 1].reshape(cache_count, blk_len, head_count, HD), (0, 2, 3, 1)
    )
    carry = attend_blocks(
        q_heads, cache_keys, cache_vals, cache_req, cache_base, cache_limit, lengths
    )
    carry, w_out_local = lax.optimization_barrier((carry, w_out))
    part_out = lax.all_gather(w_out_local, "wide", axis=0, tiled=True)

    kv_proj = jnp.einsum("tk,kcj->tcj", normed, w_kv, preferred_element_type=jnp.float32)
    keys_new = (
        rotate(kv_proj[:, 0].reshape(tok_rows, head_count, HD), positions)
        .astype(jnp.bfloat16)
        .reshape(slot_count, blk_len, head_count, HD)
    )
    vals_new = kv_proj[:, 1].astype(jnp.bfloat16).reshape(slot_count, blk_len, head_count, HD)
    new_limit = jnp.full((slot_count,), beyond, jnp.int32)
    head_max, head_den, head_num = attend_blocks(
        q_heads,
        jnp.transpose(keys_new, (0, 2, 1, 3)),
        jnp.transpose(vals_new, (0, 2, 3, 1)),
        slot_req,
        slot_start,
        new_limit,
        lengths,
        carry=carry,
    )

    split = fresh_len // tok_rows
    sent_num = (
        head_num.reshape(req_count, head_count, HD, split, tok_rows)
        .transpose(0, 3, 1, 2, 4)
        .reshape(wide_count, head_count, HD, tok_rows)
        .astype(jnp.bfloat16)
    )
    stats = jnp.concatenate([head_max, head_den], axis=2)
    sent_stats = (
        stats.reshape(req_count, head_count, 2, split, tok_rows)
        .transpose(0, 3, 1, 2, 4)
        .reshape(wide_count, head_count, 2, tok_rows)
    )
    got_num = lax.all_to_all(sent_num, "wide", split_axis=0, concat_axis=0, tiled=True)
    got_stats = lax.all_to_all(sent_stats, "wide", split_axis=0, concat_axis=0, tiled=True)
    got_max = got_stats[:, :, 0:1]
    got_den = got_stats[:, :, 1:2]
    top_max = jnp.max(got_max, axis=0)
    factor = jnp.exp(got_max - top_max[None])
    num_own = jnp.sum(got_num.astype(jnp.float32) * factor, axis=0)
    den_own = jnp.sum(got_den * factor, axis=0)
    attention = (
        jnp.transpose((num_own / den_own).astype(jnp.bfloat16), (2, 0, 1))
        .reshape(tok_rows, lane_width)
    )
    out_part = lax.dot_general(
        attention, part_out, (((1,), (1,)), ((), ())), preferred_element_type=jnp.float32
    )
    return lax.psum_scatter(
        out_part.astype(jnp.bfloat16), "narrow", scatter_dimension=1, tiled=True
    )


def solution(mesh):
    in_specs = (
        P("wide", None),
        P(),
        P("wide", None, "narrow"),
        P("wide", "narrow"),
        P("wide", None, None, "narrow"),
        P(),
        P(),
        P(),
    )
    out_specs = P("wide", "narrow")
    return jax.shard_map(body, mesh=mesh, in_specs=in_specs, out_specs=out_specs, check_vma=False)
```

```python
import jax
import jax.numpy as jnp
from jax import lax
from jax.experimental import pallas as pl
from jax.experimental.pallas import tpu as pltpu
from jax.sharding import PartitionSpec as P

HD = 96


negative = -1e30
beyond = 1073741824


def rotate(values, positions):
    half_dim = values.shape[-1] // 2
    frequency = 10000.0 ** (-2.0 * jnp.arange(half_dim, dtype=jnp.float32) / values.shape[-1])
    angles = positions.astype(jnp.float32)[:, None] * frequency[None, :]
    cos_part = jnp.cos(angles)[:, None, :]
    sin_part = jnp.sin(angles)[:, None, :]
    lower_half = values[..., :half_dim]
    upper_half = values[..., half_dim:]
    return jnp.concatenate(
        [
            lower_half * cos_part - upper_half * sin_part,
            upper_half * cos_part + lower_half * sin_part,
        ],
        axis=-1,
    )


def lookup(small_table, key_index):
    matches = key_index[..., None] == jnp.arange(small_table.shape[0], dtype=jnp.int32)
    return jnp.sum(jnp.where(matches, small_table, 0), axis=-1)


def attend_kernel(carry_in, head_count, head_dim):
    def kernel(req_ref, base_ref, limit_ref, len_ref, *refs):
        if carry_in:
            q_ref, kv_ref, m0_ref, l0_ref, o0_ref, m_ref, l_ref, o_ref = refs
        else:
            q_ref, kv_ref, m_ref, l_ref, o_ref = refs
        step = pl.program_id(0)

        @pl.when(step == 0)
        def _():
            if carry_in:
                m_ref[...] = m0_ref[...]
                l_ref[...] = l0_ref[...]
                o_ref[...] = o0_ref[...]
            else:
                m_ref[...] = jnp.full(m_ref.shape, negative, jnp.float32)
                l_ref[...] = jnp.zeros(l_ref.shape, jnp.float32)
                o_ref[...] = jnp.zeros(o_ref.shape, jnp.float32)

        req = req_ref[step]
        base = base_ref[step]
        limit = limit_ref[step]
        qlen = len_ref[req]
        blk_len = kv_ref.shape[0]
        q_len = q_ref.shape[2]
        scale = head_dim ** (-0.5)
        key_pos = base + lax.broadcasted_iota(jnp.int32, (blk_len, q_len), 0)
        query_pos = qlen + lax.broadcasted_iota(jnp.int32, (blk_len, q_len), 1)
        allowed = (key_pos < limit) & (key_pos <= query_pos)
        for head in range(head_count):
            lanes = pl.ds(head * head_dim, head_dim)
            queries = q_ref[req, head]
            keys = kv_ref[:, 0, lanes]
            vals = kv_ref[:, 1, lanes]
            scores = (
                lax.dot_general(
                    keys, queries, (((1,), (1,)), ((), ())),
                    preferred_element_type=jnp.float32,
                )
                * scale
            )
            masked = jnp.where(allowed, scores, negative)
            m_old = m_ref[req, head]
            m_new = jnp.maximum(m_old, jnp.max(masked, axis=0, keepdims=True))
            exp_terms = jnp.where(allowed, jnp.exp(masked - m_new), 0.0)
            alpha = jnp.exp(m_old - m_new)
            l_ref[req, head] = alpha * l_ref[req, head] + jnp.sum(
                exp_terms, axis=0, keepdims=True
            )
            weighted = lax.dot_general(
                vals, exp_terms.astype(jnp.bfloat16), (((0,), (0,)), ((), ())),
                preferred_element_type=jnp.float32,
            )
            o_ref[req, head] = alpha * o_ref[req, head] + weighted
            m_ref[req, head] = m_new

    return kernel


def attend_blocks(queries, kv, kv_index, blk_req, blk_base, blk_limit, lengths, carry=None):
    req_count, head_count, q_len, head_dim = queries.shape
    blk_count = blk_req.shape[0]
    blk_len = kv.shape[1]
    lane_width = kv.shape[3]
    vmem = pltpu.MemorySpace.VMEM
    whole = pl.BlockSpec(memory_space=vmem)
    in_specs = [
        whole,
        pl.BlockSpec(
            (None, blk_len, 2, lane_width), lambda j, *_: (kv_index(j), 0, 0, 0)
        ),
    ]
    args = [queries, kv]
    if carry is not None:
        in_specs += [whole, whole, whole]
        args += list(carry)
    out_shape = (
        jax.ShapeDtypeStruct((req_count, head_count, 1, q_len), jnp.float32),
        jax.ShapeDtypeStruct((req_count, head_count, 1, q_len), jnp.float32),
        jax.ShapeDtypeStruct((req_count, head_count, head_dim, q_len), jnp.float32),
    )
    grid_spec = pltpu.PrefetchScalarGridSpec(
        num_scalar_prefetch=4,
        grid=(blk_count,),
        in_specs=in_specs,
        out_specs=(whole, whole, whole),
    )
    return pl.pallas_call(
        attend_kernel(carry is not None, head_count, head_dim),
        out_shape=out_shape,
        grid_spec=grid_spec,
        compiler_params=pltpu.CompilerParams(dimension_semantics=("arbitrary",)),
    )(blk_req, blk_base, blk_limit, lengths, *args)


def body(tokens, gain, w_qkv, w_out, cache, lengths, order, pages):
    wide_count = lax.axis_size("wide")
    wide_index = lax.axis_index("wide")
    tok_rows = tokens.shape[0]
    cache_count = cache.shape[0]
    blk_len = cache.shape[1]
    lane_width = cache.shape[3]
    head_count = lane_width // HD
    slot_count = tok_rows // blk_len
    block_total = order.shape[0]
    req_count = lengths.shape[0]
    per_request = block_total // req_count
    fresh_len = per_request * blk_len
    table_len = pages.shape[0] // req_count
    tok_float = tokens.astype(jnp.float32)
    inv_rms = lax.rsqrt(jnp.mean(tok_float * tok_float, axis=1, keepdims=True) + 1e-05)
    normed = (tok_float * inv_rms * gain.astype(jnp.float32)[None, :]).astype(jnp.bfloat16)

    w_q = lax.all_gather(w_qkv[:, 0], "wide", axis=0, tiled=True)
    blk_idx = jnp.arange(blk_len, dtype=jnp.int32)
    slot_blocks = lax.dynamic_slice_in_dim(order, wide_index * slot_count, slot_count)
    slot_req = slot_blocks // per_request
    slot_start = lookup(lengths, slot_req) + slot_blocks % per_request * blk_len
    slot_pos = slot_start[:, None] + blk_idx[None, :]
    positions = slot_pos.reshape(tok_rows)
    q_proj = jnp.dot(normed, w_q, preferred_element_type=jnp.float32)
    queries = (
        rotate(q_proj.reshape(tok_rows, head_count, HD), positions)
        .astype(jnp.bfloat16)
        .reshape(tok_rows, lane_width)
    )
    all_queries = lax.all_gather(queries, "wide", axis=0, tiled=True)
    all_queries, w_kv_local = lax.optimization_barrier((all_queries, w_qkv[:, 1:]))
    w_kv = lax.all_gather(w_kv_local, "wide", axis=0, tiled=True)

    block_ids = jnp.arange(block_total, dtype=jnp.int32)
    slot_of = jnp.sum(
        jnp.where(order[None, :] == block_ids[:, None], block_ids[None, :], 0), axis=1
    )
    ordered = all_queries.reshape(block_total, blk_len, lane_width)[slot_of].reshape(
        req_count, fresh_len, head_count, HD
    )
    q_heads = jnp.transpose(ordered, (0, 2, 1, 3))

    cache_ids = wide_index * cache_count + jnp.arange(cache_count, dtype=jnp.int32)
    page_ids = jnp.arange(pages.shape[0], dtype=jnp.int32)
    entries = jnp.sum(jnp.where(pages[None, :] == cache_ids[:, None], page_ids[None, :], 0), axis=1)
    cache_req = entries // table_len
    cache_base = (entries % table_len) * blk_len
    cache_limit = lookup(lengths, cache_req)
    carry = attend_blocks(
        q_heads, cache, lambda j: j, cache_req, cache_base, cache_limit, lengths
    )
    carry, w_out_local = lax.optimization_barrier((carry, w_out))
    part_out = lax.all_gather(w_out_local, "wide", axis=0, tiled=True)

    kv_proj = jnp.einsum("tk,kcj->tcj", normed, w_kv, preferred_element_type=jnp.float32)
    keys_new = (
        rotate(kv_proj[:, 0].reshape(tok_rows, head_count, HD), positions)
        .astype(jnp.bfloat16)
        .reshape(tok_rows, lane_width)
    )
    vals_new = kv_proj[:, 1].astype(jnp.bfloat16)
    new_limit = jnp.full((slot_count,), beyond, jnp.int32)
    kv_new = jnp.stack([keys_new, vals_new], axis=1).reshape(
        slot_count, blk_len, 2, lane_width
    )
    head_max, head_den, head_num = attend_blocks(
        q_heads,
        kv_new,
        lambda j: j,
        slot_req,
        slot_start,
        new_limit,
        lengths,
        carry=carry,
    )

    split = fresh_len // tok_rows
    sent_num = (
        head_num.reshape(req_count, head_count, HD, split, tok_rows)
        .transpose(0, 3, 1, 2, 4)
        .reshape(wide_count, head_count, HD, tok_rows)
        .astype(jnp.bfloat16)
    )
    stats = jnp.concatenate([head_max, head_den], axis=2)
    sent_stats = (
        stats.reshape(req_count, head_count, 2, split, tok_rows)
        .transpose(0, 3, 1, 2, 4)
        .reshape(wide_count, head_count, 2, tok_rows)
    )
    got_num = lax.all_to_all(sent_num, "wide", split_axis=0, concat_axis=0, tiled=True)
    got_stats = lax.all_to_all(sent_stats, "wide", split_axis=0, concat_axis=0, tiled=True)
    got_max = got_stats[:, :, 0:1]
    got_den = got_stats[:, :, 1:2]
    top_max = jnp.max(got_max, axis=0)
    factor = jnp.exp(got_max - top_max[None])
    num_own = jnp.sum(got_num.astype(jnp.float32) * factor, axis=0)
    den_own = jnp.sum(got_den * factor, axis=0)
    attention = (
        jnp.transpose((num_own / den_own).astype(jnp.bfloat16), (2, 0, 1))
        .reshape(tok_rows, lane_width)
    )
    out_part = lax.dot_general(
        attention, part_out, (((1,), (1,)), ((), ())), preferred_element_type=jnp.float32
    )
    narrow_count = lax.axis_size("narrow")
    out_cols = out_part.shape[1] // narrow_count
    sent_out = jnp.transpose(
        out_part.astype(jnp.bfloat16).reshape(tok_rows, narrow_count, out_cols), (1, 0, 2)
    )
    got_out = lax.all_to_all(sent_out, "narrow", split_axis=0, concat_axis=0, tiled=True)
    return jnp.sum(got_out.astype(jnp.float32), axis=0).astype(jnp.bfloat16)


def solution(mesh):
    in_specs = (
        P("wide", None),
        P(),
        P("wide", None, "narrow"),
        P("wide", "narrow"),
        P("wide", None, None, "narrow"),
        P(),
        P(),
        P(),
    )
    out_specs = P("wide", "narrow")
    return jax.shard_map(body, mesh=mesh, in_specs=in_specs, out_specs=out_specs, check_vma=False)
```

```python
import jax
import jax.numpy as jnp
from jax import lax
from jax.experimental import pallas as pl
from jax.experimental.pallas import tpu as pltpu
from jax.sharding import PartitionSpec as P

HD = 96


negative = -1e30
beyond = 1073741824


def rotate(values, positions):
    half_dim = values.shape[-1] // 2
    frequency = 10000.0 ** (-2.0 * jnp.arange(half_dim, dtype=jnp.float32) / values.shape[-1])
    angles = positions.astype(jnp.float32)[:, None] * frequency[None, :]
    cos_part = jnp.cos(angles)[:, None, :]
    sin_part = jnp.sin(angles)[:, None, :]
    lower_half = values[..., :half_dim]
    upper_half = values[..., half_dim:]
    return jnp.concatenate(
        [
            lower_half * cos_part - upper_half * sin_part,
            upper_half * cos_part + lower_half * sin_part,
        ],
        axis=-1,
    )


def lookup(small_table, key_index):
    matches = key_index[..., None] == jnp.arange(small_table.shape[0], dtype=jnp.int32)
    return jnp.sum(jnp.where(matches, small_table, 0), axis=-1)


def attend_kernel(carry_in):
    def kernel(req_ref, base_ref, limit_ref, len_ref, *refs):
        if carry_in:
            q_ref, k_ref, v_ref, m0_ref, l0_ref, o0_ref, m_ref, l_ref, o_ref = refs
        else:
            q_ref, k_ref, v_ref, m_ref, l_ref, o_ref = refs
        step = pl.program_id(0)

        @pl.when(step == 0)
        def _():
            if carry_in:
                m_ref[...] = m0_ref[...]
                l_ref[...] = l0_ref[...]
                o_ref[...] = o0_ref[...]
            else:
                m_ref[...] = jnp.full(m_ref.shape, negative, jnp.float32)
                l_ref[...] = jnp.zeros(l_ref.shape, jnp.float32)
                o_ref[...] = jnp.zeros(o_ref.shape, jnp.float32)

        req = req_ref[step]
        base = base_ref[step]
        limit = limit_ref[step]
        qlen = len_ref[req]
        queries = q_ref[req]
        keys = k_ref[0]
        vals = v_ref[0]
        blk_len = keys.shape[1]
        q_len = queries.shape[1]
        scale = keys.shape[-1] ** (-0.5)
        scores = (
            jnp.einsum("hkd,hqd->hkq", keys, queries, preferred_element_type=jnp.float32)
            * scale
        )
        key_pos = base + lax.broadcasted_iota(jnp.int32, (blk_len, q_len), 0)
        query_pos = qlen + lax.broadcasted_iota(jnp.int32, (blk_len, q_len), 1)
        allowed = ((key_pos < limit) & (key_pos <= query_pos))[None]
        masked = jnp.where(allowed, scores, negative)
        m_old = m_ref[req]
        m_new = jnp.maximum(m_old, jnp.max(masked, axis=1, keepdims=True))
        exp_terms = jnp.where(allowed, jnp.exp(masked - m_new), 0.0)
        alpha = jnp.exp(m_old - m_new)
        l_ref[req] = alpha * l_ref[req] + jnp.sum(exp_terms, axis=1, keepdims=True)
        weighted = jnp.einsum(
            "hdk,hkq->hdq", vals, exp_terms.astype(jnp.bfloat16),
            preferred_element_type=jnp.float32,
        )
        o_ref[req] = alpha * o_ref[req] + weighted
        m_ref[req] = m_new

    return kernel


def attend_blocks(queries, keys, vals_t, blk_req, blk_base, blk_limit, lengths, carry=None):
    req_count, head_count, q_len, head_dim = queries.shape
    blk_count, _, blk_len, _ = keys.shape
    vmem = pltpu.MemorySpace.VMEM
    whole = pl.BlockSpec(memory_space=vmem)
    in_specs = [
        whole,
        pl.BlockSpec((1, head_count, blk_len, head_dim), lambda j, *_: (j, 0, 0, 0)),
        pl.BlockSpec((1, head_count, head_dim, blk_len), lambda j, *_: (j, 0, 0, 0)),
    ]
    args = [queries, keys, vals_t]
    if carry is not None:
        in_specs += [whole, whole, whole]
        args += list(carry)
    out_shape = (
        jax.ShapeDtypeStruct((req_count, head_count, 1, q_len), jnp.float32),
        jax.ShapeDtypeStruct((req_count, head_count, 1, q_len), jnp.float32),
        jax.ShapeDtypeStruct((req_count, head_count, head_dim, q_len), jnp.float32),
    )
    grid_spec = pltpu.PrefetchScalarGridSpec(
        num_scalar_prefetch=4,
        grid=(blk_count,),
        in_specs=in_specs,
        out_specs=(whole, whole, whole),
    )
    return pl.pallas_call(
        attend_kernel(carry is not None),
        out_shape=out_shape,
        grid_spec=grid_spec,
        compiler_params=pltpu.CompilerParams(
            dimension_semantics=("arbitrary",)
        ),
    )(blk_req, blk_base, blk_limit, lengths, *args)


def body(tokens, gain, w_qkv, w_out, cache, lengths, order, pages):
    wide_count = lax.axis_size("wide")
    wide_index = lax.axis_index("wide")
    tok_rows = tokens.shape[0]
    cache_count = cache.shape[0]
    blk_len = cache.shape[1]
    lane_width = cache.shape[3]
    head_count = lane_width // HD
    slot_count = tok_rows // blk_len
    block_total = order.shape[0]
    req_count = lengths.shape[0]
    per_request = block_total // req_count
    fresh_len = per_request * blk_len
    table_len = pages.shape[0] // req_count
    tok_float = tokens.astype(jnp.float32)
    inv_rms = lax.rsqrt(jnp.mean(tok_float * tok_float, axis=1, keepdims=True) + 1e-05)
    normed = (tok_float * inv_rms * gain.astype(jnp.float32)[None, :]).astype(jnp.bfloat16)

    w_q = lax.all_gather(w_qkv[:, 0], "wide", axis=0, tiled=True)
    cache_ids = wide_index * cache_count + jnp.arange(cache_count, dtype=jnp.int32)
    page_ids = jnp.arange(pages.shape[0], dtype=jnp.int32)
    entries = jnp.sum(jnp.where(pages[None, :] == cache_ids[:, None], page_ids[None, :], 0), axis=1)
    cache_req = entries // table_len
    cache_base = (entries % table_len) * blk_len
    cache_limit = lookup(lengths, cache_req)
    cache_keys = jnp.transpose(
        cache[:, :, 0].reshape(cache_count, blk_len, head_count, HD), (0, 2, 1, 3)
    )
    cache_vals = jnp.transpose(
        cache[:, :, 1].reshape(cache_count, blk_len, head_count, HD), (0, 2, 3, 1)
    )
    w_q, cache_keys, cache_vals = lax.optimization_barrier((w_q, cache_keys, cache_vals))
    blk_idx = jnp.arange(blk_len, dtype=jnp.int32)
    slot_blocks = lax.dynamic_slice_in_dim(order, wide_index * slot_count, slot_count)
    slot_req = slot_blocks // per_request
    slot_start = lookup(lengths, slot_req) + slot_blocks % per_request * blk_len
    slot_pos = slot_start[:, None] + blk_idx[None, :]
    positions = slot_pos.reshape(tok_rows)
    q_proj = jnp.dot(normed, w_q, preferred_element_type=jnp.float32)
    queries = (
        rotate(q_proj.reshape(tok_rows, head_count, HD), positions)
        .astype(jnp.bfloat16)
        .reshape(tok_rows, lane_width)
    )
    all_queries = lax.all_gather(queries, "wide", axis=0, tiled=True)
    all_queries, w_kv_local = lax.optimization_barrier((all_queries, w_qkv[:, 1:]))
    w_kv = lax.all_gather(w_kv_local, "wide", axis=0, tiled=True)

    block_ids = jnp.arange(block_total, dtype=jnp.int32)
    slot_of = jnp.sum(
        jnp.where(order[None, :] == block_ids[:, None], block_ids[None, :], 0), axis=1
    )
    ordered = all_queries.reshape(block_total, blk_len, lane_width)[slot_of].reshape(
        req_count, fresh_len, head_count, HD
    )
    q_heads = jnp.transpose(ordered, (0, 2, 1, 3))

    carry = attend_blocks(
        q_heads, cache_keys, cache_vals, cache_req, cache_base, cache_limit, lengths
    )
    carry, w_out_local = lax.optimization_barrier((carry, w_out))
    part_out = lax.all_gather(w_out_local, "wide", axis=0, tiled=True)

    kv_proj = jnp.einsum("tk,kcj->tcj", normed, w_kv, preferred_element_type=jnp.float32)
    keys_new = (
        rotate(kv_proj[:, 0].reshape(tok_rows, head_count, HD), positions)
        .astype(jnp.bfloat16)
        .reshape(slot_count, blk_len, head_count, HD)
    )
    vals_new = kv_proj[:, 1].astype(jnp.bfloat16).reshape(slot_count, blk_len, head_count, HD)
    new_limit = jnp.full((slot_count,), beyond, jnp.int32)
    head_max, head_den, head_num = attend_blocks(
        q_heads,
        jnp.transpose(keys_new, (0, 2, 1, 3)),
        jnp.transpose(vals_new, (0, 2, 3, 1)),
        slot_req,
        slot_start,
        new_limit,
        lengths,
        carry=carry,
    )

    split = fresh_len // tok_rows
    sent_num = (
        head_num.reshape(req_count, head_count, HD, split, tok_rows)
        .transpose(0, 3, 1, 2, 4)
        .reshape(wide_count, head_count, HD, tok_rows)
        .astype(jnp.bfloat16)
    )
    stats = jnp.concatenate([head_max, head_den], axis=2)
    sent_stats = (
        stats.reshape(req_count, head_count, 2, split, tok_rows)
        .transpose(0, 3, 1, 2, 4)
        .reshape(wide_count, head_count, 2, tok_rows)
    )
    got_num = lax.all_to_all(sent_num, "wide", split_axis=0, concat_axis=0, tiled=True)
    got_stats = lax.all_to_all(sent_stats, "wide", split_axis=0, concat_axis=0, tiled=True)
    got_max = got_stats[:, :, 0:1]
    got_den = got_stats[:, :, 1:2]
    top_max = jnp.max(got_max, axis=0)
    factor = jnp.exp(got_max - top_max[None])
    num_own = jnp.sum(got_num.astype(jnp.float32) * factor, axis=0)
    den_own = jnp.sum(got_den * factor, axis=0)
    attention = (
        jnp.transpose((num_own / den_own).astype(jnp.bfloat16), (2, 0, 1))
        .reshape(tok_rows, lane_width)
    )
    out_part = lax.dot_general(
        attention, part_out, (((1,), (1,)), ((), ())), preferred_element_type=jnp.float32
    )
    return lax.psum_scatter(
        out_part.astype(jnp.bfloat16), "narrow", scatter_dimension=1, tiled=True
    )


def solution(mesh):
    in_specs = (
        P("wide", None),
        P(),
        P("wide", None, "narrow"),
        P("wide", "narrow"),
        P("wide", None, None, "narrow"),
        P(),
        P(),
        P(),
    )
    out_specs = P("wide", "narrow")
    return jax.shard_map(body, mesh=mesh, in_specs=in_specs, out_specs=out_specs, check_vma=False)
```

```python
import jax
import jax.numpy as jnp
from jax import lax
from jax.experimental import pallas as pl
from jax.experimental.pallas import tpu as pltpu
from jax.sharding import PartitionSpec as P

HD = 96


negative = -1e30
beyond = 1073741824


def rotate(values, positions):
    half_dim = values.shape[-1] // 2
    frequency = 10000.0 ** (-2.0 * jnp.arange(half_dim, dtype=jnp.float32) / values.shape[-1])
    angles = positions.astype(jnp.float32)[:, None] * frequency[None, :]
    cos_part = jnp.cos(angles)[:, None, :]
    sin_part = jnp.sin(angles)[:, None, :]
    lower_half = values[..., :half_dim]
    upper_half = values[..., half_dim:]
    return jnp.concatenate(
        [
            lower_half * cos_part - upper_half * sin_part,
            upper_half * cos_part + lower_half * sin_part,
        ],
        axis=-1,
    )


def lookup(small_table, key_index):
    matches = key_index[..., None] == jnp.arange(small_table.shape[0], dtype=jnp.int32)
    return jnp.sum(jnp.where(matches, small_table, 0), axis=-1)


def attend_kernel(carry_in):
    def kernel(req_ref, base_ref, limit_ref, len_ref, slot_ref, *refs):
        if carry_in:
            q_ref, k_ref, v_ref, m0_ref, l0_ref, o0_ref, m_ref, l_ref, o_ref = refs
        else:
            q_ref, k_ref, v_ref, m_ref, l_ref, o_ref = refs
        step = pl.program_id(0)

        @pl.when(step == 0)
        def _():
            if carry_in:
                m_ref[...] = m0_ref[...]
                l_ref[...] = l0_ref[...]
                o_ref[...] = o0_ref[...]
            else:
                m_ref[...] = jnp.full(m_ref.shape, negative, jnp.float32)
                l_ref[...] = jnp.zeros(l_ref.shape, jnp.float32)
                o_ref[...] = jnp.zeros(o_ref.shape, jnp.float32)

        req = req_ref[step]
        base = base_ref[step]
        limit = limit_ref[step]
        qlen = len_ref[req]
        per_request = slot_ref.shape[0] // len_ref.shape[0]
        queries = jnp.concatenate(
            [q_ref[:, slot_ref[req * per_request + i]] for i in range(per_request)], axis=1
        )
        keys = k_ref[0]
        vals = v_ref[0]
        blk_len = keys.shape[1]
        q_len = queries.shape[1]
        scale = keys.shape[-1] ** (-0.5)
        scores = (
            jnp.einsum("hkd,hqd->hkq", keys, queries, preferred_element_type=jnp.float32)
            * scale
        )
        key_pos = base + lax.broadcasted_iota(jnp.int32, (blk_len, q_len), 0)
        query_pos = qlen + lax.broadcasted_iota(jnp.int32, (blk_len, q_len), 1)
        allowed = ((key_pos < limit) & (key_pos <= query_pos))[None]
        masked = jnp.where(allowed, scores, negative)
        m_old = m_ref[req]
        m_new = jnp.maximum(m_old, jnp.max(masked, axis=1, keepdims=True))
        exp_terms = jnp.where(allowed, jnp.exp(masked - m_new), 0.0)
        alpha = jnp.exp(m_old - m_new)
        l_ref[req] = alpha * l_ref[req] + jnp.sum(exp_terms, axis=1, keepdims=True)
        weighted = jnp.einsum(
            "hdk,hkq->hdq", vals, exp_terms.astype(jnp.bfloat16),
            preferred_element_type=jnp.float32,
        )
        o_ref[req] = alpha * o_ref[req] + weighted
        m_ref[req] = m_new

    return kernel


def attend_blocks(
    queries, keys, vals_t, blk_req, blk_base, blk_limit, lengths, slot_of, carry=None
):
    head_count, _, blk_len, head_dim = queries.shape
    req_count = lengths.shape[0]
    q_len = slot_of.shape[0] // req_count * blk_len
    blk_count = keys.shape[0]
    vmem = pltpu.MemorySpace.VMEM
    whole = pl.BlockSpec(memory_space=vmem)
    in_specs = [
        whole,
        pl.BlockSpec((1, head_count, blk_len, head_dim), lambda j, *_: (j, 0, 0, 0)),
        pl.BlockSpec((1, head_count, head_dim, blk_len), lambda j, *_: (j, 0, 0, 0)),
    ]
    args = [queries, keys, vals_t]
    if carry is not None:
        in_specs += [whole, whole, whole]
        args += list(carry)
    out_shape = (
        jax.ShapeDtypeStruct((req_count, head_count, 1, q_len), jnp.float32),
        jax.ShapeDtypeStruct((req_count, head_count, 1, q_len), jnp.float32),
        jax.ShapeDtypeStruct((req_count, head_count, head_dim, q_len), jnp.float32),
    )
    grid_spec = pltpu.PrefetchScalarGridSpec(
        num_scalar_prefetch=5,
        grid=(blk_count,),
        in_specs=in_specs,
        out_specs=(whole, whole, whole),
    )
    return pl.pallas_call(
        attend_kernel(carry is not None),
        out_shape=out_shape,
        grid_spec=grid_spec,
        compiler_params=pltpu.CompilerParams(
            dimension_semantics=("arbitrary",)
        ),
    )(blk_req, blk_base, blk_limit, lengths, slot_of, *args)


def body(tokens, gain, w_qkv, w_out, cache, lengths, order, pages):
    wide_count = lax.axis_size("wide")
    wide_index = lax.axis_index("wide")
    tok_rows = tokens.shape[0]
    cache_count = cache.shape[0]
    blk_len = cache.shape[1]
    lane_width = cache.shape[3]
    head_count = lane_width // HD
    slot_count = tok_rows // blk_len
    block_total = order.shape[0]
    req_count = lengths.shape[0]
    per_request = block_total // req_count
    fresh_len = per_request * blk_len
    table_len = pages.shape[0] // req_count
    tok_float = tokens.astype(jnp.float32)
    inv_rms = lax.rsqrt(jnp.mean(tok_float * tok_float, axis=1, keepdims=True) + 1e-05)
    normed = (tok_float * inv_rms * gain.astype(jnp.float32)[None, :]).astype(jnp.bfloat16)

    w_q = lax.all_gather(w_qkv[:, 0], "wide", axis=0, tiled=True)
    cache_ids = wide_index * cache_count + jnp.arange(cache_count, dtype=jnp.int32)
    page_ids = jnp.arange(pages.shape[0], dtype=jnp.int32)
    entries = jnp.sum(jnp.where(pages[None, :] == cache_ids[:, None], page_ids[None, :], 0), axis=1)
    cache_req = entries // table_len
    cache_base = (entries % table_len) * blk_len
    cache_limit = lookup(lengths, cache_req)
    cache_keys = jnp.transpose(
        cache[:, :, 0].reshape(cache_count, blk_len, head_count, HD), (0, 2, 1, 3)
    )
    w_q, cache_keys = lax.optimization_barrier((w_q, cache_keys))
    blk_idx = jnp.arange(blk_len, dtype=jnp.int32)
    slot_blocks = lax.dynamic_slice_in_dim(order, wide_index * slot_count, slot_count)
    slot_req = slot_blocks // per_request
    slot_start = lookup(lengths, slot_req) + slot_blocks % per_request * blk_len
    slot_pos = slot_start[:, None] + blk_idx[None, :]
    positions = slot_pos.reshape(tok_rows)
    q_proj = jnp.dot(normed, w_q, preferred_element_type=jnp.float32)
    queries = jnp.transpose(
        rotate(q_proj.reshape(tok_rows, head_count, HD), positions)
        .astype(jnp.bfloat16)
        .reshape(slot_count, blk_len, head_count, HD),
        (2, 0, 1, 3),
    )
    all_queries = lax.all_gather(queries, "wide", axis=1, tiled=True)
    queries, cache_v = lax.optimization_barrier((queries, cache))
    cache_vals = jnp.transpose(
        cache_v[:, :, 1].reshape(cache_count, blk_len, head_count, HD), (0, 2, 3, 1)
    )
    all_queries, cache_vals, w_kv_local = lax.optimization_barrier(
        (all_queries, cache_vals, w_qkv[:, 1:])
    )
    w_kv = lax.all_gather(w_kv_local, "wide", axis=0, tiled=True)

    block_ids = jnp.arange(block_total, dtype=jnp.int32)
    slot_of = jnp.sum(
        jnp.where(order[None, :] == block_ids[:, None], block_ids[None, :], 0), axis=1
    )
    q_heads = all_queries

    carry = attend_blocks(
        q_heads, cache_keys, cache_vals, cache_req, cache_base, cache_limit, lengths, slot_of
    )
    carry, w_out_local = lax.optimization_barrier((carry, w_out))
    part_out = lax.all_gather(w_out_local, "wide", axis=0, tiled=True)

    kv_proj = jnp.einsum("tk,kcj->tcj", normed, w_kv, preferred_element_type=jnp.float32)
    keys_new = (
        rotate(kv_proj[:, 0].reshape(tok_rows, head_count, HD), positions)
        .astype(jnp.bfloat16)
        .reshape(slot_count, blk_len, head_count, HD)
    )
    vals_new = kv_proj[:, 1].astype(jnp.bfloat16).reshape(slot_count, blk_len, head_count, HD)
    new_limit = jnp.full((slot_count,), beyond, jnp.int32)
    head_max, head_den, head_num = attend_blocks(
        q_heads,
        jnp.transpose(keys_new, (0, 2, 1, 3)),
        jnp.transpose(vals_new, (0, 2, 3, 1)),
        slot_req,
        slot_start,
        new_limit,
        lengths,
        slot_of,
        carry=carry,
    )

    split = fresh_len // tok_rows
    sent_num = (
        head_num.reshape(req_count, head_count, HD, split, tok_rows)
        .transpose(0, 3, 1, 2, 4)
        .reshape(wide_count, head_count, HD, tok_rows)
        .astype(jnp.bfloat16)
    )
    stats = jnp.concatenate([head_max, head_den], axis=2)
    sent_stats = (
        stats.reshape(req_count, head_count, 2, split, tok_rows)
        .transpose(0, 3, 1, 2, 4)
        .reshape(wide_count, head_count, 2, tok_rows)
    )
    got_num = lax.all_to_all(sent_num, "wide", split_axis=0, concat_axis=0, tiled=True)
    got_stats = lax.all_to_all(sent_stats, "wide", split_axis=0, concat_axis=0, tiled=True)
    got_max = got_stats[:, :, 0:1]
    got_den = got_stats[:, :, 1:2]
    top_max = jnp.max(got_max, axis=0)
    factor = jnp.exp(got_max - top_max[None])
    num_own = jnp.sum(got_num.astype(jnp.float32) * factor, axis=0)
    den_own = jnp.sum(got_den * factor, axis=0)
    attention = (
        jnp.transpose((num_own / den_own).astype(jnp.bfloat16), (2, 0, 1))
        .reshape(tok_rows, lane_width)
    )
    out_part = lax.dot_general(
        attention, part_out, (((1,), (1,)), ((), ())), preferred_element_type=jnp.float32
    )
    return lax.psum_scatter(
        out_part.astype(jnp.bfloat16), "narrow", scatter_dimension=1, tiled=True
    )


def solution(mesh):
    in_specs = (
        P("wide", None),
        P(),
        P("wide", None, "narrow"),
        P("wide", "narrow"),
        P("wide", None, None, "narrow"),
        P(),
        P(),
        P(),
    )
    out_specs = P("wide", "narrow")
    return jax.shard_map(body, mesh=mesh, in_specs=in_specs, out_specs=out_specs, check_vma=False)
```

```python
import jax
import jax.numpy as jnp
from jax import lax
from jax.experimental import pallas as pl
from jax.experimental.pallas import tpu as pltpu
from jax.sharding import PartitionSpec as P

HD = 96


negative = -1e30
beyond = 1073741824


def rotate(values, positions):
    half_dim = values.shape[-1] // 2
    frequency = 10000.0 ** (-2.0 * jnp.arange(half_dim, dtype=jnp.float32) / values.shape[-1])
    angles = positions.astype(jnp.float32)[:, None] * frequency[None, :]
    cos_part = jnp.cos(angles)[:, None, :]
    sin_part = jnp.sin(angles)[:, None, :]
    lower_half = values[..., :half_dim]
    upper_half = values[..., half_dim:]
    return jnp.concatenate(
        [
            lower_half * cos_part - upper_half * sin_part,
            upper_half * cos_part + lower_half * sin_part,
        ],
        axis=-1,
    )


def lookup(small_table, key_index):
    matches = key_index[..., None] == jnp.arange(small_table.shape[0], dtype=jnp.int32)
    return jnp.sum(jnp.where(matches, small_table, 0), axis=-1)


def block_step(step, scalars, q_ref, k_ref, v_ref, m_ref, l_ref, o_ref):
    req_ref, base_ref, limit_ref, len_ref, slot_ref = scalars
    req = req_ref[step]
    base = base_ref[step]
    limit = limit_ref[step]
    qlen = len_ref[req]
    per_request = slot_ref.shape[0] // len_ref.shape[0]
    queries = jnp.concatenate(
        [q_ref[:, slot_ref[req * per_request + i]] for i in range(per_request)], axis=1
    )
    keys = k_ref[0]
    vals = v_ref[0]
    blk_len = keys.shape[1]
    q_len = queries.shape[1]
    scale = keys.shape[-1] ** (-0.5)
    scores = (
        jnp.einsum("hkd,hqd->hkq", keys, queries, preferred_element_type=jnp.float32)
        * scale
    )
    key_pos = base + lax.broadcasted_iota(jnp.int32, (blk_len, q_len), 0)
    query_pos = qlen + lax.broadcasted_iota(jnp.int32, (blk_len, q_len), 1)
    allowed = ((key_pos < limit) & (key_pos <= query_pos))[None]
    masked = jnp.where(allowed, scores, negative)
    m_old = m_ref[req]
    m_new = jnp.maximum(m_old, jnp.max(masked, axis=1, keepdims=True))
    exp_terms = jnp.where(allowed, jnp.exp(masked - m_new), 0.0)
    alpha = jnp.exp(m_old - m_new)
    l_ref[req] = alpha * l_ref[req] + jnp.sum(exp_terms, axis=1, keepdims=True)
    weighted = jnp.einsum(
        "hdk,hkq->hdq", vals, exp_terms.astype(jnp.bfloat16),
        preferred_element_type=jnp.float32,
    )
    o_ref[req] = alpha * o_ref[req] + weighted
    m_ref[req] = m_new


def attend_kernel(cache_count):
    def kernel(req_ref, base_ref, limit_ref, len_ref, slot_ref, *refs):
        q_ref, kc_ref, vc_ref, kn_ref, vn_ref, m_ref, l_ref, o_ref = refs
        scalars = (req_ref, base_ref, limit_ref, len_ref, slot_ref)
        step = pl.program_id(0)

        @pl.when(step == 0)
        def _():
            m_ref[...] = jnp.full(m_ref.shape, negative, jnp.float32)
            l_ref[...] = jnp.zeros(l_ref.shape, jnp.float32)
            o_ref[...] = jnp.zeros(o_ref.shape, jnp.float32)

        @pl.when(step < cache_count)
        def _():
            block_step(step, scalars, q_ref, kc_ref, vc_ref, m_ref, l_ref, o_ref)

        @pl.when(step >= cache_count)
        def _():
            block_step(step, scalars, q_ref, kn_ref, vn_ref, m_ref, l_ref, o_ref)

    return kernel


def attend_blocks(
    queries, cache_keys, cache_vals, new_keys, new_vals,
    blk_req, blk_base, blk_limit, lengths, slot_of,
):
    head_count, _, blk_len, head_dim = queries.shape
    req_count = lengths.shape[0]
    q_len = slot_of.shape[0] // req_count * blk_len
    cache_count = cache_keys.shape[0]
    new_count = new_keys.shape[0]
    vmem = pltpu.MemorySpace.VMEM
    whole = pl.BlockSpec(memory_space=vmem)

    def cache_block(j, *_):
        return (jnp.minimum(j, cache_count - 1), 0, 0, 0)

    def new_block(j, *_):
        return (jnp.maximum(j - cache_count, 0), 0, 0, 0)

    key_shape = (1, head_count, blk_len, head_dim)
    val_shape = (1, head_count, head_dim, blk_len)
    in_specs = [
        whole,
        pl.BlockSpec(key_shape, cache_block),
        pl.BlockSpec(val_shape, cache_block),
        pl.BlockSpec(key_shape, new_block),
        pl.BlockSpec(val_shape, new_block),
    ]
    out_shape = (
        jax.ShapeDtypeStruct((req_count, head_count, 1, q_len), jnp.float32),
        jax.ShapeDtypeStruct((req_count, head_count, 1, q_len), jnp.float32),
        jax.ShapeDtypeStruct((req_count, head_count, head_dim, q_len), jnp.float32),
    )
    grid_spec = pltpu.PrefetchScalarGridSpec(
        num_scalar_prefetch=5,
        grid=(cache_count + new_count,),
        in_specs=in_specs,
        out_specs=(whole, whole, whole),
    )
    return pl.pallas_call(
        attend_kernel(cache_count),
        out_shape=out_shape,
        grid_spec=grid_spec,
        compiler_params=pltpu.CompilerParams(dimension_semantics=("arbitrary",)),
    )(blk_req, blk_base, blk_limit, lengths, slot_of,
      queries, cache_keys, cache_vals, new_keys, new_vals)


def body(tokens, gain, w_qkv, w_out, cache, lengths, order, pages):
    wide_count = lax.axis_size("wide")
    wide_index = lax.axis_index("wide")
    tok_rows = tokens.shape[0]
    cache_count = cache.shape[0]
    blk_len = cache.shape[1]
    lane_width = cache.shape[3]
    head_count = lane_width // HD
    slot_count = tok_rows // blk_len
    block_total = order.shape[0]
    req_count = lengths.shape[0]
    per_request = block_total // req_count
    fresh_len = per_request * blk_len
    table_len = pages.shape[0] // req_count
    tok_float = tokens.astype(jnp.float32)
    inv_rms = lax.rsqrt(jnp.mean(tok_float * tok_float, axis=1, keepdims=True) + 1e-05)
    normed = (tok_float * inv_rms * gain.astype(jnp.float32)[None, :]).astype(jnp.bfloat16)

    w_q = lax.all_gather(w_qkv[:, 0], "wide", axis=0, tiled=True)
    w_kv_local = w_qkv[:, 1:]
    w_kv = lax.all_to_all(
        jnp.broadcast_to(w_kv_local[None], (wide_count,) + w_kv_local.shape),
        "wide", split_axis=0, concat_axis=0, tiled=True,
    ).reshape((wide_count * w_kv_local.shape[0],) + w_kv_local.shape[1:])
    cache_ids = wide_index * cache_count + jnp.arange(cache_count, dtype=jnp.int32)
    page_ids = jnp.arange(pages.shape[0], dtype=jnp.int32)
    entries = jnp.sum(jnp.where(pages[None, :] == cache_ids[:, None], page_ids[None, :], 0), axis=1)
    cache_req = entries // table_len
    cache_base = (entries % table_len) * blk_len
    cache_limit = lookup(lengths, cache_req)
    cache_keys = jnp.transpose(
        cache[:, :, 0].reshape(cache_count, blk_len, head_count, HD), (0, 2, 1, 3)
    )
    w_q, cache_keys = lax.optimization_barrier((w_q, cache_keys))
    blk_idx = jnp.arange(blk_len, dtype=jnp.int32)
    slot_blocks = lax.dynamic_slice_in_dim(order, wide_index * slot_count, slot_count)
    slot_req = slot_blocks // per_request
    slot_start = lookup(lengths, slot_req) + slot_blocks % per_request * blk_len
    slot_pos = slot_start[:, None] + blk_idx[None, :]
    positions = slot_pos.reshape(tok_rows)
    q_proj = jnp.dot(normed, w_q, preferred_element_type=jnp.float32)
    queries = jnp.transpose(
        rotate(q_proj.reshape(tok_rows, head_count, HD), positions)
        .astype(jnp.bfloat16)
        .reshape(slot_count, blk_len, head_count, HD),
        (2, 0, 1, 3),
    )
    all_queries = lax.all_gather(queries, "wide", axis=1, tiled=True)
    queries, cache_v = lax.optimization_barrier((queries, cache))
    cache_vals = jnp.transpose(
        cache_v[:, :, 1].reshape(cache_count, blk_len, head_count, HD), (0, 2, 3, 1)
    )
    all_queries, cache_vals = lax.optimization_barrier((all_queries, cache_vals))

    block_ids = jnp.arange(block_total, dtype=jnp.int32)
    slot_of = jnp.sum(
        jnp.where(order[None, :] == block_ids[:, None], block_ids[None, :], 0), axis=1
    )
    q_heads = all_queries

    all_queries, w_out_local = lax.optimization_barrier((all_queries, w_out))
    part_out = lax.all_gather(w_out_local, "wide", axis=0, tiled=True)

    kv_proj = jnp.einsum("tk,kcj->tcj", normed, w_kv, preferred_element_type=jnp.float32)
    keys_new = (
        rotate(kv_proj[:, 0].reshape(tok_rows, head_count, HD), positions)
        .astype(jnp.bfloat16)
        .reshape(slot_count, blk_len, head_count, HD)
    )
    vals_new = kv_proj[:, 1].astype(jnp.bfloat16).reshape(slot_count, blk_len, head_count, HD)
    new_limit = jnp.full((slot_count,), beyond, jnp.int32)
    head_max, head_den, head_num = attend_blocks(
        q_heads,
        cache_keys,
        cache_vals,
        jnp.transpose(keys_new, (0, 2, 1, 3)),
        jnp.transpose(vals_new, (0, 2, 3, 1)),
        jnp.concatenate([cache_req, slot_req]),
        jnp.concatenate([cache_base, slot_start]),
        jnp.concatenate([cache_limit, new_limit]),
        lengths,
        slot_of,
    )

    split = fresh_len // tok_rows
    sent_num = (
        head_num.reshape(req_count, head_count, HD, split, tok_rows)
        .transpose(0, 3, 1, 2, 4)
        .reshape(wide_count, head_count, HD, tok_rows)
        .astype(jnp.bfloat16)
    )
    stats = jnp.concatenate([head_max, head_den], axis=2)
    sent_stats = (
        stats.reshape(req_count, head_count, 2, split, tok_rows)
        .transpose(0, 3, 1, 2, 4)
        .reshape(wide_count, head_count, 2, tok_rows)
    )
    got_num = lax.all_to_all(sent_num, "wide", split_axis=0, concat_axis=0, tiled=True)
    got_stats = lax.all_to_all(sent_stats, "wide", split_axis=0, concat_axis=0, tiled=True)
    got_max = got_stats[:, :, 0:1]
    got_den = got_stats[:, :, 1:2]
    top_max = jnp.max(got_max, axis=0)
    factor = jnp.exp(got_max - top_max[None])
    num_own = jnp.sum(got_num.astype(jnp.float32) * factor, axis=0)
    den_own = jnp.sum(got_den * factor, axis=0)
    attention = (
        jnp.transpose((num_own / den_own).astype(jnp.bfloat16), (2, 0, 1))
        .reshape(tok_rows, lane_width)
    )
    out_part = lax.dot_general(
        attention, part_out, (((1,), (1,)), ((), ())), preferred_element_type=jnp.float32
    )
    return lax.psum_scatter(
        out_part.astype(jnp.bfloat16), "narrow", scatter_dimension=1, tiled=True
    )


def solution(mesh):
    in_specs = (
        P("wide", None),
        P(),
        P("wide", None, "narrow"),
        P("wide", "narrow"),
        P("wide", None, None, "narrow"),
        P(),
        P(),
        P(),
    )
    out_specs = P("wide", "narrow")
    return jax.shard_map(body, mesh=mesh, in_specs=in_specs, out_specs=out_specs, check_vma=False)
```

```python
import jax
import jax.numpy as jnp
from jax import lax
from jax.experimental import pallas as pl
from jax.experimental.pallas import tpu as pltpu
from jax.sharding import PartitionSpec as P

HD = 96


negative = -1e30
beyond = 1073741824


def rotate(values, positions):
    half_dim = values.shape[-1] // 2
    frequency = 10000.0 ** (-2.0 * jnp.arange(half_dim, dtype=jnp.float32) / values.shape[-1])
    angles = positions.astype(jnp.float32)[:, None] * frequency[None, :]
    cos_part = jnp.cos(angles)[:, None, :]
    sin_part = jnp.sin(angles)[:, None, :]
    lower_half = values[..., :half_dim]
    upper_half = values[..., half_dim:]
    return jnp.concatenate(
        [
            lower_half * cos_part - upper_half * sin_part,
            upper_half * cos_part + lower_half * sin_part,
        ],
        axis=-1,
    )


def lookup(small_table, key_index):
    matches = key_index[..., None] == jnp.arange(small_table.shape[0], dtype=jnp.int32)
    return jnp.sum(jnp.where(matches, small_table, 0), axis=-1)


def block_step(step, scalars, q_ref, k_ref, v_ref, m_ref, l_ref, o_ref):
    req_ref, base_ref, limit_ref, len_ref, slot_ref = scalars
    req = req_ref[step]
    base = base_ref[step]
    limit = limit_ref[step]
    qlen = len_ref[req]
    per_request = slot_ref.shape[0] // len_ref.shape[0]
    queries = jnp.concatenate(
        [q_ref[:, slot_ref[req * per_request + i]] for i in range(per_request)], axis=1
    )
    keys = k_ref[0]
    vals = v_ref[0]
    blk_len = keys.shape[1]
    q_len = queries.shape[1]
    scale = keys.shape[-1] ** (-0.5)
    scores = (
        jnp.einsum("hkd,hqd->hkq", keys, queries, preferred_element_type=jnp.float32)
        * scale
    )
    key_pos = base + lax.broadcasted_iota(jnp.int32, (blk_len, q_len), 0)
    query_pos = qlen + lax.broadcasted_iota(jnp.int32, (blk_len, q_len), 1)
    allowed = ((key_pos < limit) & (key_pos <= query_pos))[None]
    masked = jnp.where(allowed, scores, negative)
    m_old = m_ref[req]
    m_new = jnp.maximum(m_old, jnp.max(masked, axis=1, keepdims=True))
    exp_terms = jnp.where(allowed, jnp.exp(masked - m_new), 0.0)
    alpha = jnp.exp(m_old - m_new)
    l_ref[req] = alpha * l_ref[req] + jnp.sum(exp_terms, axis=1, keepdims=True)
    weighted = jnp.einsum(
        "hdk,hkq->hdq", vals, exp_terms.astype(jnp.bfloat16),
        preferred_element_type=jnp.float32,
    )
    o_ref[req] = alpha * o_ref[req] + weighted
    m_ref[req] = m_new


def attend_kernel(cache_count):
    def kernel(req_ref, base_ref, limit_ref, len_ref, slot_ref, *refs):
        q_ref, kc_ref, vc_ref, kn_ref, vn_ref, m_ref, l_ref, o_ref = refs
        scalars = (req_ref, base_ref, limit_ref, len_ref, slot_ref)
        step = pl.program_id(0)

        @pl.when(step == 0)
        def _():
            m_ref[...] = jnp.full(m_ref.shape, negative, jnp.float32)
            l_ref[...] = jnp.zeros(l_ref.shape, jnp.float32)
            o_ref[...] = jnp.zeros(o_ref.shape, jnp.float32)

        @pl.when(step < cache_count)
        def _():
            block_step(step, scalars, q_ref, kc_ref, vc_ref, m_ref, l_ref, o_ref)

        @pl.when(step >= cache_count)
        def _():
            block_step(step, scalars, q_ref, kn_ref, vn_ref, m_ref, l_ref, o_ref)

    return kernel


def attend_blocks(
    queries, cache_keys, cache_vals, new_keys, new_vals,
    blk_req, blk_base, blk_limit, lengths, slot_of,
):
    head_count, _, blk_len, head_dim = queries.shape
    req_count = lengths.shape[0]
    q_len = slot_of.shape[0] // req_count * blk_len
    cache_count = cache_keys.shape[0]
    new_count = new_keys.shape[0]
    vmem = pltpu.MemorySpace.VMEM
    whole = pl.BlockSpec(memory_space=vmem)

    def cache_block(j, *_):
        return (jnp.minimum(j, cache_count - 1), 0, 0, 0)

    def new_block(j, *_):
        return (jnp.maximum(j - cache_count, 0), 0, 0, 0)

    key_shape = (1, head_count, blk_len, head_dim)
    val_shape = (1, head_count, head_dim, blk_len)
    in_specs = [
        whole,
        pl.BlockSpec(key_shape, cache_block),
        pl.BlockSpec(val_shape, cache_block),
        pl.BlockSpec(key_shape, new_block),
        pl.BlockSpec(val_shape, new_block),
    ]
    out_shape = (
        jax.ShapeDtypeStruct((req_count, head_count, 1, q_len), jnp.float32),
        jax.ShapeDtypeStruct((req_count, head_count, 1, q_len), jnp.float32),
        jax.ShapeDtypeStruct((req_count, head_count, head_dim, q_len), jnp.float32),
    )
    grid_spec = pltpu.PrefetchScalarGridSpec(
        num_scalar_prefetch=5,
        grid=(cache_count + new_count,),
        in_specs=in_specs,
        out_specs=(whole, whole, whole),
    )
    return pl.pallas_call(
        attend_kernel(cache_count),
        out_shape=out_shape,
        grid_spec=grid_spec,
        compiler_params=pltpu.CompilerParams(dimension_semantics=("arbitrary",)),
    )(blk_req, blk_base, blk_limit, lengths, slot_of,
      queries, cache_keys, cache_vals, new_keys, new_vals)


def body(tokens, gain, w_qkv, w_out, cache, lengths, order, pages):
    wide_count = lax.axis_size("wide")
    wide_index = lax.axis_index("wide")
    tok_rows = tokens.shape[0]
    cache_count = cache.shape[0]
    blk_len = cache.shape[1]
    lane_width = cache.shape[3]
    head_count = lane_width // HD
    slot_count = tok_rows // blk_len
    block_total = order.shape[0]
    req_count = lengths.shape[0]
    per_request = block_total // req_count
    fresh_len = per_request * blk_len
    table_len = pages.shape[0] // req_count
    tok_float = tokens.astype(jnp.float32)
    inv_rms = lax.rsqrt(jnp.mean(tok_float * tok_float, axis=1, keepdims=True) + 1e-05)
    normed = (tok_float * inv_rms * gain.astype(jnp.float32)[None, :]).astype(jnp.bfloat16)

    w_all = lax.all_gather(w_qkv, "wide", axis=0, tiled=True)
    w_q = w_all[:, 0]
    w_kv = w_all[:, 1:]
    cache_ids = wide_index * cache_count + jnp.arange(cache_count, dtype=jnp.int32)
    page_ids = jnp.arange(pages.shape[0], dtype=jnp.int32)
    entries = jnp.sum(jnp.where(pages[None, :] == cache_ids[:, None], page_ids[None, :], 0), axis=1)
    cache_req = entries // table_len
    cache_base = (entries % table_len) * blk_len
    cache_limit = lookup(lengths, cache_req)
    cache_keys = jnp.transpose(
        cache[:, :, 0].reshape(cache_count, blk_len, head_count, HD), (0, 2, 1, 3)
    )
    cache_vals = jnp.transpose(
        cache[:, :, 1].reshape(cache_count, blk_len, head_count, HD), (0, 2, 3, 1)
    )
    w_q, w_kv, cache_keys, cache_vals = lax.optimization_barrier(
        (w_q, w_kv, cache_keys, cache_vals)
    )
    blk_idx = jnp.arange(blk_len, dtype=jnp.int32)
    slot_blocks = lax.dynamic_slice_in_dim(order, wide_index * slot_count, slot_count)
    slot_req = slot_blocks // per_request
    slot_start = lookup(lengths, slot_req) + slot_blocks % per_request * blk_len
    slot_pos = slot_start[:, None] + blk_idx[None, :]
    positions = slot_pos.reshape(tok_rows)
    q_proj = jnp.dot(normed, w_q, preferred_element_type=jnp.float32)
    queries = jnp.transpose(
        rotate(q_proj.reshape(tok_rows, head_count, HD), positions)
        .astype(jnp.bfloat16)
        .reshape(slot_count, blk_len, head_count, HD),
        (2, 0, 1, 3),
    )
    all_queries = lax.all_gather(queries, "wide", axis=1, tiled=True)

    block_ids = jnp.arange(block_total, dtype=jnp.int32)
    slot_of = jnp.sum(
        jnp.where(order[None, :] == block_ids[:, None], block_ids[None, :], 0), axis=1
    )
    q_heads = all_queries

    all_queries, w_out_local = lax.optimization_barrier((all_queries, w_out))
    part_out = lax.all_gather(w_out_local, "wide", axis=0, tiled=True)

    queries, normed_kv, w_kv = lax.optimization_barrier((queries, normed, w_kv))
    kv_proj = jnp.einsum("tk,kcj->tcj", normed_kv, w_kv, preferred_element_type=jnp.float32)
    keys_new = (
        rotate(kv_proj[:, 0].reshape(tok_rows, head_count, HD), positions)
        .astype(jnp.bfloat16)
        .reshape(slot_count, blk_len, head_count, HD)
    )
    vals_new = kv_proj[:, 1].astype(jnp.bfloat16).reshape(slot_count, blk_len, head_count, HD)
    new_limit = jnp.full((slot_count,), beyond, jnp.int32)
    new_keys = jnp.transpose(keys_new, (0, 2, 1, 3))
    new_vals = jnp.transpose(vals_new, (0, 2, 3, 1))
    q_heads, new_keys, new_vals = lax.optimization_barrier((q_heads, new_keys, new_vals))
    head_max, head_den, head_num = attend_blocks(
        q_heads,
        cache_keys,
        cache_vals,
        new_keys,
        new_vals,
        jnp.concatenate([cache_req, slot_req]),
        jnp.concatenate([cache_base, slot_start]),
        jnp.concatenate([cache_limit, new_limit]),
        lengths,
        slot_of,
    )

    split = fresh_len // tok_rows
    sent_num = (
        head_num.reshape(req_count, head_count, HD, split, tok_rows)
        .transpose(0, 3, 1, 2, 4)
        .reshape(wide_count, head_count, HD, tok_rows)
        .astype(jnp.bfloat16)
    )
    stats = jnp.concatenate([head_max, head_den], axis=2)
    sent_stats = (
        stats.reshape(req_count, head_count, 2, split, tok_rows)
        .transpose(0, 3, 1, 2, 4)
        .reshape(wide_count, head_count, 2, tok_rows)
    )
    got_num = lax.all_to_all(sent_num, "wide", split_axis=0, concat_axis=0, tiled=True)
    got_stats = lax.all_to_all(sent_stats, "wide", split_axis=0, concat_axis=0, tiled=True)
    got_max = got_stats[:, :, 0:1]
    got_den = got_stats[:, :, 1:2]
    top_max = jnp.max(got_max, axis=0)
    factor = jnp.exp(got_max - top_max[None])
    num_own = jnp.sum(got_num.astype(jnp.float32) * factor, axis=0)
    den_own = jnp.sum(got_den * factor, axis=0)
    attention = (
        jnp.transpose((num_own / den_own).astype(jnp.bfloat16), (2, 0, 1))
        .reshape(tok_rows, lane_width)
    )
    out_part = lax.dot_general(
        attention, part_out, (((1,), (1,)), ((), ())), preferred_element_type=jnp.float32
    )
    return lax.psum_scatter(
        out_part.astype(jnp.bfloat16), "narrow", scatter_dimension=1, tiled=True
    )


def solution(mesh):
    in_specs = (
        P("wide", None),
        P(),
        P("wide", None, "narrow"),
        P("wide", "narrow"),
        P("wide", None, None, "narrow"),
        P(),
        P(),
        P(),
    )
    out_specs = P("wide", "narrow")
    return jax.shard_map(body, mesh=mesh, in_specs=in_specs, out_specs=out_specs, check_vma=False)
```

```python
import jax
import jax.numpy as jnp
from jax import lax
from jax.experimental import pallas as pl
from jax.experimental.pallas import tpu as pltpu
from jax.sharding import PartitionSpec as P

HD = 96


negative = -1e30
beyond = 1073741824


def rotate(values, positions):
    half_dim = values.shape[-1] // 2
    frequency = 10000.0 ** (-2.0 * jnp.arange(half_dim, dtype=jnp.float32) / values.shape[-1])
    angles = positions.astype(jnp.float32)[:, None] * frequency[None, :]
    cos_part = jnp.cos(angles)[:, None, :]
    sin_part = jnp.sin(angles)[:, None, :]
    lower_half = values[..., :half_dim]
    upper_half = values[..., half_dim:]
    return jnp.concatenate(
        [
            lower_half * cos_part - upper_half * sin_part,
            upper_half * cos_part + lower_half * sin_part,
        ],
        axis=-1,
    )


def lookup(small_table, key_index):
    matches = key_index[..., None] == jnp.arange(small_table.shape[0], dtype=jnp.int32)
    return jnp.sum(jnp.where(matches, small_table, 0), axis=-1)


def attend_kernel(carry_in):
    def kernel(req_ref, base_ref, limit_ref, len_ref, slot_ref, *refs):
        if carry_in:
            q_ref, k_ref, v_ref, m0_ref, l0_ref, o0_ref, m_ref, l_ref, o_ref = refs
        else:
            q_ref, k_ref, v_ref, m_ref, l_ref, o_ref = refs
        step = pl.program_id(0)

        @pl.when(step == 0)
        def _():
            if carry_in:
                m_ref[...] = m0_ref[...]
                l_ref[...] = l0_ref[...]
                o_ref[...] = o0_ref[...]
            else:
                m_ref[...] = jnp.full(m_ref.shape, negative, jnp.float32)
                l_ref[...] = jnp.zeros(l_ref.shape, jnp.float32)
                o_ref[...] = jnp.zeros(o_ref.shape, jnp.float32)

        req = req_ref[step]
        base = base_ref[step]
        limit = limit_ref[step]
        qlen = len_ref[req]
        per_request = slot_ref.shape[0] // len_ref.shape[0]
        queries = jnp.concatenate(
            [q_ref[:, slot_ref[req * per_request + i]] for i in range(per_request)], axis=1
        )
        keys = k_ref[0]
        vals = v_ref[0]
        blk_len = keys.shape[1]
        q_len = queries.shape[1]
        scale = keys.shape[-1] ** (-0.5)
        scores = (
            jnp.einsum("hkd,hqd->hkq", keys, queries, preferred_element_type=jnp.float32)
            * scale
        )
        key_pos = base + lax.broadcasted_iota(jnp.int32, (blk_len, q_len), 0)
        query_pos = qlen + lax.broadcasted_iota(jnp.int32, (blk_len, q_len), 1)
        allowed = ((key_pos < limit) & (key_pos <= query_pos))[None]
        masked = jnp.where(allowed, scores, negative)
        m_old = m_ref[req]
        m_new = jnp.maximum(m_old, jnp.max(masked, axis=1, keepdims=True))
        exp_terms = jnp.where(allowed, jnp.exp(masked - m_new), 0.0)
        alpha = jnp.exp(m_old - m_new)
        l_ref[req] = alpha * l_ref[req] + jnp.sum(exp_terms, axis=1, keepdims=True)
        weighted = jnp.einsum(
            "hdk,hkq->hdq", vals, exp_terms.astype(jnp.bfloat16),
            preferred_element_type=jnp.float32,
        )
        o_ref[req] = alpha * o_ref[req] + weighted
        m_ref[req] = m_new

    return kernel


def attend_blocks(
    queries, keys, vals_t, blk_req, blk_base, blk_limit, lengths, slot_of, carry=None
):
    head_count, _, blk_len, head_dim = queries.shape
    req_count = lengths.shape[0]
    q_len = slot_of.shape[0] // req_count * blk_len
    blk_count = keys.shape[0]
    vmem = pltpu.MemorySpace.VMEM
    whole = pl.BlockSpec(memory_space=vmem)
    in_specs = [
        whole,
        pl.BlockSpec((1, head_count, blk_len, head_dim), lambda j, *_: (j, 0, 0, 0)),
        pl.BlockSpec((1, head_count, head_dim, blk_len), lambda j, *_: (j, 0, 0, 0)),
    ]
    args = [queries, keys, vals_t]
    if carry is not None:
        in_specs += [whole, whole, whole]
        args += list(carry)
    out_shape = (
        jax.ShapeDtypeStruct((req_count, head_count, 1, q_len), jnp.float32),
        jax.ShapeDtypeStruct((req_count, head_count, 1, q_len), jnp.float32),
        jax.ShapeDtypeStruct((req_count, head_count, head_dim, q_len), jnp.float32),
    )
    grid_spec = pltpu.PrefetchScalarGridSpec(
        num_scalar_prefetch=5,
        grid=(blk_count,),
        in_specs=in_specs,
        out_specs=(whole, whole, whole),
    )
    return pl.pallas_call(
        attend_kernel(carry is not None),
        out_shape=out_shape,
        grid_spec=grid_spec,
        compiler_params=pltpu.CompilerParams(
            dimension_semantics=("arbitrary",)
        ),
    )(blk_req, blk_base, blk_limit, lengths, slot_of, *args)


def body(tokens, gain, w_qkv, w_out, cache, lengths, order, pages):
    wide_count = lax.axis_size("wide")
    wide_index = lax.axis_index("wide")
    tok_rows = tokens.shape[0]
    cache_count = cache.shape[0]
    blk_len = cache.shape[1]
    lane_width = cache.shape[3]
    head_count = lane_width // HD
    slot_count = tok_rows // blk_len
    block_total = order.shape[0]
    req_count = lengths.shape[0]
    per_request = block_total // req_count
    fresh_len = per_request * blk_len
    table_len = pages.shape[0] // req_count
    tok_float = tokens.astype(jnp.float32)
    inv_rms = lax.rsqrt(jnp.mean(tok_float * tok_float, axis=1, keepdims=True) + 1e-05)
    normed = (tok_float * inv_rms * gain.astype(jnp.float32)[None, :]).astype(jnp.bfloat16)

    w_q = lax.all_gather(w_qkv[:, 0], "wide", axis=0, tiled=True)
    cache_ids = wide_index * cache_count + jnp.arange(cache_count, dtype=jnp.int32)
    page_ids = jnp.arange(pages.shape[0], dtype=jnp.int32)
    entries = jnp.sum(jnp.where(pages[None, :] == cache_ids[:, None], page_ids[None, :], 0), axis=1)
    cache_req = entries // table_len
    cache_base = (entries % table_len) * blk_len
    cache_limit = lookup(lengths, cache_req)
    cache_keys = jnp.transpose(
        cache[:, :, 0].reshape(cache_count, blk_len, head_count, HD), (0, 2, 1, 3)
    )
    w_q, cache_keys = lax.optimization_barrier((w_q, cache_keys))
    blk_idx = jnp.arange(blk_len, dtype=jnp.int32)
    slot_blocks = lax.dynamic_slice_in_dim(order, wide_index * slot_count, slot_count)
    slot_req = slot_blocks // per_request
    slot_start = lookup(lengths, slot_req) + slot_blocks % per_request * blk_len
    slot_pos = slot_start[:, None] + blk_idx[None, :]
    positions = slot_pos.reshape(tok_rows)
    q_proj = jnp.dot(normed, w_q, preferred_element_type=jnp.float32)
    queries = jnp.transpose(
        rotate(q_proj.reshape(tok_rows, head_count, HD), positions)
        .astype(jnp.bfloat16)
        .reshape(slot_count, blk_len, head_count, HD),
        (2, 0, 1, 3),
    )
    received = [queries] + [
        lax.ppermute(
            queries, "wide", [(src, (src + shift) % wide_count) for src in range(wide_count)]
        )
        for shift in range(1, wide_count)
    ]
    all_queries = jnp.concatenate(received, axis=1)
    queries, cache_v = lax.optimization_barrier((queries, cache))
    cache_vals = jnp.transpose(
        cache_v[:, :, 1].reshape(cache_count, blk_len, head_count, HD), (0, 2, 3, 1)
    )
    all_queries, cache_vals, w_kv_local = lax.optimization_barrier(
        (all_queries, cache_vals, w_qkv[:, 1:])
    )
    w_kv = lax.all_gather(w_kv_local, "wide", axis=0, tiled=True)

    block_ids = jnp.arange(block_total, dtype=jnp.int32)
    slot_of = jnp.sum(
        jnp.where(order[None, :] == block_ids[:, None], block_ids[None, :], 0), axis=1
    )
    slot_src = slot_of // slot_count
    slot_of = (wide_index - slot_src) % wide_count * slot_count + slot_of % slot_count
    q_heads = all_queries

    carry = attend_blocks(
        q_heads, cache_keys, cache_vals, cache_req, cache_base, cache_limit, lengths, slot_of
    )
    carry, w_out_local = lax.optimization_barrier((carry, w_out))
    part_out = lax.all_gather(w_out_local, "wide", axis=0, tiled=True)

    kv_proj = jnp.einsum("tk,kcj->tcj", normed, w_kv, preferred_element_type=jnp.float32)
    keys_new = (
        rotate(kv_proj[:, 0].reshape(tok_rows, head_count, HD), positions)
        .astype(jnp.bfloat16)
        .reshape(slot_count, blk_len, head_count, HD)
    )
    vals_new = kv_proj[:, 1].astype(jnp.bfloat16).reshape(slot_count, blk_len, head_count, HD)
    new_limit = jnp.full((slot_count,), beyond, jnp.int32)
    head_max, head_den, head_num = attend_blocks(
        q_heads,
        jnp.transpose(keys_new, (0, 2, 1, 3)),
        jnp.transpose(vals_new, (0, 2, 3, 1)),
        slot_req,
        slot_start,
        new_limit,
        lengths,
        slot_of,
        carry=carry,
    )

    split = fresh_len // tok_rows
    sent_num = (
        head_num.reshape(req_count, head_count, HD, split, tok_rows)
        .transpose(0, 3, 1, 2, 4)
        .reshape(wide_count, head_count, HD, tok_rows)
        .astype(jnp.bfloat16)
    )
    stats = jnp.concatenate([head_max, head_den], axis=2)
    sent_stats = (
        stats.reshape(req_count, head_count, 2, split, tok_rows)
        .transpose(0, 3, 1, 2, 4)
        .reshape(wide_count, head_count, 2, tok_rows)
    )
    got_num = lax.all_to_all(sent_num, "wide", split_axis=0, concat_axis=0, tiled=True)
    got_stats = lax.all_to_all(sent_stats, "wide", split_axis=0, concat_axis=0, tiled=True)
    got_max = got_stats[:, :, 0:1]
    got_den = got_stats[:, :, 1:2]
    top_max = jnp.max(got_max, axis=0)
    factor = jnp.exp(got_max - top_max[None])
    num_own = jnp.sum(got_num.astype(jnp.float32) * factor, axis=0)
    den_own = jnp.sum(got_den * factor, axis=0)
    attention = (
        jnp.transpose((num_own / den_own).astype(jnp.bfloat16), (2, 0, 1))
        .reshape(tok_rows, lane_width)
    )
    out_part = lax.dot_general(
        attention, part_out, (((1,), (1,)), ((), ())), preferred_element_type=jnp.float32
    )
    return lax.psum_scatter(
        out_part.astype(jnp.bfloat16), "narrow", scatter_dimension=1, tiled=True
    )


def solution(mesh):
    in_specs = (
        P("wide", None),
        P(),
        P("wide", None, "narrow"),
        P("wide", "narrow"),
        P("wide", None, None, "narrow"),
        P(),
        P(),
        P(),
    )
    out_specs = P("wide", "narrow")
    return jax.shard_map(body, mesh=mesh, in_specs=in_specs, out_specs=out_specs, check_vma=False)
```

```python
import jax
import jax.numpy as jnp
from jax import lax
from jax.experimental import pallas as pl
from jax.experimental.pallas import tpu as pltpu
from jax.sharding import PartitionSpec as P

HD = 96


negative = -1e30
beyond = 1073741824


def rotate(values, positions):
    half_dim = values.shape[-1] // 2
    frequency = 10000.0 ** (-2.0 * jnp.arange(half_dim, dtype=jnp.float32) / values.shape[-1])
    angles = positions.astype(jnp.float32)[:, None] * frequency[None, :]
    cos_part = jnp.cos(angles)[:, None, :]
    sin_part = jnp.sin(angles)[:, None, :]
    lower_half = values[..., :half_dim]
    upper_half = values[..., half_dim:]
    return jnp.concatenate(
        [
            lower_half * cos_part - upper_half * sin_part,
            upper_half * cos_part + lower_half * sin_part,
        ],
        axis=-1,
    )


def lookup(small_table, key_index):
    matches = key_index[..., None] == jnp.arange(small_table.shape[0], dtype=jnp.int32)
    return jnp.sum(jnp.where(matches, small_table, 0), axis=-1)


def attend_kernel(carry_in, out_rows):
    def kernel(req_ref, base_ref, limit_ref, len_ref, slot_ref, *refs):
        if carry_in:
            (q_ref, k_ref, v_ref, m0_ref, l0_ref, o0_ref,
             num_ref, stats_ref, m_ref, l_ref, o_ref) = refs
        else:
            q_ref, k_ref, v_ref, m_ref, l_ref, o_ref = refs
        step = pl.program_id(0)

        @pl.when(step == 0)
        def _():
            if carry_in:
                m_ref[...] = m0_ref[...]
                l_ref[...] = l0_ref[...]
                o_ref[...] = o0_ref[...]
            else:
                m_ref[...] = jnp.full(m_ref.shape, negative, jnp.float32)
                l_ref[...] = jnp.zeros(l_ref.shape, jnp.float32)
                o_ref[...] = jnp.zeros(o_ref.shape, jnp.float32)

        req = req_ref[step]
        base = base_ref[step]
        limit = limit_ref[step]
        qlen = len_ref[req]
        per_request = slot_ref.shape[0] // len_ref.shape[0]
        queries = jnp.concatenate(
            [q_ref[:, slot_ref[req * per_request + i]] for i in range(per_request)], axis=1
        )
        keys = k_ref[0]
        vals = v_ref[0]
        blk_len = keys.shape[1]
        q_len = queries.shape[1]
        scale = keys.shape[-1] ** (-0.5)
        scores = (
            jnp.einsum("hkd,hqd->hkq", keys, queries, preferred_element_type=jnp.float32)
            * scale
        )
        key_pos = base + lax.broadcasted_iota(jnp.int32, (blk_len, q_len), 0)
        query_pos = qlen + lax.broadcasted_iota(jnp.int32, (blk_len, q_len), 1)
        allowed = ((key_pos < limit) & (key_pos <= query_pos))[None]
        masked = jnp.where(allowed, scores, negative)
        m_old = m_ref[req]
        m_new = jnp.maximum(m_old, jnp.max(masked, axis=1, keepdims=True))
        shift = jnp.where(m_new == negative, 0.0, m_new)
        exp_terms = jnp.exp(masked - shift)
        alpha = jnp.exp(m_old - m_new)
        l_ref[req] = alpha * l_ref[req] + jnp.sum(exp_terms, axis=1, keepdims=True)
        weighted = jnp.einsum(
            "hdk,hkq->hdq", vals, exp_terms.astype(jnp.bfloat16),
            preferred_element_type=jnp.float32,
        )
        o_ref[req] = alpha * o_ref[req] + weighted
        m_ref[req] = m_new

        if carry_in:
            @pl.when(step == pl.num_programs(0) - 1)
            def _():
                split = q_len // out_rows
                for r in range(len_ref.shape[0]):
                    for c in range(split):
                        cols = pl.ds(c * out_rows, out_rows)
                        num_ref[r * split + c] = o_ref[r, :, :, cols].astype(jnp.bfloat16)
                        stats_ref[r * split + c, :, 0:1] = m_ref[r, :, :, cols]
                        stats_ref[r * split + c, :, 1:2] = l_ref[r, :, :, cols]

    return kernel


def attend_blocks(
    queries, keys, vals_t, blk_req, blk_base, blk_limit, lengths, slot_of,
    carry=None, out_rows=None,
):
    head_count, _, blk_len, head_dim = queries.shape
    req_count = lengths.shape[0]
    q_len = slot_of.shape[0] // req_count * blk_len
    blk_count = keys.shape[0]
    vmem = pltpu.MemorySpace.VMEM
    whole = pl.BlockSpec(memory_space=vmem)
    in_specs = [
        whole,
        pl.BlockSpec((1, head_count, blk_len, head_dim), lambda j, *_: (j, 0, 0, 0)),
        pl.BlockSpec((1, head_count, head_dim, blk_len), lambda j, *_: (j, 0, 0, 0)),
    ]
    args = [queries, keys, vals_t]
    acc_shapes = (
        ((req_count, head_count, 1, q_len), jnp.float32),
        ((req_count, head_count, 1, q_len), jnp.float32),
        ((req_count, head_count, head_dim, q_len), jnp.float32),
    )
    if carry is None:
        out_shape = tuple(jax.ShapeDtypeStruct(*a) for a in acc_shapes)
        out_specs = (whole, whole, whole)
        scratch = ()
    else:
        in_specs += [whole, whole, whole]
        args += list(carry)
        groups = req_count * q_len // out_rows
        out_shape = (
            jax.ShapeDtypeStruct((groups, head_count, head_dim, out_rows), jnp.bfloat16),
            jax.ShapeDtypeStruct((groups, head_count, 2, out_rows), jnp.float32),
        )
        out_specs = (whole, whole)
        scratch = tuple(pltpu.VMEM(*a) for a in acc_shapes)
    grid_spec = pltpu.PrefetchScalarGridSpec(
        num_scalar_prefetch=5,
        grid=(blk_count,),
        in_specs=in_specs,
        out_specs=out_specs,
        scratch_shapes=scratch,
    )
    return pl.pallas_call(
        attend_kernel(carry is not None, out_rows),
        out_shape=out_shape,
        grid_spec=grid_spec,
        compiler_params=pltpu.CompilerParams(dimension_semantics=("arbitrary",)),
    )(blk_req, blk_base, blk_limit, lengths, slot_of, *args)


def body(tokens, gain, w_qkv, w_out, cache, lengths, order, pages):
    wide_count = lax.axis_size("wide")
    wide_index = lax.axis_index("wide")
    tok_rows = tokens.shape[0]
    cache_count = cache.shape[0]
    blk_len = cache.shape[1]
    lane_width = cache.shape[3]
    head_count = lane_width // HD
    slot_count = tok_rows // blk_len
    block_total = order.shape[0]
    req_count = lengths.shape[0]
    per_request = block_total // req_count
    fresh_len = per_request * blk_len
    table_len = pages.shape[0] // req_count
    tok_float = tokens.astype(jnp.float32)
    inv_rms = lax.rsqrt(jnp.mean(tok_float * tok_float, axis=1, keepdims=True) + 1e-05)
    normed = (tok_float * inv_rms * gain.astype(jnp.float32)[None, :]).astype(jnp.bfloat16)

    w_q = lax.all_gather(w_qkv[:, 0], "wide", axis=0, tiled=True)
    cache_ids = wide_index * cache_count + jnp.arange(cache_count, dtype=jnp.int32)
    page_ids = jnp.arange(pages.shape[0], dtype=jnp.int32)
    entries = jnp.sum(jnp.where(pages[None, :] == cache_ids[:, None], page_ids[None, :], 0), axis=1)
    cache_req = entries // table_len
    cache_base = (entries % table_len) * blk_len
    cache_limit = lookup(lengths, cache_req)
    cache_keys = jnp.transpose(
        cache[:, :, 0].reshape(cache_count, blk_len, head_count, HD), (0, 2, 1, 3)
    )
    w_q, cache_keys = lax.optimization_barrier((w_q, cache_keys))
    blk_idx = jnp.arange(blk_len, dtype=jnp.int32)
    slot_blocks = lax.dynamic_slice_in_dim(order, wide_index * slot_count, slot_count)
    slot_req = slot_blocks // per_request
    slot_start = lookup(lengths, slot_req) + slot_blocks % per_request * blk_len
    slot_pos = slot_start[:, None] + blk_idx[None, :]
    positions = slot_pos.reshape(tok_rows)
    q_proj = jnp.dot(normed, w_q, preferred_element_type=jnp.float32)
    queries = jnp.transpose(
        rotate(q_proj.reshape(tok_rows, head_count, HD), positions)
        .astype(jnp.bfloat16)
        .reshape(slot_count, blk_len, head_count, HD),
        (2, 0, 1, 3),
    )
    all_queries = lax.all_gather(queries, "wide", axis=1, tiled=True)
    queries, cache_v = lax.optimization_barrier((queries, cache))
    cache_vals = jnp.transpose(
        cache_v[:, :, 1].reshape(cache_count, blk_len, head_count, HD), (0, 2, 3, 1)
    )
    all_queries, cache_vals, w_kv_local = lax.optimization_barrier(
        (all_queries, cache_vals, w_qkv[:, 1:])
    )
    w_kv = lax.all_gather(w_kv_local, "wide", axis=0, tiled=True)

    block_ids = jnp.arange(block_total, dtype=jnp.int32)
    slot_of = jnp.sum(
        jnp.where(order[None, :] == block_ids[:, None], block_ids[None, :], 0), axis=1
    )
    q_heads = all_queries

    carry = attend_blocks(
        q_heads, cache_keys, cache_vals, cache_req, cache_base, cache_limit, lengths, slot_of
    )
    carry, w_out_local = lax.optimization_barrier((carry, w_out))
    part_out = lax.all_gather(w_out_local, "wide", axis=0, tiled=True)

    kv_proj = jnp.einsum("tk,kcj->tcj", normed, w_kv, preferred_element_type=jnp.float32)
    keys_new = (
        rotate(kv_proj[:, 0].reshape(tok_rows, head_count, HD), positions)
        .astype(jnp.bfloat16)
        .reshape(slot_count, blk_len, head_count, HD)
    )
    vals_new = kv_proj[:, 1].astype(jnp.bfloat16).reshape(slot_count, blk_len, head_count, HD)
    new_limit = jnp.full((slot_count,), beyond, jnp.int32)
    sent_num, sent_stats = attend_blocks(
        q_heads,
        jnp.transpose(keys_new, (0, 2, 1, 3)),
        jnp.transpose(vals_new, (0, 2, 3, 1)),
        slot_req,
        slot_start,
        new_limit,
        lengths,
        slot_of,
        carry=carry,
        out_rows=tok_rows,
    )

    got_num = lax.all_to_all(sent_num, "wide", split_axis=0, concat_axis=0, tiled=True)
    got_stats = lax.all_to_all(sent_stats, "wide", split_axis=0, concat_axis=0, tiled=True)
    got_max = got_stats[:, :, 0:1]
    got_den = got_stats[:, :, 1:2]
    top_max = jnp.max(got_max, axis=0)
    factor = jnp.exp(got_max - top_max[None])
    num_own = jnp.sum(got_num.astype(jnp.float32) * factor, axis=0)
    den_own = jnp.sum(got_den * factor, axis=0)
    attention = (
        jnp.transpose((num_own / den_own).astype(jnp.bfloat16), (2, 0, 1))
        .reshape(tok_rows, lane_width)
    )
    out_part = lax.dot_general(
        attention, part_out, (((1,), (1,)), ((), ())), preferred_element_type=jnp.float32
    )
    return lax.psum_scatter(
        out_part.astype(jnp.bfloat16), "narrow", scatter_dimension=1, tiled=True
    )


def solution(mesh):
    in_specs = (
        P("wide", None),
        P(),
        P("wide", None, "narrow"),
        P("wide", "narrow"),
        P("wide", None, None, "narrow"),
        P(),
        P(),
        P(),
    )
    out_specs = P("wide", "narrow")
    return jax.shard_map(body, mesh=mesh, in_specs=in_specs, out_specs=out_specs, check_vma=False)
```

```python
import jax
import jax.numpy as jnp
from jax import lax
from jax.experimental import pallas as pl
from jax.experimental.pallas import tpu as pltpu
from jax.sharding import PartitionSpec as P

HD = 96


negative = -1e30
beyond = 1073741824


def rotate(values, positions):
    half_dim = values.shape[-1] // 2
    frequency = 10000.0 ** (-2.0 * jnp.arange(half_dim, dtype=jnp.float32) / values.shape[-1])
    angles = positions.astype(jnp.float32)[:, None] * frequency[None, :]
    cos_part = jnp.cos(angles)[:, None, :]
    sin_part = jnp.sin(angles)[:, None, :]
    lower_half = values[..., :half_dim]
    upper_half = values[..., half_dim:]
    return jnp.concatenate(
        [
            lower_half * cos_part - upper_half * sin_part,
            upper_half * cos_part + lower_half * sin_part,
        ],
        axis=-1,
    )


def lookup(small_table, key_index):
    matches = key_index[..., None] == jnp.arange(small_table.shape[0], dtype=jnp.int32)
    return jnp.sum(jnp.where(matches, small_table, 0), axis=-1)


def attend_kernel(carry_in, out_rows):
    def kernel(req_ref, base_ref, limit_ref, len_ref, slot_ref, *refs):
        if carry_in:
            (q_ref, k_ref, v_ref, m0_ref, l0_ref, o0_ref,
             num_ref, stats_ref, m_ref, l_ref, o_ref) = refs
        else:
            q_ref, k_ref, v_ref, m_ref, l_ref, o_ref = refs
        step = pl.program_id(0)

        @pl.when(step == 0)
        def _():
            if carry_in:
                m_ref[...] = m0_ref[...]
                l_ref[...] = l0_ref[...]
                o_ref[...] = o0_ref[...]
            else:
                m_ref[...] = jnp.full(m_ref.shape, negative, jnp.float32)
                l_ref[...] = jnp.zeros(l_ref.shape, jnp.float32)
                o_ref[...] = jnp.zeros(o_ref.shape, jnp.float32)

        req = req_ref[step]
        base = base_ref[step]
        limit = limit_ref[step]
        qlen = len_ref[req]
        per_request = slot_ref.shape[0] // len_ref.shape[0]
        queries = jnp.concatenate(
            [q_ref[:, slot_ref[req * per_request + i]] for i in range(per_request)], axis=1
        )
        keys = k_ref[0]
        vals = v_ref[0]
        blk_len = keys.shape[1]
        q_len = queries.shape[1]
        scale = keys.shape[-1] ** (-0.5)
        scores = (
            jnp.einsum("hkd,hqd->hkq", keys, queries, preferred_element_type=jnp.float32)
            * scale
        )
        key_pos = base + lax.broadcasted_iota(jnp.int32, (blk_len, q_len), 0)
        query_pos = qlen + lax.broadcasted_iota(jnp.int32, (blk_len, q_len), 1)
        allowed = ((key_pos < limit) & (key_pos <= query_pos))[None]
        masked = jnp.where(allowed, scores, negative)
        m_old = m_ref[req]
        m_new = jnp.maximum(m_old, jnp.max(masked, axis=1, keepdims=True))
        shift = jnp.where(m_new == negative, 0.0, m_new)
        exp_terms = jnp.exp(masked - shift)
        alpha = jnp.exp(m_old - m_new)
        l_ref[req] = alpha * l_ref[req] + jnp.sum(exp_terms, axis=1, keepdims=True)
        weighted = jnp.einsum(
            "hdk,hkq->hdq", vals, exp_terms.astype(jnp.bfloat16),
            preferred_element_type=jnp.float32,
        )
        o_ref[req] = alpha * o_ref[req] + weighted
        m_ref[req] = m_new

        if carry_in:
            @pl.when(step == pl.num_programs(0) - 1)
            def _():
                split = q_len // out_rows
                for r in range(len_ref.shape[0]):
                    for c in range(split):
                        cols = pl.ds(c * out_rows, out_rows)
                        num_ref[r * split + c] = o_ref[r, :, :, cols].astype(jnp.bfloat16)
                        stats_ref[r * split + c, :, 0:1] = m_ref[r, :, :, cols]
                        stats_ref[r * split + c, :, 1:2] = l_ref[r, :, :, cols]

    return kernel


def attend_blocks(
    queries, keys, vals_t, blk_req, blk_base, blk_limit, lengths, slot_of,
    carry=None, out_rows=None,
):
    head_count, _, blk_len, head_dim = queries.shape
    req_count = lengths.shape[0]
    q_len = slot_of.shape[0] // req_count * blk_len
    blk_count = keys.shape[0]
    vmem = pltpu.MemorySpace.VMEM
    whole = pl.BlockSpec(memory_space=vmem)
    in_specs = [
        whole,
        pl.BlockSpec((1, head_count, blk_len, head_dim), lambda j, *_: (j, 0, 0, 0)),
        pl.BlockSpec((1, head_count, head_dim, blk_len), lambda j, *_: (j, 0, 0, 0)),
    ]
    args = [queries, keys, vals_t]
    acc_shapes = (
        ((req_count, head_count, 1, q_len), jnp.float32),
        ((req_count, head_count, 1, q_len), jnp.float32),
        ((req_count, head_count, head_dim, q_len), jnp.float32),
    )
    if carry is None:
        out_shape = tuple(jax.ShapeDtypeStruct(*a) for a in acc_shapes)
        out_specs = (whole, whole, whole)
        scratch = ()
    else:
        in_specs += [whole, whole, whole]
        args += list(carry)
        groups = req_count * q_len // out_rows
        out_shape = (
            jax.ShapeDtypeStruct((groups, head_count, head_dim, out_rows), jnp.bfloat16),
            jax.ShapeDtypeStruct((groups, head_count, 2, out_rows), jnp.float32),
        )
        out_specs = (whole, whole)
        scratch = tuple(pltpu.VMEM(*a) for a in acc_shapes)
    grid_spec = pltpu.PrefetchScalarGridSpec(
        num_scalar_prefetch=5,
        grid=(blk_count,),
        in_specs=in_specs,
        out_specs=out_specs,
        scratch_shapes=scratch,
    )
    return pl.pallas_call(
        attend_kernel(carry is not None, out_rows),
        out_shape=out_shape,
        grid_spec=grid_spec,
        compiler_params=pltpu.CompilerParams(dimension_semantics=("arbitrary",)),
    )(blk_req, blk_base, blk_limit, lengths, slot_of, *args)


def body(tokens, gain, w_qkv, w_out, cache, lengths, order, pages):
    wide_count = lax.axis_size("wide")
    wide_index = lax.axis_index("wide")
    tok_rows = tokens.shape[0]
    cache_count = cache.shape[0]
    blk_len = cache.shape[1]
    lane_width = cache.shape[3]
    head_count = lane_width // HD
    slot_count = tok_rows // blk_len
    block_total = order.shape[0]
    req_count = lengths.shape[0]
    per_request = block_total // req_count
    fresh_len = per_request * blk_len
    table_len = pages.shape[0] // req_count
    tok_float = tokens.astype(jnp.float32)
    inv_rms = lax.rsqrt(jnp.mean(tok_float * tok_float, axis=1, keepdims=True) + 1e-05)
    normed = (tok_float * inv_rms * gain.astype(jnp.float32)[None, :]).astype(jnp.bfloat16)

    w_q = lax.all_gather(w_qkv[:, 0], "wide", axis=0, tiled=True)
    cache_ids = wide_index * cache_count + jnp.arange(cache_count, dtype=jnp.int32)
    page_ids = jnp.arange(pages.shape[0], dtype=jnp.int32)
    entries = jnp.sum(jnp.where(pages[None, :] == cache_ids[:, None], page_ids[None, :], 0), axis=1)
    cache_req = entries // table_len
    cache_base = (entries % table_len) * blk_len
    cache_limit = lookup(lengths, cache_req)
    cache_keys = jnp.transpose(
        cache[:, :, 0].reshape(cache_count, blk_len, head_count, HD), (0, 2, 1, 3)
    )
    w_q, cache_keys = lax.optimization_barrier((w_q, cache_keys))
    blk_idx = jnp.arange(blk_len, dtype=jnp.int32)
    slot_blocks = lax.dynamic_slice_in_dim(order, wide_index * slot_count, slot_count)
    slot_req = slot_blocks // per_request
    slot_start = lookup(lengths, slot_req) + slot_blocks % per_request * blk_len
    slot_pos = slot_start[:, None] + blk_idx[None, :]
    positions = slot_pos.reshape(tok_rows)
    q_proj = jnp.dot(normed, w_q, preferred_element_type=jnp.float32)
    queries = jnp.transpose(
        rotate(q_proj.reshape(tok_rows, head_count, HD), positions)
        .astype(jnp.bfloat16)
        .reshape(slot_count, blk_len, head_count, HD),
        (2, 0, 1, 3),
    )
    all_queries = lax.all_gather(queries, "wide", axis=1, tiled=True)
    queries, cache_v = lax.optimization_barrier((queries, cache))
    cache_vals = jnp.transpose(
        cache_v[:, :, 1].reshape(cache_count, blk_len, head_count, HD), (0, 2, 3, 1)
    )
    all_queries, cache_vals, w_kv_local = lax.optimization_barrier(
        (all_queries, cache_vals, w_qkv[:, 1:])
    )
    w_kv = lax.all_gather(w_kv_local, "wide", axis=0, tiled=True)

    block_ids = jnp.arange(block_total, dtype=jnp.int32)
    slot_of = jnp.sum(
        jnp.where(order[None, :] == block_ids[:, None], block_ids[None, :], 0), axis=1
    )
    q_heads = all_queries

    carry = attend_blocks(
        q_heads, cache_keys, cache_vals, cache_req, cache_base, cache_limit, lengths, slot_of
    )
    carry, w_out_local = lax.optimization_barrier((carry, w_out))
    part_out = lax.all_gather(w_out_local, "wide", axis=0, tiled=True)

    kv_proj = jnp.einsum("tk,kcj->tcj", normed, w_kv, preferred_element_type=jnp.float32)
    keys_new = (
        rotate(kv_proj[:, 0].reshape(tok_rows, head_count, HD), positions)
        .astype(jnp.bfloat16)
        .reshape(slot_count, blk_len, head_count, HD)
    )
    vals_new = kv_proj[:, 1].astype(jnp.bfloat16).reshape(slot_count, blk_len, head_count, HD)
    new_limit = jnp.full((slot_count,), beyond, jnp.int32)
    sent_num, sent_stats = attend_blocks(
        q_heads,
        jnp.transpose(keys_new, (0, 2, 1, 3)),
        jnp.transpose(vals_new, (0, 2, 3, 1)),
        slot_req,
        slot_start,
        new_limit,
        lengths,
        slot_of,
        carry=carry,
        out_rows=tok_rows,
    )

    parts = []
    rest = sent_stats
    for _ in range(3):
        part = rest.astype(jnp.bfloat16)
        parts.append(part)
        rest = rest - part.astype(jnp.float32)
    pad_rows = (-(HD + 6)) % 8
    packed = jnp.concatenate(
        [sent_num] + parts
        + [jnp.zeros(sent_num.shape[:2] + (pad_rows,) + sent_num.shape[3:], jnp.bfloat16)],
        axis=2,
    )
    got = lax.all_to_all(packed, "wide", split_axis=0, concat_axis=0, tiled=True)
    got_num = got[:, :, :HD]
    got_stats = (
        got[:, :, HD:HD + 2].astype(jnp.float32)
        + got[:, :, HD + 2:HD + 4].astype(jnp.float32)
        + got[:, :, HD + 4:HD + 6].astype(jnp.float32)
    )
    got_max = got_stats[:, :, 0:1]
    got_den = got_stats[:, :, 1:2]
    top_max = jnp.max(got_max, axis=0)
    factor = jnp.exp(got_max - top_max[None])
    num_own = jnp.sum(got_num.astype(jnp.float32) * factor, axis=0)
    den_own = jnp.sum(got_den * factor, axis=0)
    attention = (
        jnp.transpose((num_own / den_own).astype(jnp.bfloat16), (2, 0, 1))
        .reshape(tok_rows, lane_width)
    )
    out_part = lax.dot_general(
        attention, part_out, (((1,), (1,)), ((), ())), preferred_element_type=jnp.float32
    )
    return lax.psum_scatter(
        out_part.astype(jnp.bfloat16), "narrow", scatter_dimension=1, tiled=True
    )


def solution(mesh):
    in_specs = (
        P("wide", None),
        P(),
        P("wide", None, "narrow"),
        P("wide", "narrow"),
        P("wide", None, None, "narrow"),
        P(),
        P(),
        P(),
    )
    out_specs = P("wide", "narrow")
    return jax.shard_map(body, mesh=mesh, in_specs=in_specs, out_specs=out_specs, check_vma=False)
```

```python
import jax
import jax.numpy as jnp
from jax import lax
from jax.experimental import pallas as pl
from jax.experimental.pallas import tpu as pltpu
from jax.sharding import PartitionSpec as P

HD = 96


negative = -1e30
beyond = 1073741824


def rotate(values, positions):
    half_dim = values.shape[-1] // 2
    frequency = 10000.0 ** (-2.0 * jnp.arange(half_dim, dtype=jnp.float32) / values.shape[-1])
    angles = positions.astype(jnp.float32)[:, None] * frequency[None, :]
    cos_part = jnp.cos(angles)[:, None, :]
    sin_part = jnp.sin(angles)[:, None, :]
    lower_half = values[..., :half_dim]
    upper_half = values[..., half_dim:]
    return jnp.concatenate(
        [
            lower_half * cos_part - upper_half * sin_part,
            upper_half * cos_part + lower_half * sin_part,
        ],
        axis=-1,
    )


def lookup(small_table, key_index):
    matches = key_index[..., None] == jnp.arange(small_table.shape[0], dtype=jnp.int32)
    return jnp.sum(jnp.where(matches, small_table, 0), axis=-1)


def attend_kernel(carry_in, out_rows):
    def kernel(req_ref, base_ref, limit_ref, len_ref, slot_ref, *refs):
        if carry_in:
            (q_ref, k_ref, v_ref, m0_ref, l0_ref, o0_ref,
             num_ref, m_ref, l_ref, o_ref) = refs
        else:
            q_ref, k_ref, v_ref, m_ref, l_ref, o_ref = refs
        step = pl.program_id(0)

        @pl.when(step == 0)
        def _():
            if carry_in:
                m_ref[...] = m0_ref[...]
                l_ref[...] = l0_ref[...]
                o_ref[...] = o0_ref[...]
            else:
                m_ref[...] = jnp.full(m_ref.shape, negative, jnp.float32)
                l_ref[...] = jnp.zeros(l_ref.shape, jnp.float32)
                o_ref[...] = jnp.zeros(o_ref.shape, jnp.float32)

        req = req_ref[step]
        base = base_ref[step]
        limit = limit_ref[step]
        qlen = len_ref[req]
        per_request = slot_ref.shape[0] // len_ref.shape[0]
        queries = jnp.concatenate(
            [q_ref[:, slot_ref[req * per_request + i]] for i in range(per_request)], axis=1
        )
        keys = k_ref[0]
        vals = v_ref[0]
        blk_len = keys.shape[1]
        q_len = queries.shape[1]
        scale = keys.shape[-1] ** (-0.5)
        scores = (
            jnp.einsum("hkd,hqd->hkq", keys, queries, preferred_element_type=jnp.float32)
            * scale
        )
        key_pos = base + lax.broadcasted_iota(jnp.int32, (blk_len, q_len), 0)
        query_pos = qlen + lax.broadcasted_iota(jnp.int32, (blk_len, q_len), 1)
        allowed = ((key_pos < limit) & (key_pos <= query_pos))[None]
        masked = jnp.where(allowed, scores, negative)
        m_old = m_ref[req]
        m_new = jnp.maximum(m_old, jnp.max(masked, axis=1, keepdims=True))
        shift = jnp.where(m_new == negative, 0.0, m_new)
        exp_terms = jnp.exp(masked - shift)
        alpha = jnp.exp(m_old - m_new)
        l_ref[req] = alpha * l_ref[req] + jnp.sum(exp_terms, axis=1, keepdims=True)
        weighted = jnp.einsum(
            "hdk,hkq->hdq", vals, exp_terms.astype(jnp.bfloat16),
            preferred_element_type=jnp.float32,
        )
        o_ref[req] = alpha * o_ref[req] + weighted
        m_ref[req] = m_new

        if carry_in:
            @pl.when(step == pl.num_programs(0) - 1)
            def _():
                split = q_len // out_rows
                head_dim = o_ref.shape[2]
                for r in range(len_ref.shape[0]):
                    for c in range(split):
                        cols = pl.ds(c * out_rows, out_rows)
                        group = r * split + c
                        num_ref[group, :, 0:head_dim] = o_ref[r, :, :, cols].astype(jnp.bfloat16)
                        pieces = []
                        for stat in (m_ref[r, :, :, cols], l_ref[r, :, :, cols]):
                            rest = stat
                            for _ in range(3):
                                part = rest.astype(jnp.bfloat16).astype(jnp.float32)
                                pieces.append(part)
                                rest = rest - part
                        shape = (pieces[0].shape[0], 8, out_rows)
                        row = lax.broadcasted_iota(jnp.int32, shape, 1)
                        tail = jnp.zeros(shape, jnp.float32)
                        for index, piece in enumerate(pieces):
                            tail = jnp.where(row == index, piece, tail)
                        num_ref[group, :, head_dim:head_dim + 8] = tail.astype(jnp.bfloat16)

    return kernel


def attend_blocks(
    queries, keys, vals_t, blk_req, blk_base, blk_limit, lengths, slot_of,
    carry=None, out_rows=None,
):
    head_count, _, blk_len, head_dim = queries.shape
    req_count = lengths.shape[0]
    q_len = slot_of.shape[0] // req_count * blk_len
    blk_count = keys.shape[0]
    vmem = pltpu.MemorySpace.VMEM
    whole = pl.BlockSpec(memory_space=vmem)
    in_specs = [
        whole,
        pl.BlockSpec((1, head_count, blk_len, head_dim), lambda j, *_: (j, 0, 0, 0)),
        pl.BlockSpec((1, head_count, head_dim, blk_len), lambda j, *_: (j, 0, 0, 0)),
    ]
    args = [queries, keys, vals_t]
    acc_shapes = (
        ((req_count, head_count, 1, q_len), jnp.float32),
        ((req_count, head_count, 1, q_len), jnp.float32),
        ((req_count, head_count, head_dim, q_len), jnp.float32),
    )
    if carry is None:
        out_shape = tuple(jax.ShapeDtypeStruct(*a) for a in acc_shapes)
        out_specs = (whole, whole, whole)
        scratch = ()
    else:
        in_specs += [whole, whole, whole]
        args += list(carry)
        groups = req_count * q_len // out_rows
        out_shape = jax.ShapeDtypeStruct(
            (groups, head_count, head_dim + 8, out_rows), jnp.bfloat16
        )
        out_specs = whole
        scratch = tuple(pltpu.VMEM(*a) for a in acc_shapes)
    grid_spec = pltpu.PrefetchScalarGridSpec(
        num_scalar_prefetch=5,
        grid=(blk_count,),
        in_specs=in_specs,
        out_specs=out_specs,
        scratch_shapes=scratch,
    )
    return pl.pallas_call(
        attend_kernel(carry is not None, out_rows),
        out_shape=out_shape,
        grid_spec=grid_spec,
        compiler_params=pltpu.CompilerParams(dimension_semantics=("arbitrary",)),
    )(blk_req, blk_base, blk_limit, lengths, slot_of, *args)


def body(tokens, gain, w_qkv, w_out, cache, lengths, order, pages):
    wide_count = lax.axis_size("wide")
    wide_index = lax.axis_index("wide")
    tok_rows = tokens.shape[0]
    cache_count = cache.shape[0]
    blk_len = cache.shape[1]
    lane_width = cache.shape[3]
    head_count = lane_width // HD
    slot_count = tok_rows // blk_len
    block_total = order.shape[0]
    req_count = lengths.shape[0]
    per_request = block_total // req_count
    fresh_len = per_request * blk_len
    table_len = pages.shape[0] // req_count
    tok_float = tokens.astype(jnp.float32)
    inv_rms = lax.rsqrt(jnp.mean(tok_float * tok_float, axis=1, keepdims=True) + 1e-05)
    normed = (tok_float * inv_rms * gain.astype(jnp.float32)[None, :]).astype(jnp.bfloat16)

    w_q = lax.all_gather(w_qkv[:, 0], "wide", axis=0, tiled=True)
    cache_ids = wide_index * cache_count + jnp.arange(cache_count, dtype=jnp.int32)
    page_ids = jnp.arange(pages.shape[0], dtype=jnp.int32)
    entries = jnp.sum(jnp.where(pages[None, :] == cache_ids[:, None], page_ids[None, :], 0), axis=1)
    cache_req = entries // table_len
    cache_base = (entries % table_len) * blk_len
    cache_limit = lookup(lengths, cache_req)
    cache_keys = jnp.transpose(
        cache[:, :, 0].reshape(cache_count, blk_len, head_count, HD), (0, 2, 1, 3)
    )
    w_q, cache_keys = lax.optimization_barrier((w_q, cache_keys))
    blk_idx = jnp.arange(blk_len, dtype=jnp.int32)
    slot_blocks = lax.dynamic_slice_in_dim(order, wide_index * slot_count, slot_count)
    slot_req = slot_blocks // per_request
    slot_start = lookup(lengths, slot_req) + slot_blocks % per_request * blk_len
    slot_pos = slot_start[:, None] + blk_idx[None, :]
    positions = slot_pos.reshape(tok_rows)
    q_proj = jnp.dot(normed, w_q, preferred_element_type=jnp.float32)
    queries = jnp.transpose(
        rotate(q_proj.reshape(tok_rows, head_count, HD), positions)
        .astype(jnp.bfloat16)
        .reshape(slot_count, blk_len, head_count, HD),
        (2, 0, 1, 3),
    )
    all_queries = lax.all_gather(queries, "wide", axis=1, tiled=True)
    queries, cache_v = lax.optimization_barrier((queries, cache))
    cache_vals = jnp.transpose(
        cache_v[:, :, 1].reshape(cache_count, blk_len, head_count, HD), (0, 2, 3, 1)
    )
    all_queries, cache_vals, w_kv_local = lax.optimization_barrier(
        (all_queries, cache_vals, w_qkv[:, 1:])
    )
    w_kv = lax.all_gather(w_kv_local, "wide", axis=0, tiled=True)

    block_ids = jnp.arange(block_total, dtype=jnp.int32)
    slot_of = jnp.sum(
        jnp.where(order[None, :] == block_ids[:, None], block_ids[None, :], 0), axis=1
    )
    q_heads = all_queries

    carry = attend_blocks(
        q_heads, cache_keys, cache_vals, cache_req, cache_base, cache_limit, lengths, slot_of
    )
    carry, w_out_local = lax.optimization_barrier((carry, w_out))
    part_out = lax.all_gather(w_out_local, "wide", axis=0, tiled=True)

    kv_proj = jnp.einsum("tk,kcj->tcj", normed, w_kv, preferred_element_type=jnp.float32)
    keys_new = (
        rotate(kv_proj[:, 0].reshape(tok_rows, head_count, HD), positions)
        .astype(jnp.bfloat16)
        .reshape(slot_count, blk_len, head_count, HD)
    )
    vals_new = kv_proj[:, 1].astype(jnp.bfloat16).reshape(slot_count, blk_len, head_count, HD)
    new_limit = jnp.full((slot_count,), beyond, jnp.int32)
    packed = attend_blocks(
        q_heads,
        jnp.transpose(keys_new, (0, 2, 1, 3)),
        jnp.transpose(vals_new, (0, 2, 3, 1)),
        slot_req,
        slot_start,
        new_limit,
        lengths,
        slot_of,
        carry=carry,
        out_rows=tok_rows,
    )

    got = lax.all_to_all(packed, "wide", split_axis=0, concat_axis=0, tiled=True)
    got_num = got[:, :, :HD]
    tail = got[:, :, HD:HD + 6].astype(jnp.float32)
    got_max = tail[:, :, 0:1] + tail[:, :, 1:2] + tail[:, :, 2:3]
    got_den = tail[:, :, 3:4] + tail[:, :, 4:5] + tail[:, :, 5:6]
    top_max = jnp.max(got_max, axis=0)
    factor = jnp.exp(got_max - top_max[None])
    num_own = jnp.sum(got_num.astype(jnp.float32) * factor, axis=0)
    den_own = jnp.sum(got_den * factor, axis=0)
    attention = (
        jnp.transpose((num_own / den_own).astype(jnp.bfloat16), (2, 0, 1))
        .reshape(tok_rows, lane_width)
    )
    out_part = lax.dot_general(
        attention, part_out, (((1,), (1,)), ((), ())), preferred_element_type=jnp.float32
    )
    return lax.psum_scatter(
        out_part.astype(jnp.bfloat16), "narrow", scatter_dimension=1, tiled=True
    )


def solution(mesh):
    in_specs = (
        P("wide", None),
        P(),
        P("wide", None, "narrow"),
        P("wide", "narrow"),
        P("wide", None, None, "narrow"),
        P(),
        P(),
        P(),
    )
    out_specs = P("wide", "narrow")
    return jax.shard_map(body, mesh=mesh, in_specs=in_specs, out_specs=out_specs, check_vma=False)
```

```python
import jax
import jax.numpy as jnp
from jax import lax
from jax.experimental import pallas as pl
from jax.experimental.pallas import tpu as pltpu
from jax.sharding import PartitionSpec as P

HD = 96


negative = -1e30
beyond = 1073741824


def rotate(values, positions):
    half_dim = values.shape[-1] // 2
    frequency = 10000.0 ** (-2.0 * jnp.arange(half_dim, dtype=jnp.float32) / values.shape[-1])
    angles = positions.astype(jnp.float32)[:, None] * frequency[None, :]
    cos_part = jnp.cos(angles)[:, None, :]
    sin_part = jnp.sin(angles)[:, None, :]
    lower_half = values[..., :half_dim]
    upper_half = values[..., half_dim:]
    return jnp.concatenate(
        [
            lower_half * cos_part - upper_half * sin_part,
            upper_half * cos_part + lower_half * sin_part,
        ],
        axis=-1,
    )


def lookup(small_table, key_index):
    matches = key_index[..., None] == jnp.arange(small_table.shape[0], dtype=jnp.int32)
    return jnp.sum(jnp.where(matches, small_table, 0), axis=-1)


def attend_kernel(carry_in, out_rows):
    def kernel(req_ref, base_ref, limit_ref, len_ref, slot_ref, *refs):
        if carry_in:
            (q_ref, k_ref, v_ref, m0_ref, l0_ref, o0_ref,
             num_ref, stats_ref, m_ref, l_ref, o_ref) = refs
        else:
            q_ref, k_ref, v_ref, m_ref, l_ref, o_ref = refs
        step = pl.program_id(0)

        @pl.when(step == 0)
        def _():
            if carry_in:
                m_ref[...] = m0_ref[...]
                l_ref[...] = l0_ref[...]
                o_ref[...] = o0_ref[...]
            else:
                m_ref[...] = jnp.full(m_ref.shape, negative, jnp.float32)
                l_ref[...] = jnp.zeros(l_ref.shape, jnp.float32)
                o_ref[...] = jnp.zeros(o_ref.shape, jnp.float32)

        req = req_ref[step]
        base = base_ref[step]
        limit = limit_ref[step]
        qlen = len_ref[req]
        per_request = slot_ref.shape[0] // len_ref.shape[0]
        queries = jnp.concatenate(
            [q_ref[:, slot_ref[req * per_request + i]] for i in range(per_request)], axis=1
        )
        keys = k_ref[0]
        vals = v_ref[0]
        blk_len = keys.shape[1]
        q_len = queries.shape[1]
        scale = keys.shape[-1] ** (-0.5)
        scores = (
            jnp.einsum("hkd,hqd->hkq", keys, queries, preferred_element_type=jnp.float32)
            * scale
        )
        key_pos = base + lax.broadcasted_iota(jnp.int32, (blk_len, q_len), 0)
        query_pos = qlen + lax.broadcasted_iota(jnp.int32, (blk_len, q_len), 1)
        allowed = ((key_pos < limit) & (key_pos <= query_pos))[None]
        masked = jnp.where(allowed, scores, negative)
        m_old = m_ref[req]
        m_new = jnp.maximum(m_old, jnp.max(masked, axis=1, keepdims=True))
        shift = jnp.where(m_new == negative, 0.0, m_new)
        exp_terms = jnp.exp(masked - shift)
        alpha = jnp.exp(m_old - m_new)
        l_ref[req] = alpha * l_ref[req] + jnp.sum(exp_terms, axis=1, keepdims=True)
        weighted = jnp.einsum(
            "hdk,hkq->hdq", vals, exp_terms.astype(jnp.bfloat16),
            preferred_element_type=jnp.float32,
        )
        o_ref[req] = alpha * o_ref[req] + weighted
        m_ref[req] = m_new

        if carry_in:
            @pl.when(step == pl.num_programs(0) - 1)
            def _():
                split = q_len // out_rows
                for r in range(len_ref.shape[0]):
                    for c in range(split):
                        cols = pl.ds(c * out_rows, out_rows)
                        num_ref[r * split + c] = o_ref[r, :, :, cols].astype(jnp.bfloat16)
                        stats_ref[r * split + c, :, 0:1] = m_ref[r, :, :, cols]
                        stats_ref[r * split + c, :, 1:2] = l_ref[r, :, :, cols]

    return kernel


def attend_blocks(
    queries, keys, vals_t, blk_req, blk_base, blk_limit, lengths, slot_of,
    carry=None, out_rows=None,
):
    head_count, _, blk_len, head_dim = queries.shape
    req_count = lengths.shape[0]
    q_len = slot_of.shape[0] // req_count * blk_len
    blk_count = keys.shape[0]
    vmem = pltpu.MemorySpace.VMEM
    whole = pl.BlockSpec(memory_space=vmem)
    in_specs = [
        whole,
        pl.BlockSpec((1, head_count, blk_len, head_dim), lambda j, *_: (j, 0, 0, 0)),
        pl.BlockSpec((1, head_count, head_dim, blk_len), lambda j, *_: (j, 0, 0, 0)),
    ]
    args = [queries, keys, vals_t]
    acc_shapes = (
        ((req_count, head_count, 1, q_len), jnp.float32),
        ((req_count, head_count, 1, q_len), jnp.float32),
        ((req_count, head_count, head_dim, q_len), jnp.float32),
    )
    if carry is None:
        out_shape = tuple(jax.ShapeDtypeStruct(*a) for a in acc_shapes)
        out_specs = (whole, whole, whole)
        scratch = ()
    else:
        in_specs += [whole, whole, whole]
        args += list(carry)
        groups = req_count * q_len // out_rows
        out_shape = (
            jax.ShapeDtypeStruct((groups, head_count, head_dim, out_rows), jnp.bfloat16),
            jax.ShapeDtypeStruct((groups, head_count, 2, out_rows), jnp.float32),
        )
        out_specs = (whole, whole)
        scratch = tuple(pltpu.VMEM(*a) for a in acc_shapes)
    grid_spec = pltpu.PrefetchScalarGridSpec(
        num_scalar_prefetch=5,
        grid=(blk_count,),
        in_specs=in_specs,
        out_specs=out_specs,
        scratch_shapes=scratch,
    )
    return pl.pallas_call(
        attend_kernel(carry is not None, out_rows),
        out_shape=out_shape,
        grid_spec=grid_spec,
        compiler_params=pltpu.CompilerParams(dimension_semantics=("arbitrary",)),
    )(blk_req, blk_base, blk_limit, lengths, slot_of, *args)


def body(tokens, gain, w_qkv, w_out, cache, lengths, order, pages):
    wide_count = lax.axis_size("wide")
    wide_index = lax.axis_index("wide")
    tok_rows = tokens.shape[0]
    cache_count = cache.shape[0]
    blk_len = cache.shape[1]
    lane_width = cache.shape[3]
    head_count = lane_width // HD
    slot_count = tok_rows // blk_len
    block_total = order.shape[0]
    req_count = lengths.shape[0]
    per_request = block_total // req_count
    fresh_len = per_request * blk_len
    table_len = pages.shape[0] // req_count
    tok_float = tokens.astype(jnp.float32)
    inv_rms = lax.rsqrt(jnp.mean(tok_float * tok_float, axis=1, keepdims=True) + 1e-05)
    normed = (tok_float * inv_rms * gain.astype(jnp.float32)[None, :]).astype(jnp.bfloat16)

    w_q = lax.all_gather(w_qkv[:, 0], "wide", axis=0, tiled=True)
    cache_ids = wide_index * cache_count + jnp.arange(cache_count, dtype=jnp.int32)
    page_ids = jnp.arange(pages.shape[0], dtype=jnp.int32)
    entries = jnp.sum(jnp.where(pages[None, :] == cache_ids[:, None], page_ids[None, :], 0), axis=1)
    cache_req = entries // table_len
    cache_base = (entries % table_len) * blk_len
    cache_limit = lookup(lengths, cache_req)
    cache_keys = jnp.transpose(
        cache[:, :, 0].reshape(cache_count, blk_len, head_count, HD), (0, 2, 1, 3)
    )
    w_q, cache_keys = lax.optimization_barrier((w_q, cache_keys))
    blk_idx = jnp.arange(blk_len, dtype=jnp.int32)
    slot_blocks = lax.dynamic_slice_in_dim(order, wide_index * slot_count, slot_count)
    slot_req = slot_blocks // per_request
    slot_start = lookup(lengths, slot_req) + slot_blocks % per_request * blk_len
    slot_pos = slot_start[:, None] + blk_idx[None, :]
    positions = slot_pos.reshape(tok_rows)
    q_proj = jnp.dot(normed, w_q, preferred_element_type=jnp.float32)
    queries = jnp.transpose(
        rotate(q_proj.reshape(tok_rows, head_count, HD), positions)
        .astype(jnp.bfloat16)
        .reshape(slot_count, blk_len, head_count, HD),
        (2, 0, 1, 3),
    )
    all_queries = lax.all_gather(queries, "wide", axis=1, tiled=True)
    queries, cache_v = lax.optimization_barrier((queries, cache))
    cache_vals = jnp.transpose(
        cache_v[:, :, 1].reshape(cache_count, blk_len, head_count, HD), (0, 2, 3, 1)
    )
    all_queries, cache_vals, w_kv_local = lax.optimization_barrier(
        (all_queries, cache_vals, w_qkv[:, 1:])
    )
    w_kv = lax.all_gather(w_kv_local, "wide", axis=0, tiled=True)

    block_ids = jnp.arange(block_total, dtype=jnp.int32)
    slot_of = jnp.sum(
        jnp.where(order[None, :] == block_ids[:, None], block_ids[None, :], 0), axis=1
    )
    q_heads = all_queries

    carry = attend_blocks(
        q_heads, cache_keys, cache_vals, cache_req, cache_base, cache_limit, lengths, slot_of
    )
    carry, w_out_local = lax.optimization_barrier((carry, w_out))
    part_out = lax.all_gather(w_out_local, "wide", axis=0, tiled=True)

    kv_proj = jnp.einsum("tk,kcj->tcj", normed, w_kv, preferred_element_type=jnp.float32)
    keys_new = (
        rotate(kv_proj[:, 0].reshape(tok_rows, head_count, HD), positions)
        .astype(jnp.bfloat16)
        .reshape(slot_count, blk_len, head_count, HD)
    )
    vals_new = kv_proj[:, 1].astype(jnp.bfloat16).reshape(slot_count, blk_len, head_count, HD)
    new_limit = jnp.full((slot_count,), beyond, jnp.int32)
    sent_num, sent_stats = attend_blocks(
        q_heads,
        jnp.transpose(keys_new, (0, 2, 1, 3)),
        jnp.transpose(vals_new, (0, 2, 3, 1)),
        slot_req,
        slot_start,
        new_limit,
        lengths,
        slot_of,
        carry=carry,
        out_rows=tok_rows,
    )

    got_num = lax.all_to_all(sent_num, "wide", split_axis=0, concat_axis=0, tiled=True)
    all_stats = lax.all_gather(sent_stats, "wide", axis=0, tiled=False)
    got_stats = lax.dynamic_index_in_dim(all_stats, wide_index, axis=1, keepdims=False)
    got_max = got_stats[:, :, 0:1]
    got_den = got_stats[:, :, 1:2]
    top_max = jnp.max(got_max, axis=0)
    factor = jnp.exp(got_max - top_max[None])
    num_own = jnp.sum(got_num.astype(jnp.float32) * factor, axis=0)
    den_own = jnp.sum(got_den * factor, axis=0)
    attention = (
        jnp.transpose((num_own / den_own).astype(jnp.bfloat16), (2, 0, 1))
        .reshape(tok_rows, lane_width)
    )
    out_part = lax.dot_general(
        attention, part_out, (((1,), (1,)), ((), ())), preferred_element_type=jnp.float32
    )
    return lax.psum_scatter(
        out_part.astype(jnp.bfloat16), "narrow", scatter_dimension=1, tiled=True
    )


def solution(mesh):
    in_specs = (
        P("wide", None),
        P(),
        P("wide", None, "narrow"),
        P("wide", "narrow"),
        P("wide", None, None, "narrow"),
        P(),
        P(),
        P(),
    )
    out_specs = P("wide", "narrow")
    return jax.shard_map(body, mesh=mesh, in_specs=in_specs, out_specs=out_specs, check_vma=False)
```

```python
import jax
import jax.numpy as jnp
from jax import lax
from jax.experimental import pallas as pl
from jax.experimental.pallas import tpu as pltpu
from jax.sharding import PartitionSpec as P

HD = 96


negative = -1e30
beyond = 1073741824


def rotate(values, positions):
    half_dim = values.shape[-1] // 2
    frequency = 10000.0 ** (-2.0 * jnp.arange(half_dim, dtype=jnp.float32) / values.shape[-1])
    angles = positions.astype(jnp.float32)[:, None] * frequency[None, :]
    cos_part = jnp.cos(angles)[:, None, :]
    sin_part = jnp.sin(angles)[:, None, :]
    lower_half = values[..., :half_dim]
    upper_half = values[..., half_dim:]
    return jnp.concatenate(
        [
            lower_half * cos_part - upper_half * sin_part,
            upper_half * cos_part + lower_half * sin_part,
        ],
        axis=-1,
    )


def lookup(small_table, key_index):
    matches = key_index[..., None] == jnp.arange(small_table.shape[0], dtype=jnp.int32)
    return jnp.sum(jnp.where(matches, small_table, 0), axis=-1)


def attend_kernel(carry_in, out_rows):
    def kernel(req_ref, base_ref, limit_ref, len_ref, slot_ref, *refs):
        if carry_in:
            (q_ref, k_ref, v_ref, m_ref, l_ref, o_ref, num_ref, stats_ref) = refs
        else:
            q_ref, k_ref, v_ref, m_ref, l_ref, o_ref = refs
        step = pl.program_id(0)

        if not carry_in:
            @pl.when(step == 0)
            def _():
                m_ref[...] = jnp.full(m_ref.shape, negative, jnp.float32)
                l_ref[...] = jnp.zeros(l_ref.shape, jnp.float32)
                o_ref[...] = jnp.zeros(o_ref.shape, jnp.float32)

        req = req_ref[step]
        base = base_ref[step]
        limit = limit_ref[step]
        qlen = len_ref[req]
        per_request = slot_ref.shape[0] // len_ref.shape[0]
        queries = jnp.concatenate(
            [q_ref[:, slot_ref[req * per_request + i]] for i in range(per_request)], axis=1
        )
        keys = k_ref[0]
        vals = v_ref[0]
        blk_len = keys.shape[1]
        q_len = queries.shape[1]
        scale = keys.shape[-1] ** (-0.5)
        scores = (
            jnp.einsum("hkd,hqd->hkq", keys, queries, preferred_element_type=jnp.float32)
            * scale
        )
        key_pos = base + lax.broadcasted_iota(jnp.int32, (blk_len, q_len), 0)
        query_pos = qlen + lax.broadcasted_iota(jnp.int32, (blk_len, q_len), 1)
        allowed = ((key_pos < limit) & (key_pos <= query_pos))[None]
        masked = jnp.where(allowed, scores, negative)
        m_old = m_ref[req]
        m_new = jnp.maximum(m_old, jnp.max(masked, axis=1, keepdims=True))
        shift = jnp.where(m_new == negative, 0.0, m_new)
        exp_terms = jnp.exp(masked - shift)
        alpha = jnp.exp(m_old - m_new)
        l_ref[req] = alpha * l_ref[req] + jnp.sum(exp_terms, axis=1, keepdims=True)
        weighted = jnp.einsum(
            "hdk,hkq->hdq", vals, exp_terms.astype(jnp.bfloat16),
            preferred_element_type=jnp.float32,
        )
        o_ref[req] = alpha * o_ref[req] + weighted
        m_ref[req] = m_new

        if carry_in:
            @pl.when(step == pl.num_programs(0) - 1)
            def _():
                split = q_len // out_rows
                for r in range(len_ref.shape[0]):
                    for c in range(split):
                        cols = pl.ds(c * out_rows, out_rows)
                        num_ref[r * split + c] = o_ref[r, :, :, cols].astype(jnp.bfloat16)
                        stats_ref[r * split + c, :, 0:1] = m_ref[r, :, :, cols]
                        stats_ref[r * split + c, :, 1:2] = l_ref[r, :, :, cols]

    return kernel


def attend_blocks(
    queries, keys, vals_t, blk_req, blk_base, blk_limit, lengths, slot_of,
    carry=None, out_rows=None,
):
    head_count, _, blk_len, head_dim = queries.shape
    req_count = lengths.shape[0]
    q_len = slot_of.shape[0] // req_count * blk_len
    blk_count = keys.shape[0]
    vmem = pltpu.MemorySpace.VMEM
    whole = pl.BlockSpec(memory_space=vmem)
    in_specs = [
        whole,
        pl.BlockSpec((1, head_count, blk_len, head_dim), lambda j, *_: (j, 0, 0, 0)),
        pl.BlockSpec((1, head_count, head_dim, blk_len), lambda j, *_: (j, 0, 0, 0)),
    ]
    args = [queries, keys, vals_t]
    acc_shapes = (
        ((req_count, head_count, 1, q_len), jnp.float32),
        ((req_count, head_count, 1, q_len), jnp.float32),
        ((req_count, head_count, head_dim, q_len), jnp.float32),
    )
    if carry is None:
        out_shape = tuple(jax.ShapeDtypeStruct(*a) for a in acc_shapes)
        out_specs = (whole, whole, whole)
        scratch = ()
    else:
        in_specs += [whole, whole, whole]
        args += list(carry)
        groups = req_count * q_len // out_rows
        out_shape = (
            jax.ShapeDtypeStruct((groups, head_count, head_dim, out_rows), jnp.bfloat16),
            jax.ShapeDtypeStruct((groups, head_count, 2, out_rows), jnp.float32),
        )
        out_specs = (whole, whole)
        scratch = ()
    grid_spec = pltpu.PrefetchScalarGridSpec(
        num_scalar_prefetch=5,
        grid=(blk_count,),
        in_specs=in_specs,
        out_specs=out_specs,
        scratch_shapes=scratch,
    )
    return pl.pallas_call(
        attend_kernel(carry is not None, out_rows),
        out_shape=out_shape,
        grid_spec=grid_spec,
        compiler_params=pltpu.CompilerParams(dimension_semantics=("arbitrary",)),
    )(blk_req, blk_base, blk_limit, lengths, slot_of, *args)


def body(tokens, gain, w_qkv, w_out, cache, lengths, order, pages):
    wide_count = lax.axis_size("wide")
    wide_index = lax.axis_index("wide")
    tok_rows = tokens.shape[0]
    cache_count = cache.shape[0]
    blk_len = cache.shape[1]
    lane_width = cache.shape[3]
    head_count = lane_width // HD
    slot_count = tok_rows // blk_len
    block_total = order.shape[0]
    req_count = lengths.shape[0]
    per_request = block_total // req_count
    fresh_len = per_request * blk_len
    table_len = pages.shape[0] // req_count
    tok_float = tokens.astype(jnp.float32)
    inv_rms = lax.rsqrt(jnp.mean(tok_float * tok_float, axis=1, keepdims=True) + 1e-05)
    normed = (tok_float * inv_rms * gain.astype(jnp.float32)[None, :]).astype(jnp.bfloat16)

    w_q = lax.all_gather(w_qkv[:, 0], "wide", axis=0, tiled=True)
    cache_ids = wide_index * cache_count + jnp.arange(cache_count, dtype=jnp.int32)
    page_ids = jnp.arange(pages.shape[0], dtype=jnp.int32)
    entries = jnp.sum(jnp.where(pages[None, :] == cache_ids[:, None], page_ids[None, :], 0), axis=1)
    cache_req = entries // table_len
    cache_base = (entries % table_len) * blk_len
    cache_limit = lookup(lengths, cache_req)
    cache_keys = jnp.transpose(
        cache[:, :, 0].reshape(cache_count, blk_len, head_count, HD), (0, 2, 1, 3)
    )
    w_q, cache_keys = lax.optimization_barrier((w_q, cache_keys))
    blk_idx = jnp.arange(blk_len, dtype=jnp.int32)
    slot_blocks = lax.dynamic_slice_in_dim(order, wide_index * slot_count, slot_count)
    slot_req = slot_blocks // per_request
    slot_start = lookup(lengths, slot_req) + slot_blocks % per_request * blk_len
    slot_pos = slot_start[:, None] + blk_idx[None, :]
    positions = slot_pos.reshape(tok_rows)
    q_proj = jnp.dot(normed, w_q, preferred_element_type=jnp.float32)
    queries = jnp.transpose(
        rotate(q_proj.reshape(tok_rows, head_count, HD), positions)
        .astype(jnp.bfloat16)
        .reshape(slot_count, blk_len, head_count, HD),
        (2, 0, 1, 3),
    )
    all_queries = lax.all_gather(queries, "wide", axis=1, tiled=True)
    queries, cache_v = lax.optimization_barrier((queries, cache))
    cache_vals = jnp.transpose(
        cache_v[:, :, 1].reshape(cache_count, blk_len, head_count, HD), (0, 2, 3, 1)
    )
    all_queries, cache_vals, w_kv_local = lax.optimization_barrier(
        (all_queries, cache_vals, w_qkv[:, 1:])
    )
    w_kv = lax.all_gather(w_kv_local, "wide", axis=0, tiled=True)

    block_ids = jnp.arange(block_total, dtype=jnp.int32)
    slot_of = jnp.sum(
        jnp.where(order[None, :] == block_ids[:, None], block_ids[None, :], 0), axis=1
    )
    q_heads = all_queries

    carry = attend_blocks(
        q_heads, cache_keys, cache_vals, cache_req, cache_base, cache_limit, lengths, slot_of
    )
    carry, w_out_local = lax.optimization_barrier((carry, w_out))
    part_out = lax.all_gather(w_out_local, "wide", axis=0, tiled=True)

    kv_proj = jnp.einsum("tk,kcj->tcj", normed, w_kv, preferred_element_type=jnp.float32)
    keys_new = (
        rotate(kv_proj[:, 0].reshape(tok_rows, head_count, HD), positions)
        .astype(jnp.bfloat16)
        .reshape(slot_count, blk_len, head_count, HD)
    )
    vals_new = kv_proj[:, 1].astype(jnp.bfloat16).reshape(slot_count, blk_len, head_count, HD)
    new_limit = jnp.full((slot_count,), beyond, jnp.int32)
    sent_num, sent_stats = attend_blocks(
        q_heads,
        jnp.transpose(keys_new, (0, 2, 1, 3)),
        jnp.transpose(vals_new, (0, 2, 3, 1)),
        slot_req,
        slot_start,
        new_limit,
        lengths,
        slot_of,
        carry=carry,
        out_rows=tok_rows,
    )

    got_num = lax.all_to_all(sent_num, "wide", split_axis=0, concat_axis=0, tiled=True)
    got_stats = lax.all_to_all(sent_stats, "wide", split_axis=0, concat_axis=0, tiled=True)
    got_max = got_stats[:, :, 0:1]
    got_den = got_stats[:, :, 1:2]
    top_max = jnp.max(got_max, axis=0)
    factor = jnp.exp(got_max - top_max[None])
    num_own = jnp.sum(got_num.astype(jnp.float32) * factor, axis=0)
    den_own = jnp.sum(got_den * factor, axis=0)
    attention = (
        jnp.transpose((num_own / den_own).astype(jnp.bfloat16), (2, 0, 1))
        .reshape(tok_rows, lane_width)
    )
    out_part = lax.dot_general(
        attention, part_out, (((1,), (1,)), ((), ())), preferred_element_type=jnp.float32
    )
    return lax.psum_scatter(
        out_part.astype(jnp.bfloat16), "narrow", scatter_dimension=1, tiled=True
    )


def solution(mesh):
    in_specs = (
        P("wide", None),
        P(),
        P("wide", None, "narrow"),
        P("wide", "narrow"),
        P("wide", None, None, "narrow"),
        P(),
        P(),
        P(),
    )
    out_specs = P("wide", "narrow")
    return jax.shard_map(body, mesh=mesh, in_specs=in_specs, out_specs=out_specs, check_vma=False)
```

```python
import jax
import jax.numpy as jnp
from jax import lax
from jax.experimental import pallas as pl
from jax.experimental.pallas import tpu as pltpu
from jax.sharding import PartitionSpec as P

HD = 96


negative = -1e30
beyond = 1073741824


def rotate(values, positions):
    half_dim = values.shape[-1] // 2
    frequency = 10000.0 ** (-2.0 * jnp.arange(half_dim, dtype=jnp.float32) / values.shape[-1])
    angles = positions.astype(jnp.float32)[:, None] * frequency[None, :]
    cos_part = jnp.cos(angles)[:, None, :]
    sin_part = jnp.sin(angles)[:, None, :]
    lower_half = values[..., :half_dim]
    upper_half = values[..., half_dim:]
    return jnp.concatenate(
        [
            lower_half * cos_part - upper_half * sin_part,
            upper_half * cos_part + lower_half * sin_part,
        ],
        axis=-1,
    )


def lookup(small_table, key_index):
    matches = key_index[..., None] == jnp.arange(small_table.shape[0], dtype=jnp.int32)
    return jnp.sum(jnp.where(matches, small_table, 0), axis=-1)


def attend_kernel(carry_in, out_rows):
    def kernel(req_ref, base_ref, limit_ref, len_ref, slot_ref, *refs):
        if carry_in:
            (q_ref, k_ref, v_ref, m_ref, l_ref, o_ref, num_ref, stats_ref) = refs
        else:
            q_ref, k_ref, v_ref, m_ref, l_ref, o_ref = refs
        step = pl.program_id(0)

        if not carry_in:
            @pl.when(step == 0)
            def _():
                m_ref[...] = jnp.full(m_ref.shape, negative, jnp.float32)
                l_ref[...] = jnp.zeros(l_ref.shape, jnp.float32)
                o_ref[...] = jnp.zeros(o_ref.shape, jnp.float32)

        req = req_ref[step]
        base = base_ref[step]
        limit = limit_ref[step]
        qlen = len_ref[req]
        per_request = slot_ref.shape[0] // len_ref.shape[0]
        if carry_in:
            queries = q_ref[0]
        else:
            queries = jnp.concatenate(
                [q_ref[:, slot_ref[req * per_request + i]] for i in range(per_request)],
                axis=1,
            )
        keys = k_ref[0]
        vals = v_ref[0]
        blk_len = keys.shape[1]
        q_len = queries.shape[1]
        scale = keys.shape[-1] ** (-0.5)
        scores = (
            jnp.einsum("hkd,hqd->hkq", keys, queries, preferred_element_type=jnp.float32)
            * scale
        )
        key_pos = base + lax.broadcasted_iota(jnp.int32, (blk_len, q_len), 0)
        query_pos = qlen + lax.broadcasted_iota(jnp.int32, (blk_len, q_len), 1)
        allowed = ((key_pos < limit) & (key_pos <= query_pos))[None]
        masked = jnp.where(allowed, scores, negative)
        m_old = m_ref[req]
        m_new = jnp.maximum(m_old, jnp.max(masked, axis=1, keepdims=True))
        shift = jnp.where(m_new == negative, 0.0, m_new)
        exp_terms = jnp.exp(masked - shift)
        alpha = jnp.exp(m_old - m_new)
        l_ref[req] = alpha * l_ref[req] + jnp.sum(exp_terms, axis=1, keepdims=True)
        weighted = jnp.einsum(
            "hdk,hkq->hdq", vals, exp_terms.astype(jnp.bfloat16),
            preferred_element_type=jnp.float32,
        )
        o_ref[req] = alpha * o_ref[req] + weighted
        m_ref[req] = m_new

        if carry_in:
            @pl.when(step == pl.num_programs(0) - 1)
            def _():
                split = q_len // out_rows
                for r in range(len_ref.shape[0]):
                    for c in range(split):
                        cols = pl.ds(c * out_rows, out_rows)
                        num_ref[r * split + c] = o_ref[r, :, :, cols].astype(jnp.bfloat16)
                        stats_ref[r * split + c, :, 0:1] = m_ref[r, :, :, cols]
                        stats_ref[r * split + c, :, 1:2] = l_ref[r, :, :, cols]

    return kernel


def attend_blocks(
    queries, keys, vals_t, blk_req, blk_base, blk_limit, lengths, slot_of,
    carry=None, out_rows=None,
):
    _, head_count, blk_len, head_dim = keys.shape
    req_count = lengths.shape[0]
    q_len = slot_of.shape[0] // req_count * blk_len
    blk_count = keys.shape[0]
    vmem = pltpu.MemorySpace.VMEM
    whole = pl.BlockSpec(memory_space=vmem)
    if carry is None:
        q_spec = whole
    else:
        q_spec = pl.BlockSpec(
            (1, head_count, q_len, head_dim), lambda j, req_ref, *_: (req_ref[j], 0, 0, 0)
        )
    in_specs = [
        q_spec,
        pl.BlockSpec((1, head_count, blk_len, head_dim), lambda j, *_: (j, 0, 0, 0)),
        pl.BlockSpec((1, head_count, head_dim, blk_len), lambda j, *_: (j, 0, 0, 0)),
    ]
    args = [queries, keys, vals_t]
    acc_shapes = (
        ((req_count, head_count, 1, q_len), jnp.float32),
        ((req_count, head_count, 1, q_len), jnp.float32),
        ((req_count, head_count, head_dim, q_len), jnp.float32),
    )
    if carry is None:
        out_shape = tuple(jax.ShapeDtypeStruct(*a) for a in acc_shapes)
        out_specs = (whole, whole, whole)
        scratch = ()
    else:
        in_specs += [whole, whole, whole]
        args += list(carry)
        groups = req_count * q_len // out_rows
        out_shape = (
            jax.ShapeDtypeStruct((groups, head_count, head_dim, out_rows), jnp.bfloat16),
            jax.ShapeDtypeStruct((groups, head_count, 2, out_rows), jnp.float32),
        )
        out_specs = (whole, whole)
        scratch = ()
    grid_spec = pltpu.PrefetchScalarGridSpec(
        num_scalar_prefetch=5,
        grid=(blk_count,),
        in_specs=in_specs,
        out_specs=out_specs,
        scratch_shapes=scratch,
    )
    return pl.pallas_call(
        attend_kernel(carry is not None, out_rows),
        out_shape=out_shape,
        grid_spec=grid_spec,
        compiler_params=pltpu.CompilerParams(dimension_semantics=("arbitrary",)),
    )(blk_req, blk_base, blk_limit, lengths, slot_of, *args)


def body(tokens, gain, w_qkv, w_out, cache, lengths, order, pages):
    wide_count = lax.axis_size("wide")
    wide_index = lax.axis_index("wide")
    tok_rows = tokens.shape[0]
    cache_count = cache.shape[0]
    blk_len = cache.shape[1]
    lane_width = cache.shape[3]
    head_count = lane_width // HD
    slot_count = tok_rows // blk_len
    block_total = order.shape[0]
    req_count = lengths.shape[0]
    per_request = block_total // req_count
    fresh_len = per_request * blk_len
    table_len = pages.shape[0] // req_count
    tok_float = tokens.astype(jnp.float32)
    inv_rms = lax.rsqrt(jnp.mean(tok_float * tok_float, axis=1, keepdims=True) + 1e-05)
    normed = (tok_float * inv_rms * gain.astype(jnp.float32)[None, :]).astype(jnp.bfloat16)

    w_q = lax.all_gather(w_qkv[:, 0], "wide", axis=0, tiled=True)
    cache_ids = wide_index * cache_count + jnp.arange(cache_count, dtype=jnp.int32)
    page_ids = jnp.arange(pages.shape[0], dtype=jnp.int32)
    entries = jnp.sum(jnp.where(pages[None, :] == cache_ids[:, None], page_ids[None, :], 0), axis=1)
    cache_req = entries // table_len
    cache_base = (entries % table_len) * blk_len
    cache_limit = lookup(lengths, cache_req)
    cache_keys = jnp.transpose(
        cache[:, :, 0].reshape(cache_count, blk_len, head_count, HD), (0, 2, 1, 3)
    )
    w_q, cache_keys = lax.optimization_barrier((w_q, cache_keys))
    blk_idx = jnp.arange(blk_len, dtype=jnp.int32)
    slot_blocks = lax.dynamic_slice_in_dim(order, wide_index * slot_count, slot_count)
    slot_req = slot_blocks // per_request
    slot_start = lookup(lengths, slot_req) + slot_blocks % per_request * blk_len
    slot_pos = slot_start[:, None] + blk_idx[None, :]
    positions = slot_pos.reshape(tok_rows)
    q_proj = jnp.dot(normed, w_q, preferred_element_type=jnp.float32)
    queries = jnp.transpose(
        rotate(q_proj.reshape(tok_rows, head_count, HD), positions)
        .astype(jnp.bfloat16)
        .reshape(slot_count, blk_len, head_count, HD),
        (2, 0, 1, 3),
    )
    all_queries = lax.all_gather(queries, "wide", axis=1, tiled=True)
    queries, cache_v = lax.optimization_barrier((queries, cache))
    cache_vals = jnp.transpose(
        cache_v[:, :, 1].reshape(cache_count, blk_len, head_count, HD), (0, 2, 3, 1)
    )
    all_queries, cache_vals, w_kv_local = lax.optimization_barrier(
        (all_queries, cache_vals, w_qkv[:, 1:])
    )
    w_kv = lax.all_gather(w_kv_local, "wide", axis=0, tiled=True)

    block_ids = jnp.arange(block_total, dtype=jnp.int32)
    slot_of = jnp.sum(
        jnp.where(order[None, :] == block_ids[:, None], block_ids[None, :], 0), axis=1
    )
    q_heads = all_queries

    carry = attend_blocks(
        q_heads, cache_keys, cache_vals, cache_req, cache_base, cache_limit, lengths, slot_of
    )
    q_req = jnp.transpose(
        q_heads[:, slot_of.reshape(req_count, per_request)], (1, 0, 2, 3, 4)
    ).reshape(req_count, head_count, fresh_len, HD)
    carry, w_out_local, q_req = lax.optimization_barrier((carry, w_out, q_req))
    part_out = lax.all_gather(w_out_local, "wide", axis=0, tiled=True)

    kv_proj = jnp.einsum("tk,kcj->tcj", normed, w_kv, preferred_element_type=jnp.float32)
    keys_new = (
        rotate(kv_proj[:, 0].reshape(tok_rows, head_count, HD), positions)
        .astype(jnp.bfloat16)
        .reshape(slot_count, blk_len, head_count, HD)
    )
    vals_new = kv_proj[:, 1].astype(jnp.bfloat16).reshape(slot_count, blk_len, head_count, HD)
    new_limit = jnp.full((slot_count,), beyond, jnp.int32)
    sent_num, sent_stats = attend_blocks(
        q_req,
        jnp.transpose(keys_new, (0, 2, 1, 3)),
        jnp.transpose(vals_new, (0, 2, 3, 1)),
        slot_req,
        slot_start,
        new_limit,
        lengths,
        slot_of,
        carry=carry,
        out_rows=tok_rows,
    )

    got_num = lax.all_to_all(sent_num, "wide", split_axis=0, concat_axis=0, tiled=True)
    got_stats = lax.all_to_all(sent_stats, "wide", split_axis=0, concat_axis=0, tiled=True)
    got_max = got_stats[:, :, 0:1]
    got_den = got_stats[:, :, 1:2]
    top_max = jnp.max(got_max, axis=0)
    factor = jnp.exp(got_max - top_max[None])
    num_own = jnp.sum(got_num.astype(jnp.float32) * factor, axis=0)
    den_own = jnp.sum(got_den * factor, axis=0)
    attention = (
        jnp.transpose((num_own / den_own).astype(jnp.bfloat16), (2, 0, 1))
        .reshape(tok_rows, lane_width)
    )
    out_part = lax.dot_general(
        attention, part_out, (((1,), (1,)), ((), ())), preferred_element_type=jnp.float32
    )
    return lax.psum_scatter(
        out_part.astype(jnp.bfloat16), "narrow", scatter_dimension=1, tiled=True
    )


def solution(mesh):
    in_specs = (
        P("wide", None),
        P(),
        P("wide", None, "narrow"),
        P("wide", "narrow"),
        P("wide", None, None, "narrow"),
        P(),
        P(),
        P(),
    )
    out_specs = P("wide", "narrow")
    return jax.shard_map(body, mesh=mesh, in_specs=in_specs, out_specs=out_specs, check_vma=False)
```

```python
import jax
import jax.numpy as jnp
from jax import lax
from jax.experimental import pallas as pl
from jax.experimental.pallas import tpu as pltpu
from jax.sharding import PartitionSpec as P

HD = 96


negative = -1e30
beyond = 1073741824


def rotate(values, positions):
    half_dim = values.shape[-1] // 2
    frequency = 10000.0 ** (-2.0 * jnp.arange(half_dim, dtype=jnp.float32) / values.shape[-1])
    angles = positions.astype(jnp.float32)[:, None] * frequency[None, :]
    cos_part = jnp.cos(angles)[:, None, :]
    sin_part = jnp.sin(angles)[:, None, :]
    lower_half = values[..., :half_dim]
    upper_half = values[..., half_dim:]
    return jnp.concatenate(
        [
            lower_half * cos_part - upper_half * sin_part,
            upper_half * cos_part + lower_half * sin_part,
        ],
        axis=-1,
    )


def lookup(small_table, key_index):
    matches = key_index[..., None] == jnp.arange(small_table.shape[0], dtype=jnp.int32)
    return jnp.sum(jnp.where(matches, small_table, 0), axis=-1)


def attend_kernel(carry_in, out_rows):
    def kernel(req_ref, base_ref, limit_ref, len_ref, slot_ref, *refs):
        if carry_in:
            (q_ref, k_ref, v_ref, m_ref, l_ref, o_ref, num_ref, stats_ref) = refs
        else:
            q_ref, k_ref, v_ref, m_ref, l_ref, o_ref = refs
        step = pl.program_id(0)

        if not carry_in:
            @pl.when(step == 0)
            def _():
                m_ref[...] = jnp.full(m_ref.shape, negative, jnp.float32)
                l_ref[...] = jnp.zeros(l_ref.shape, jnp.float32)
                o_ref[...] = jnp.zeros(o_ref.shape, jnp.float32)

        req = req_ref[step]
        base = base_ref[step]
        limit = limit_ref[step]
        qlen = len_ref[req]
        per_request = slot_ref.shape[0] // len_ref.shape[0]
        if carry_in:
            queries = q_ref[0]
        else:
            queries = jnp.concatenate(
                [q_ref[:, slot_ref[req * per_request + i]] for i in range(per_request)],
                axis=1,
            )
        keys = k_ref[0]
        vals = v_ref[0]
        blk_len = keys.shape[1]
        q_len = queries.shape[1]
        scale = keys.shape[-1] ** (-0.5)
        scores = (
            jnp.einsum("hkd,hqd->hkq", keys, queries, preferred_element_type=jnp.float32)
            * scale
        )
        key_pos = base + lax.broadcasted_iota(jnp.int32, (blk_len, q_len), 0)
        query_pos = qlen + lax.broadcasted_iota(jnp.int32, (blk_len, q_len), 1)
        allowed = ((key_pos < limit) & (key_pos <= query_pos))[None]
        masked = jnp.where(allowed, scores, negative)
        m_old = m_ref[req]
        m_new = jnp.maximum(m_old, jnp.max(masked, axis=1, keepdims=True))
        shift = jnp.where(m_new == negative, 0.0, m_new)
        exp_terms = jnp.exp(masked - shift)
        alpha = jnp.exp(m_old - m_new)
        l_ref[req] = alpha * l_ref[req] + jnp.sum(exp_terms, axis=1, keepdims=True)
        weighted = jnp.einsum(
            "hdk,hkq->hdq", vals, exp_terms.astype(jnp.bfloat16),
            preferred_element_type=jnp.float32,
        )
        o_ref[req] = alpha * o_ref[req] + weighted
        m_ref[req] = m_new

        if carry_in:
            @pl.when(step == pl.num_programs(0) - 1)
            def _():
                split = q_len // out_rows
                for r in range(len_ref.shape[0]):
                    for c in range(split):
                        cols = pl.ds(c * out_rows, out_rows)
                        num_ref[r * split + c] = o_ref[r, :, :, cols].astype(jnp.bfloat16)
                        stats_ref[r * split + c, :, 0:1] = m_ref[r, :, :, cols]
                        stats_ref[r * split + c, :, 1:2] = l_ref[r, :, :, cols]

    return kernel


def attend_blocks(
    queries, keys, vals_t, blk_req, blk_base, blk_limit, lengths, slot_of,
    carry=None, out_rows=None,
):
    _, head_count, blk_len, head_dim = keys.shape
    req_count = lengths.shape[0]
    q_len = slot_of.shape[0] // req_count * blk_len
    blk_count = keys.shape[0]
    vmem = pltpu.MemorySpace.VMEM
    whole = pl.BlockSpec(memory_space=vmem)
    if carry is None:
        q_spec = whole
    else:
        q_spec = pl.BlockSpec(
            (1, head_count, q_len, head_dim), lambda j, req_ref, *_: (req_ref[j], 0, 0, 0)
        )
    in_specs = [
        q_spec,
        pl.BlockSpec((1, head_count, blk_len, head_dim), lambda j, *_: (j, 0, 0, 0)),
        pl.BlockSpec((1, head_count, head_dim, blk_len), lambda j, *_: (j, 0, 0, 0)),
    ]
    args = [queries, keys, vals_t]
    acc_shapes = (
        ((req_count, head_count, 1, q_len), jnp.float32),
        ((req_count, head_count, 1, q_len), jnp.float32),
        ((req_count, head_count, head_dim, q_len), jnp.float32),
    )
    if carry is None:
        out_shape = tuple(jax.ShapeDtypeStruct(*a) for a in acc_shapes)
        out_specs = (whole, whole, whole)
        scratch = ()
    else:
        in_specs += [whole, whole, whole]
        args += list(carry)
        groups = req_count * q_len // out_rows
        out_shape = (
            jax.ShapeDtypeStruct((groups, head_count, head_dim, out_rows), jnp.bfloat16),
            jax.ShapeDtypeStruct((groups, head_count, 2, out_rows), jnp.float32),
        )
        out_specs = (whole, whole)
        scratch = ()
    grid_spec = pltpu.PrefetchScalarGridSpec(
        num_scalar_prefetch=5,
        grid=(blk_count,),
        in_specs=in_specs,
        out_specs=out_specs,
        scratch_shapes=scratch,
    )
    return pl.pallas_call(
        attend_kernel(carry is not None, out_rows),
        out_shape=out_shape,
        grid_spec=grid_spec,
        compiler_params=pltpu.CompilerParams(dimension_semantics=("arbitrary",)),
    )(blk_req, blk_base, blk_limit, lengths, slot_of, *args)


def body(tokens, gain, w_qkv, w_out, cache, lengths, order, pages):
    wide_count = lax.axis_size("wide")
    wide_index = lax.axis_index("wide")
    tok_rows = tokens.shape[0]
    cache_count = cache.shape[0]
    blk_len = cache.shape[1]
    lane_width = cache.shape[3]
    head_count = lane_width // HD
    slot_count = tok_rows // blk_len
    block_total = order.shape[0]
    req_count = lengths.shape[0]
    per_request = block_total // req_count
    fresh_len = per_request * blk_len
    table_len = pages.shape[0] // req_count
    tok_float = tokens.astype(jnp.float32)
    inv_rms = lax.rsqrt(jnp.mean(tok_float * tok_float, axis=1, keepdims=True) + 1e-05)
    normed = (tok_float * inv_rms * gain.astype(jnp.float32)[None, :]).astype(jnp.bfloat16)

    w_q = lax.all_gather(w_qkv[:, 0], "wide", axis=0, tiled=True)
    cache_ids = wide_index * cache_count + jnp.arange(cache_count, dtype=jnp.int32)
    page_ids = jnp.arange(pages.shape[0], dtype=jnp.int32)
    entries = jnp.sum(jnp.where(pages[None, :] == cache_ids[:, None], page_ids[None, :], 0), axis=1)
    cache_req = entries // table_len
    cache_base = (entries % table_len) * blk_len
    cache_limit = lookup(lengths, cache_req)
    cache_keys = jnp.transpose(
        cache[:, :, 0].reshape(cache_count, blk_len, head_count, HD), (0, 2, 1, 3)
    )
    w_q, cache_keys = lax.optimization_barrier((w_q, cache_keys))
    blk_idx = jnp.arange(blk_len, dtype=jnp.int32)
    slot_blocks = lax.dynamic_slice_in_dim(order, wide_index * slot_count, slot_count)
    slot_req = slot_blocks // per_request
    slot_start = lookup(lengths, slot_req) + slot_blocks % per_request * blk_len
    slot_pos = slot_start[:, None] + blk_idx[None, :]
    positions = slot_pos.reshape(tok_rows)
    q_proj = jnp.dot(normed, w_q, preferred_element_type=jnp.float32)
    queries = (
        rotate(q_proj.reshape(tok_rows, head_count, HD), positions)
        .astype(jnp.bfloat16)
        .reshape(tok_rows, lane_width)
    )
    all_queries = lax.all_gather(queries, "wide", axis=0, tiled=True)
    queries, cache_v = lax.optimization_barrier((queries, cache))
    cache_vals = jnp.transpose(
        cache_v[:, :, 1].reshape(cache_count, blk_len, head_count, HD), (0, 2, 3, 1)
    )
    all_queries, cache_vals, w_kv_local = lax.optimization_barrier(
        (all_queries, cache_vals, w_qkv[:, 1:])
    )
    w_kv = lax.all_gather(w_kv_local, "wide", axis=0, tiled=True)

    block_ids = jnp.arange(block_total, dtype=jnp.int32)
    slot_of = jnp.sum(
        jnp.where(order[None, :] == block_ids[:, None], block_ids[None, :], 0), axis=1
    )
    q_heads = jnp.transpose(
        all_queries.reshape(block_total, blk_len, head_count, HD), (2, 0, 1, 3)
    )

    carry = attend_blocks(
        q_heads, cache_keys, cache_vals, cache_req, cache_base, cache_limit, lengths, slot_of
    )
    q_req = jnp.transpose(
        q_heads[:, slot_of.reshape(req_count, per_request)], (1, 0, 2, 3, 4)
    ).reshape(req_count, head_count, fresh_len, HD)
    carry, w_out_local, q_req = lax.optimization_barrier((carry, w_out, q_req))
    part_out = lax.all_gather(w_out_local, "wide", axis=0, tiled=True)

    kv_proj = jnp.einsum("tk,kcj->tcj", normed, w_kv, preferred_element_type=jnp.float32)
    keys_new = (
        rotate(kv_proj[:, 0].reshape(tok_rows, head_count, HD), positions)
        .astype(jnp.bfloat16)
        .reshape(slot_count, blk_len, head_count, HD)
    )
    vals_new = kv_proj[:, 1].astype(jnp.bfloat16).reshape(slot_count, blk_len, head_count, HD)
    new_limit = jnp.full((slot_count,), beyond, jnp.int32)
    sent_num, sent_stats = attend_blocks(
        q_req,
        jnp.transpose(keys_new, (0, 2, 1, 3)),
        jnp.transpose(vals_new, (0, 2, 3, 1)),
        slot_req,
        slot_start,
        new_limit,
        lengths,
        slot_of,
        carry=carry,
        out_rows=tok_rows,
    )

    got_num = lax.all_to_all(sent_num, "wide", split_axis=0, concat_axis=0, tiled=True)
    got_stats = lax.all_to_all(sent_stats, "wide", split_axis=0, concat_axis=0, tiled=True)
    got_max = got_stats[:, :, 0:1]
    got_den = got_stats[:, :, 1:2]
    top_max = jnp.max(got_max, axis=0)
    factor = jnp.exp(got_max - top_max[None])
    num_own = jnp.sum(got_num.astype(jnp.float32) * factor, axis=0)
    den_own = jnp.sum(got_den * factor, axis=0)
    attention = (
        jnp.transpose((num_own / den_own).astype(jnp.bfloat16), (2, 0, 1))
        .reshape(tok_rows, lane_width)
    )
    out_part = lax.dot_general(
        attention, part_out, (((1,), (1,)), ((), ())), preferred_element_type=jnp.float32
    )
    return lax.psum_scatter(
        out_part.astype(jnp.bfloat16), "narrow", scatter_dimension=1, tiled=True
    )


def solution(mesh):
    in_specs = (
        P("wide", None),
        P(),
        P("wide", None, "narrow"),
        P("wide", "narrow"),
        P("wide", None, None, "narrow"),
        P(),
        P(),
        P(),
    )
    out_specs = P("wide", "narrow")
    return jax.shard_map(body, mesh=mesh, in_specs=in_specs, out_specs=out_specs, check_vma=False)
```

```python
import jax
import jax.numpy as jnp
from jax import lax
from jax.experimental import pallas as pl
from jax.experimental.pallas import tpu as pltpu
from jax.sharding import PartitionSpec as P

HD = 96


negative = -1e30
beyond = 1073741824


def rotate(values, positions):
    half_dim = values.shape[-1] // 2
    frequency = 10000.0 ** (-2.0 * jnp.arange(half_dim, dtype=jnp.float32) / values.shape[-1])
    angles = positions.astype(jnp.float32)[:, None] * frequency[None, :]
    cos_part = jnp.cos(angles)[:, None, :]
    sin_part = jnp.sin(angles)[:, None, :]
    lower_half = values[..., :half_dim]
    upper_half = values[..., half_dim:]
    return jnp.concatenate(
        [
            lower_half * cos_part - upper_half * sin_part,
            upper_half * cos_part + lower_half * sin_part,
        ],
        axis=-1,
    )


def lookup(small_table, key_index):
    matches = key_index[..., None] == jnp.arange(small_table.shape[0], dtype=jnp.int32)
    return jnp.sum(jnp.where(matches, small_table, 0), axis=-1)


def attend_kernel(carry_in, out_rows):
    def kernel(req_ref, base_ref, limit_ref, len_ref, slot_ref, *refs):
        if carry_in:
            (q_ref, k_ref, v_ref, m_ref, l_ref, o_ref, num_ref, stats_ref) = refs
        else:
            q_ref, k_ref, v_ref, m_ref, l_ref, o_ref = refs
        step = pl.program_id(0)

        if not carry_in:
            @pl.when(step == 0)
            def _():
                m_ref[...] = jnp.full(m_ref.shape, negative, jnp.float32)
                l_ref[...] = jnp.zeros(l_ref.shape, jnp.float32)
                o_ref[...] = jnp.zeros(o_ref.shape, jnp.float32)

        req = req_ref[step]
        base = base_ref[step]
        limit = limit_ref[step]
        qlen = len_ref[req]
        per_request = slot_ref.shape[0] // len_ref.shape[0]
        if carry_in:
            queries = q_ref[0]
        else:
            queries = jnp.concatenate(
                [q_ref[:, slot_ref[req * per_request + i]] for i in range(per_request)],
                axis=1,
            )
        keys = k_ref[0]
        vals = v_ref[0]
        blk_len = keys.shape[1]
        q_len = queries.shape[1]
        scale = keys.shape[-1] ** (-0.5)
        scores = (
            jnp.einsum("hkd,hqd->hkq", keys, queries, preferred_element_type=jnp.float32)
            * scale
        )
        key_pos = base + lax.broadcasted_iota(jnp.int32, (blk_len, q_len), 0)
        query_pos = qlen + lax.broadcasted_iota(jnp.int32, (blk_len, q_len), 1)
        allowed = ((key_pos < limit) & (key_pos <= query_pos))[None]
        masked = jnp.where(allowed, scores, negative)
        m_old = m_ref[req]
        m_new = jnp.maximum(m_old, jnp.max(masked, axis=1, keepdims=True))
        shift = jnp.where(m_new == negative, 0.0, m_new)
        exp_terms = jnp.exp(masked - shift)
        alpha = jnp.exp(m_old - m_new)
        l_ref[req] = alpha * l_ref[req] + jnp.sum(exp_terms, axis=1, keepdims=True)
        weighted = jnp.einsum(
            "hdk,hkq->hdq", vals, exp_terms.astype(jnp.bfloat16),
            preferred_element_type=jnp.float32,
        )
        o_ref[req] = alpha * o_ref[req] + weighted
        m_ref[req] = m_new

        if carry_in:
            @pl.when(step == pl.num_programs(0) - 1)
            def _():
                split = q_len // out_rows
                for r in range(len_ref.shape[0]):
                    for c in range(split):
                        cols = pl.ds(c * out_rows, out_rows)
                        num_ref[r * split + c] = o_ref[r, :, :, cols].astype(jnp.bfloat16)
                        stats_ref[r * split + c, :, 0:1] = m_ref[r, :, :, cols]
                        stats_ref[r * split + c, :, 1:2] = l_ref[r, :, :, cols]

    return kernel


def attend_blocks(
    queries, keys, vals_t, blk_req, blk_base, blk_limit, lengths, slot_of,
    carry=None, out_rows=None,
):
    _, head_count, blk_len, head_dim = keys.shape
    req_count = lengths.shape[0]
    q_len = slot_of.shape[0] // req_count * blk_len
    blk_count = keys.shape[0]
    vmem = pltpu.MemorySpace.VMEM
    whole = pl.BlockSpec(memory_space=vmem)
    if carry is None:
        q_spec = whole
    else:
        q_spec = pl.BlockSpec(
            (1, head_count, q_len, head_dim), lambda j, req_ref, *_: (req_ref[j], 0, 0, 0)
        )
    in_specs = [
        q_spec,
        pl.BlockSpec((1, head_count, blk_len, head_dim), lambda j, *_: (j, 0, 0, 0)),
        pl.BlockSpec((1, head_count, head_dim, blk_len), lambda j, *_: (j, 0, 0, 0)),
    ]
    args = [queries, keys, vals_t]
    acc_shapes = (
        ((req_count, head_count, 1, q_len), jnp.float32),
        ((req_count, head_count, 1, q_len), jnp.float32),
        ((req_count, head_count, head_dim, q_len), jnp.float32),
    )
    if carry is None:
        out_shape = tuple(jax.ShapeDtypeStruct(*a) for a in acc_shapes)
        out_specs = (whole, whole, whole)
        scratch = ()
    else:
        in_specs += [whole, whole, whole]
        args += list(carry)
        groups = req_count * q_len // out_rows
        out_shape = (
            jax.ShapeDtypeStruct((groups, head_count, head_dim, out_rows), jnp.bfloat16),
            jax.ShapeDtypeStruct((groups, head_count, 2, out_rows), jnp.float32),
        )
        out_specs = (whole, whole)
        scratch = ()
    grid_spec = pltpu.PrefetchScalarGridSpec(
        num_scalar_prefetch=5,
        grid=(blk_count,),
        in_specs=in_specs,
        out_specs=out_specs,
        scratch_shapes=scratch,
    )
    return pl.pallas_call(
        attend_kernel(carry is not None, out_rows),
        out_shape=out_shape,
        grid_spec=grid_spec,
        compiler_params=pltpu.CompilerParams(dimension_semantics=("arbitrary",)),
    )(blk_req, blk_base, blk_limit, lengths, slot_of, *args)


def body(tokens, gain, w_qkv, w_out, cache, lengths, order, pages):
    wide_count = lax.axis_size("wide")
    wide_index = lax.axis_index("wide")
    tok_rows = tokens.shape[0]
    cache_count = cache.shape[0]
    blk_len = cache.shape[1]
    lane_width = cache.shape[3]
    head_count = lane_width // HD
    slot_count = tok_rows // blk_len
    block_total = order.shape[0]
    req_count = lengths.shape[0]
    per_request = block_total // req_count
    fresh_len = per_request * blk_len
    table_len = pages.shape[0] // req_count
    tok_float = tokens.astype(jnp.float32)
    inv_rms = lax.rsqrt(jnp.mean(tok_float * tok_float, axis=1, keepdims=True) + 1e-05)
    normed = (tok_float * inv_rms * gain.astype(jnp.float32)[None, :]).astype(jnp.bfloat16)

    w_q = lax.all_gather(w_qkv[:, 0], "wide", axis=0, tiled=True)
    cache_ids = wide_index * cache_count + jnp.arange(cache_count, dtype=jnp.int32)
    page_ids = jnp.arange(pages.shape[0], dtype=jnp.int32)
    entries = jnp.sum(jnp.where(pages[None, :] == cache_ids[:, None], page_ids[None, :], 0), axis=1)
    cache_req = entries // table_len
    cache_base = (entries % table_len) * blk_len
    cache_limit = lookup(lengths, cache_req)
    cache_keys = jnp.transpose(
        cache[:, :, 0].reshape(cache_count, blk_len, head_count, HD), (0, 2, 1, 3)
    )
    w_q, cache_keys = lax.optimization_barrier((w_q, cache_keys))
    blk_idx = jnp.arange(blk_len, dtype=jnp.int32)
    slot_blocks = lax.dynamic_slice_in_dim(order, wide_index * slot_count, slot_count)
    slot_req = slot_blocks // per_request
    slot_start = lookup(lengths, slot_req) + slot_blocks % per_request * blk_len
    slot_pos = slot_start[:, None] + blk_idx[None, :]
    positions = slot_pos.reshape(tok_rows)
    q_proj = jnp.dot(normed, w_q, preferred_element_type=jnp.float32)
    queries = jnp.transpose(
        rotate(q_proj.reshape(tok_rows, head_count, HD), positions)
        .astype(jnp.bfloat16)
        .reshape(slot_count, blk_len, head_count, HD),
        (2, 0, 1, 3),
    )
    all_queries = lax.all_gather(queries, "wide", axis=1, tiled=True)
    queries, cache_v = lax.optimization_barrier((queries, cache))
    cache_vals = jnp.transpose(
        cache_v[:, :, 1].reshape(cache_count, blk_len, head_count, HD), (0, 2, 3, 1)
    )
    all_queries, cache_vals, w_kv_local = lax.optimization_barrier(
        (all_queries, cache_vals, w_qkv[:, 1:])
    )
    w_kv = lax.all_gather(w_kv_local, "wide", axis=0, tiled=True)

    block_ids = jnp.arange(block_total, dtype=jnp.int32)
    slot_of = jnp.sum(
        jnp.where(order[None, :] == block_ids[:, None], block_ids[None, :], 0), axis=1
    )
    q_heads = all_queries

    carry = attend_blocks(
        q_heads, cache_keys, cache_vals, cache_req, cache_base, cache_limit, lengths, slot_of
    )
    q_req = jnp.transpose(
        q_heads[:, slot_of.reshape(req_count, per_request)], (1, 0, 2, 3, 4)
    ).reshape(req_count, head_count, fresh_len, HD)
    carry, w_out_local, q_req = lax.optimization_barrier((carry, w_out, q_req))
    part_out = lax.all_gather(w_out_local, "wide", axis=0, tiled=True)

    kv_proj = jnp.einsum("tk,kcj->tcj", normed, w_kv, preferred_element_type=jnp.float32)
    keys_new = (
        rotate(kv_proj[:, 0].reshape(tok_rows, head_count, HD), positions)
        .astype(jnp.bfloat16)
        .reshape(slot_count, blk_len, head_count, HD)
    )
    vals_new = kv_proj[:, 1].astype(jnp.bfloat16).reshape(slot_count, blk_len, head_count, HD)
    new_limit = jnp.full((slot_count,), beyond, jnp.int32)
    sent_num, sent_stats = attend_blocks(
        q_req,
        jnp.transpose(keys_new, (0, 2, 1, 3)),
        jnp.transpose(vals_new, (0, 2, 3, 1)),
        slot_req,
        slot_start,
        new_limit,
        lengths,
        slot_of,
        carry=carry,
        out_rows=tok_rows,
    )

    out_t, sent_num = lax.optimization_barrier((jnp.transpose(part_out), sent_num))
    got_num = lax.all_to_all(sent_num, "wide", split_axis=0, concat_axis=0, tiled=True)
    got_stats = lax.all_to_all(sent_stats, "wide", split_axis=0, concat_axis=0, tiled=True)
    got_max = got_stats[:, :, 0:1]
    got_den = got_stats[:, :, 1:2]
    top_max = jnp.max(got_max, axis=0)
    factor = jnp.exp(got_max - top_max[None])
    num_own = jnp.sum(got_num.astype(jnp.float32) * factor, axis=0)
    den_own = jnp.sum(got_den * factor, axis=0)
    attention = (
        jnp.transpose((num_own / den_own).astype(jnp.bfloat16), (2, 0, 1))
        .reshape(tok_rows, lane_width)
    )
    out_part = lax.dot_general(
        attention, out_t, (((1,), (0,)), ((), ())), preferred_element_type=jnp.float32
    )
    return lax.psum_scatter(
        out_part.astype(jnp.bfloat16), "narrow", scatter_dimension=1, tiled=True
    )


def solution(mesh):
    in_specs = (
        P("wide", None),
        P(),
        P("wide", None, "narrow"),
        P("wide", "narrow"),
        P("wide", None, None, "narrow"),
        P(),
        P(),
        P(),
    )
    out_specs = P("wide", "narrow")
    return jax.shard_map(body, mesh=mesh, in_specs=in_specs, out_specs=out_specs, check_vma=False)
```

```python
import jax
import jax.numpy as jnp
from jax import lax
from jax.experimental import pallas as pl
from jax.experimental.pallas import tpu as pltpu
from jax.sharding import PartitionSpec as P

HD = 96


negative = -1e30
beyond = 1073741824


def rotate(values, positions):
    half_dim = values.shape[-1] // 2
    frequency = 10000.0 ** (-2.0 * jnp.arange(half_dim, dtype=jnp.float32) / values.shape[-1])
    angles = positions.astype(jnp.float32)[:, None] * frequency[None, :]
    cos_part = jnp.cos(angles)[:, None, :]
    sin_part = jnp.sin(angles)[:, None, :]
    lower_half = values[..., :half_dim]
    upper_half = values[..., half_dim:]
    return jnp.concatenate(
        [
            lower_half * cos_part - upper_half * sin_part,
            upper_half * cos_part + lower_half * sin_part,
        ],
        axis=-1,
    )


def lookup(small_table, key_index):
    matches = key_index[..., None] == jnp.arange(small_table.shape[0], dtype=jnp.int32)
    return jnp.sum(jnp.where(matches, small_table, 0), axis=-1)


def attend_kernel(carry_in, out_rows):
    def kernel(req_ref, base_ref, limit_ref, len_ref, slot_ref, *refs):
        if carry_in:
            (q_ref, k_ref, v_ref, m_ref, l_ref, o_ref, num_ref, stats_ref) = refs
        else:
            q_ref, k_ref, v_ref, m_ref, l_ref, o_ref = refs
        step = pl.program_id(0)

        if not carry_in:
            @pl.when(step == 0)
            def _():
                m_ref[...] = jnp.full(m_ref.shape, negative, jnp.float32)
                l_ref[...] = jnp.zeros(l_ref.shape, jnp.float32)
                o_ref[...] = jnp.zeros(o_ref.shape, jnp.float32)

        req = req_ref[step]
        base = base_ref[step]
        limit = limit_ref[step]
        qlen = len_ref[req]
        per_request = slot_ref.shape[0] // len_ref.shape[0]
        if carry_in:
            queries = q_ref[0]
        else:
            queries = jnp.concatenate(
                [q_ref[:, slot_ref[req * per_request + i]] for i in range(per_request)],
                axis=1,
            )
        keys = k_ref[0]
        vals = v_ref[0]
        blk_len = keys.shape[1]
        q_len = queries.shape[1]
        scale = keys.shape[-1] ** (-0.5)
        scores = (
            jnp.einsum("hkd,hqd->hkq", keys, queries, preferred_element_type=jnp.float32)
            * scale
        )
        key_pos = base + lax.broadcasted_iota(jnp.int32, (blk_len, q_len), 0)
        query_pos = qlen + lax.broadcasted_iota(jnp.int32, (blk_len, q_len), 1)
        allowed = ((key_pos < limit) & (key_pos <= query_pos))[None]
        masked = jnp.where(allowed, scores, negative)
        m_old = m_ref[req]
        m_new = jnp.maximum(m_old, jnp.max(masked, axis=1, keepdims=True))
        shift = jnp.where(m_new == negative, 0.0, m_new)
        exp_terms = jnp.exp(masked - shift)
        alpha = jnp.exp(m_old - m_new)
        l_ref[req] = alpha * l_ref[req] + jnp.sum(exp_terms, axis=1, keepdims=True)
        weighted = jnp.einsum(
            "hdk,hkq->hdq", vals, exp_terms.astype(jnp.bfloat16),
            preferred_element_type=jnp.float32,
        )
        o_ref[req] = alpha * o_ref[req] + weighted
        m_ref[req] = m_new

        if carry_in:
            @pl.when(step == pl.num_programs(0) - 1)
            def _():
                split = q_len // out_rows
                for r in range(len_ref.shape[0]):
                    for c in range(split):
                        cols = pl.ds(c * out_rows, out_rows)
                        num_ref[r * split + c] = o_ref[r, :, :, cols].astype(jnp.bfloat16)
                        stats_ref[r * split + c, :, 0:1] = m_ref[r, :, :, cols]
                        stats_ref[r * split + c, :, 1:2] = l_ref[r, :, :, cols]

    return kernel


def attend_blocks(
    queries, keys, vals_t, blk_req, blk_base, blk_limit, lengths, slot_of,
    carry=None, out_rows=None,
):
    _, head_count, blk_len, head_dim = keys.shape
    req_count = lengths.shape[0]
    q_len = slot_of.shape[0] // req_count * blk_len
    blk_count = keys.shape[0]
    vmem = pltpu.MemorySpace.VMEM
    whole = pl.BlockSpec(memory_space=vmem)
    if carry is None:
        q_spec = whole
    else:
        q_spec = pl.BlockSpec(
            (1, head_count, q_len, head_dim), lambda j, req_ref, *_: (req_ref[j], 0, 0, 0)
        )
    in_specs = [
        q_spec,
        pl.BlockSpec((1, head_count, blk_len, head_dim), lambda j, *_: (j, 0, 0, 0)),
        pl.BlockSpec((1, head_count, head_dim, blk_len), lambda j, *_: (j, 0, 0, 0)),
    ]
    args = [queries, keys, vals_t]
    acc_shapes = (
        ((req_count, head_count, 1, q_len), jnp.float32),
        ((req_count, head_count, 1, q_len), jnp.float32),
        ((req_count, head_count, head_dim, q_len), jnp.float32),
    )
    if carry is None:
        out_shape = tuple(jax.ShapeDtypeStruct(*a) for a in acc_shapes)
        out_specs = (whole, whole, whole)
        scratch = ()
    else:
        in_specs += [whole, whole, whole]
        args += list(carry)
        groups = req_count * q_len // out_rows
        out_shape = (
            jax.ShapeDtypeStruct((groups, head_count, head_dim, out_rows), jnp.bfloat16),
            jax.ShapeDtypeStruct((groups, head_count, 2, out_rows), jnp.float32),
        )
        out_specs = (whole, whole)
        scratch = ()
    grid_spec = pltpu.PrefetchScalarGridSpec(
        num_scalar_prefetch=5,
        grid=(blk_count,),
        in_specs=in_specs,
        out_specs=out_specs,
        scratch_shapes=scratch,
    )
    return pl.pallas_call(
        attend_kernel(carry is not None, out_rows),
        out_shape=out_shape,
        grid_spec=grid_spec,
        compiler_params=pltpu.CompilerParams(dimension_semantics=("arbitrary",)),
    )(blk_req, blk_base, blk_limit, lengths, slot_of, *args)


def body(tokens, gain, w_qkv, w_out, cache, lengths, order, pages):
    wide_count = lax.axis_size("wide")
    wide_index = lax.axis_index("wide")
    tok_rows = tokens.shape[0]
    cache_count = cache.shape[0]
    blk_len = cache.shape[1]
    lane_width = cache.shape[3]
    head_count = lane_width // HD
    slot_count = tok_rows // blk_len
    block_total = order.shape[0]
    req_count = lengths.shape[0]
    per_request = block_total // req_count
    fresh_len = per_request * blk_len
    table_len = pages.shape[0] // req_count
    tok_float = tokens.astype(jnp.float32)
    inv_rms = lax.rsqrt(jnp.mean(tok_float * tok_float, axis=1, keepdims=True) + 1e-05)
    normed = (tok_float * inv_rms * gain.astype(jnp.float32)[None, :]).astype(jnp.bfloat16)

    w_q = lax.all_gather(w_qkv[:, 0], "wide", axis=0, tiled=True)
    cache_ids = wide_index * cache_count + jnp.arange(cache_count, dtype=jnp.int32)
    page_ids = jnp.arange(pages.shape[0], dtype=jnp.int32)
    entries = jnp.sum(jnp.where(pages[None, :] == cache_ids[:, None], page_ids[None, :], 0), axis=1)
    cache_req = entries // table_len
    cache_base = (entries % table_len) * blk_len
    cache_limit = lookup(lengths, cache_req)
    cache_keys = jnp.transpose(
        cache[:, :, 0].reshape(cache_count, blk_len, head_count, HD), (0, 2, 1, 3)
    )
    w_q, cache_keys = lax.optimization_barrier((w_q, cache_keys))
    blk_idx = jnp.arange(blk_len, dtype=jnp.int32)
    slot_blocks = lax.dynamic_slice_in_dim(order, wide_index * slot_count, slot_count)
    slot_req = slot_blocks // per_request
    slot_start = lookup(lengths, slot_req) + slot_blocks % per_request * blk_len
    slot_pos = slot_start[:, None] + blk_idx[None, :]
    positions = slot_pos.reshape(tok_rows)
    q_proj = jnp.dot(normed, w_q, preferred_element_type=jnp.float32)
    queries = jnp.transpose(
        rotate(q_proj.reshape(tok_rows, head_count, HD), positions)
        .astype(jnp.bfloat16)
        .reshape(slot_count, blk_len, head_count, HD),
        (2, 0, 1, 3),
    )
    all_queries = lax.all_gather(queries, "wide", axis=1, tiled=True)
    queries, cache_v = lax.optimization_barrier((queries, cache))
    cache_vals = jnp.transpose(
        cache_v[:, :, 1].reshape(cache_count, blk_len, head_count, HD), (0, 2, 3, 1)
    )
    all_queries, cache_vals, w_kv_local = lax.optimization_barrier(
        (all_queries, cache_vals, w_qkv[:, 1:])
    )
    w_kv = lax.all_gather(w_kv_local, "wide", axis=0, tiled=True)

    block_ids = jnp.arange(block_total, dtype=jnp.int32)
    slot_of = jnp.sum(
        jnp.where(order[None, :] == block_ids[:, None], block_ids[None, :], 0), axis=1
    )
    q_heads = all_queries

    carry = attend_blocks(
        q_heads, cache_keys, cache_vals, cache_req, cache_base, cache_limit, lengths, slot_of
    )
    q_req = jnp.transpose(
        q_heads[:, slot_of.reshape(req_count, per_request)], (1, 0, 2, 3, 4)
    ).reshape(req_count, head_count, fresh_len, HD)
    carry, w_out_local, q_req = lax.optimization_barrier((carry, w_out, q_req))
    part_out = lax.all_gather(w_out_local, "wide", axis=0, tiled=True)

    kv_proj = jnp.einsum("tk,kcj->tcj", normed, w_kv, preferred_element_type=jnp.float32)
    keys_new = (
        rotate(kv_proj[:, 0].reshape(tok_rows, head_count, HD), positions)
        .astype(jnp.bfloat16)
        .reshape(slot_count, blk_len, head_count, HD)
    )
    vals_new = kv_proj[:, 1].astype(jnp.bfloat16).reshape(slot_count, blk_len, head_count, HD)
    new_limit = jnp.full((slot_count,), beyond, jnp.int32)
    sent_num, sent_stats = attend_blocks(
        q_req,
        jnp.transpose(keys_new, (0, 2, 1, 3)),
        jnp.transpose(vals_new, (0, 2, 3, 1)),
        slot_req,
        slot_start,
        new_limit,
        lengths,
        slot_of,
        carry=carry,
        out_rows=tok_rows,
    )

    got_num = lax.all_to_all(sent_num, "wide", split_axis=0, concat_axis=0, tiled=True)
    got_stats = lax.all_to_all(
        jnp.transpose(sent_stats, (0, 2, 1, 3)), "wide", split_axis=0, concat_axis=0, tiled=True
    )
    got_max = got_stats[:, 0][:, :, None]
    got_den = got_stats[:, 1][:, :, None]
    top_max = jnp.max(got_max, axis=0)
    factor = jnp.exp(got_max - top_max[None])
    num_own = jnp.sum(got_num.astype(jnp.float32) * factor, axis=0)
    den_own = jnp.sum(got_den * factor, axis=0)
    attention = (
        jnp.transpose((num_own / den_own).astype(jnp.bfloat16), (2, 0, 1))
        .reshape(tok_rows, lane_width)
    )
    out_part = lax.dot_general(
        attention, part_out, (((1,), (1,)), ((), ())), preferred_element_type=jnp.float32
    )
    return lax.psum_scatter(
        out_part.astype(jnp.bfloat16), "narrow", scatter_dimension=1, tiled=True
    )


def solution(mesh):
    in_specs = (
        P("wide", None),
        P(),
        P("wide", None, "narrow"),
        P("wide", "narrow"),
        P("wide", None, None, "narrow"),
        P(),
        P(),
        P(),
    )
    out_specs = P("wide", "narrow")
    return jax.shard_map(body, mesh=mesh, in_specs=in_specs, out_specs=out_specs, check_vma=False)
```

```python
import jax
import jax.numpy as jnp
from jax import lax
from jax.experimental import pallas as pl
from jax.experimental.pallas import tpu as pltpu
from jax.sharding import PartitionSpec as P

HD = 96


negative = -1e30
beyond = 1073741824


def rotate(values, positions):
    half_dim = values.shape[-1] // 2
    frequency = 10000.0 ** (-2.0 * jnp.arange(half_dim, dtype=jnp.float32) / values.shape[-1])
    angles = positions.astype(jnp.float32)[:, None] * frequency[None, :]
    cos_part = jnp.cos(angles)[:, None, :]
    sin_part = jnp.sin(angles)[:, None, :]
    lower_half = values[..., :half_dim]
    upper_half = values[..., half_dim:]
    return jnp.concatenate(
        [
            lower_half * cos_part - upper_half * sin_part,
            upper_half * cos_part + lower_half * sin_part,
        ],
        axis=-1,
    )


def lookup(small_table, key_index):
    matches = key_index[..., None] == jnp.arange(small_table.shape[0], dtype=jnp.int32)
    return jnp.sum(jnp.where(matches, small_table, 0), axis=-1)


def attend_kernel(carry_in, out_rows):
    def kernel(req_ref, base_ref, limit_ref, len_ref, slot_ref, *refs):
        if carry_in:
            (q_ref, k_ref, v_ref, m_ref, l_ref, o_ref, num_ref, stats_ref) = refs
        else:
            q_ref, k_ref, v_ref, m_ref, l_ref, o_ref = refs
        step = pl.program_id(0)

        if not carry_in:
            @pl.when(step == 0)
            def _():
                m_ref[...] = jnp.full(m_ref.shape, negative, jnp.float32)
                l_ref[...] = jnp.zeros(l_ref.shape, jnp.float32)
                o_ref[...] = jnp.zeros(o_ref.shape, jnp.float32)

        req = req_ref[step]
        base = base_ref[step]
        limit = limit_ref[step]
        qlen = len_ref[req]
        per_request = slot_ref.shape[0] // len_ref.shape[0]
        if carry_in:
            queries = q_ref[0]
        else:
            queries = jnp.concatenate(
                [q_ref[:, slot_ref[req * per_request + i]] for i in range(per_request)],
                axis=1,
            )
        keys = k_ref[0]
        vals = v_ref[0]
        blk_len = keys.shape[1]
        q_len = queries.shape[1]
        scale = keys.shape[-1] ** (-0.5)
        scores = (
            jnp.einsum("hkd,hqd->hkq", keys, queries, preferred_element_type=jnp.float32)
            * scale
        )
        key_pos = base + lax.broadcasted_iota(jnp.int32, (blk_len, q_len), 0)
        query_pos = qlen + lax.broadcasted_iota(jnp.int32, (blk_len, q_len), 1)
        allowed = ((key_pos < limit) & (key_pos <= query_pos))[None]
        masked = jnp.where(allowed, scores, negative)
        m_old = m_ref[req]
        m_new = jnp.maximum(m_old, jnp.max(masked, axis=1, keepdims=True))
        shift = jnp.where(m_new == negative, 0.0, m_new)
        exp_terms = jnp.exp(masked - shift)
        alpha = jnp.exp(m_old - m_new)
        l_ref[req] = alpha * l_ref[req] + jnp.sum(exp_terms, axis=1, keepdims=True)
        weighted = jnp.einsum(
            "hdk,hkq->hdq", vals, exp_terms.astype(jnp.bfloat16),
            preferred_element_type=jnp.float32,
        )
        o_ref[req] = alpha * o_ref[req] + weighted
        m_ref[req] = m_new

        if carry_in:
            @pl.when(step == pl.num_programs(0) - 1)
            def _():
                split = q_len // out_rows
                for r in range(len_ref.shape[0]):
                    for c in range(split):
                        cols = pl.ds(c * out_rows, out_rows)
                        num_ref[r * split + c] = o_ref[r, :, :, cols].astype(jnp.bfloat16)
                        stats_ref[r * split + c, :, 0:1] = m_ref[r, :, :, cols]
                        stats_ref[r * split + c, :, 1:2] = l_ref[r, :, :, cols]

    return kernel


def attend_blocks(
    queries, keys, vals_t, blk_req, blk_base, blk_limit, lengths, slot_of,
    carry=None, out_rows=None,
):
    _, head_count, blk_len, head_dim = keys.shape
    req_count = lengths.shape[0]
    q_len = slot_of.shape[0] // req_count * blk_len
    blk_count = keys.shape[0]
    vmem = pltpu.MemorySpace.VMEM
    whole = pl.BlockSpec(memory_space=vmem)
    if carry is None:
        q_spec = whole
    else:
        q_spec = pl.BlockSpec(
            (1, head_count, q_len, head_dim), lambda j, req_ref, *_: (req_ref[j], 0, 0, 0)
        )
    in_specs = [
        q_spec,
        pl.BlockSpec((1, head_count, blk_len, head_dim), lambda j, *_: (j, 0, 0, 0)),
        pl.BlockSpec((1, head_count, head_dim, blk_len), lambda j, *_: (j, 0, 0, 0)),
    ]
    args = [queries, keys, vals_t]
    acc_shapes = (
        ((req_count, head_count, 1, q_len), jnp.float32),
        ((req_count, head_count, 1, q_len), jnp.float32),
        ((req_count, head_count, head_dim, q_len), jnp.float32),
    )
    if carry is None:
        out_shape = tuple(jax.ShapeDtypeStruct(*a) for a in acc_shapes)
        out_specs = (whole, whole, whole)
        scratch = ()
    else:
        in_specs += [whole, whole, whole]
        args += list(carry)
        groups = req_count * q_len // out_rows
        out_shape = (
            jax.ShapeDtypeStruct((groups, head_count, head_dim, out_rows), jnp.bfloat16),
            jax.ShapeDtypeStruct((groups, head_count, 2, out_rows), jnp.float32),
        )
        out_specs = (whole, whole)
        scratch = ()
    grid_spec = pltpu.PrefetchScalarGridSpec(
        num_scalar_prefetch=5,
        grid=(blk_count,),
        in_specs=in_specs,
        out_specs=out_specs,
        scratch_shapes=scratch,
    )
    return pl.pallas_call(
        attend_kernel(carry is not None, out_rows),
        out_shape=out_shape,
        grid_spec=grid_spec,
        compiler_params=pltpu.CompilerParams(dimension_semantics=("arbitrary",)),
    )(blk_req, blk_base, blk_limit, lengths, slot_of, *args)


def body(tokens, gain, w_qkv, w_out, cache, lengths, order, pages):
    wide_count = lax.axis_size("wide")
    wide_index = lax.axis_index("wide")
    tok_rows = tokens.shape[0]
    cache_count = cache.shape[0]
    blk_len = cache.shape[1]
    lane_width = cache.shape[3]
    head_count = lane_width // HD
    slot_count = tok_rows // blk_len
    block_total = order.shape[0]
    req_count = lengths.shape[0]
    per_request = block_total // req_count
    fresh_len = per_request * blk_len
    table_len = pages.shape[0] // req_count
    tok_float = tokens.astype(jnp.float32)
    inv_rms = lax.rsqrt(jnp.mean(tok_float * tok_float, axis=1, keepdims=True) + 1e-05)
    normed = (tok_float * inv_rms * gain.astype(jnp.float32)[None, :]).astype(jnp.bfloat16)

    w_q = lax.all_gather(w_qkv[:, 0], "wide", axis=0, tiled=True)
    cache_ids = wide_index * cache_count + jnp.arange(cache_count, dtype=jnp.int32)
    page_ids = jnp.arange(pages.shape[0], dtype=jnp.int32)
    entries = jnp.sum(jnp.where(pages[None, :] == cache_ids[:, None], page_ids[None, :], 0), axis=1)
    cache_req = entries // table_len
    cache_base = (entries % table_len) * blk_len
    cache_limit = lookup(lengths, cache_req)
    cache_keys = jnp.transpose(
        cache[:, :, 0].reshape(cache_count, blk_len, head_count, HD), (0, 2, 1, 3)
    )
    w_q, cache_keys = lax.optimization_barrier((w_q, cache_keys))
    blk_idx = jnp.arange(blk_len, dtype=jnp.int32)
    slot_blocks = lax.dynamic_slice_in_dim(order, wide_index * slot_count, slot_count)
    slot_req = slot_blocks // per_request
    slot_start = lookup(lengths, slot_req) + slot_blocks % per_request * blk_len
    slot_pos = slot_start[:, None] + blk_idx[None, :]
    positions = slot_pos.reshape(tok_rows)
    q_proj = jnp.dot(normed, w_q, preferred_element_type=jnp.float32)
    queries = jnp.transpose(
        rotate(q_proj.reshape(tok_rows, head_count, HD), positions)
        .astype(jnp.bfloat16)
        .reshape(slot_count, blk_len, head_count, HD),
        (2, 0, 1, 3),
    )
    all_queries = lax.all_gather(queries, "wide", axis=1, tiled=True)
    queries, cache_v = lax.optimization_barrier((queries, cache))
    cache_vals = jnp.transpose(
        cache_v[:, :, 1].reshape(cache_count, blk_len, head_count, HD), (0, 2, 3, 1)
    )
    all_queries, cache_vals, w_kv_local = lax.optimization_barrier(
        (all_queries, cache_vals, w_qkv[:, 1:])
    )
    w_kv = lax.all_gather(w_kv_local, "wide", axis=0, tiled=True)

    block_ids = jnp.arange(block_total, dtype=jnp.int32)
    slot_of = jnp.sum(
        jnp.where(order[None, :] == block_ids[:, None], block_ids[None, :], 0), axis=1
    )
    q_heads = all_queries

    carry = attend_blocks(
        q_heads, cache_keys, cache_vals, cache_req, cache_base, cache_limit, lengths, slot_of
    )
    q_req = jnp.transpose(
        q_heads[:, slot_of.reshape(req_count, per_request)], (1, 0, 2, 3, 4)
    ).reshape(req_count, head_count, fresh_len, HD)
    carry, w_out_local, q_req = lax.optimization_barrier((carry, w_out, q_req))
    part_out = lax.all_gather(w_out_local, "wide", axis=0, tiled=True)

    kv_proj = jnp.dot(
        normed, w_kv.reshape(w_kv.shape[0], 2 * lane_width), preferred_element_type=jnp.float32
    ).reshape(tok_rows, 2, lane_width)
    keys_new = (
        rotate(kv_proj[:, 0].reshape(tok_rows, head_count, HD), positions)
        .astype(jnp.bfloat16)
        .reshape(slot_count, blk_len, head_count, HD)
    )
    vals_new = kv_proj[:, 1].astype(jnp.bfloat16).reshape(slot_count, blk_len, head_count, HD)
    new_limit = jnp.full((slot_count,), beyond, jnp.int32)
    sent_num, sent_stats = attend_blocks(
        q_req,
        jnp.transpose(keys_new, (0, 2, 1, 3)),
        jnp.transpose(vals_new, (0, 2, 3, 1)),
        slot_req,
        slot_start,
        new_limit,
        lengths,
        slot_of,
        carry=carry,
        out_rows=tok_rows,
    )

    got_num = lax.all_to_all(sent_num, "wide", split_axis=0, concat_axis=0, tiled=True)
    got_stats = lax.all_to_all(sent_stats, "wide", split_axis=0, concat_axis=0, tiled=True)
    got_max = got_stats[:, :, 0:1]
    got_den = got_stats[:, :, 1:2]
    top_max = jnp.max(got_max, axis=0)
    factor = jnp.exp(got_max - top_max[None])
    num_own = jnp.sum(got_num.astype(jnp.float32) * factor, axis=0)
    den_own = jnp.sum(got_den * factor, axis=0)
    attention = (
        jnp.transpose((num_own / den_own).astype(jnp.bfloat16), (2, 0, 1))
        .reshape(tok_rows, lane_width)
    )
    out_part = lax.dot_general(
        attention, part_out, (((1,), (1,)), ((), ())), preferred_element_type=jnp.float32
    )
    return lax.psum_scatter(
        out_part.astype(jnp.bfloat16), "narrow", scatter_dimension=1, tiled=True
    )


def solution(mesh):
    in_specs = (
        P("wide", None),
        P(),
        P("wide", None, "narrow"),
        P("wide", "narrow"),
        P("wide", None, None, "narrow"),
        P(),
        P(),
        P(),
    )
    out_specs = P("wide", "narrow")
    return jax.shard_map(body, mesh=mesh, in_specs=in_specs, out_specs=out_specs, check_vma=False)
```
